32 devices in a mesh: group: 4 (over y, core), gx: 4 (over z), gy: 2 (over x).
Axes of the slice: x: 2, y: 2, z: 4, core: 2. Of those that a mesh axis runs over, the one named last changes fastest.
Arguments:
- populations: bfloat16 [19, 32, 16, 128], P(None, ('group', 'gx'), 'gy'), may hold values from 0 to 1, as said below
- solid_mask: int32 [32, 16, 128], P(('group', 'gx'), 'gy'), may hold values 0 or 1
- wall_cells: int32 [16, 2, 512], P(('group', 'gx'), 'gy'), may hold values from 0 to 2047
- body_load: float32 [3, 64, 8, 128], P(None, ('group', 'gx'), 'gy'), may hold values from -3 to 3
- elem_scale: float32 [64, 8, 128], P(('group', 'gx'), 'gy'), may hold values from 0.05 to 0.5
- elem_active: int32 [64, 8, 128], P(('group', 'gx'), 'gy'), may hold values 0 or 1
- elem_matrix: float32 [24, 24], replicated, may hold values from -0.25 to 8, as said below
- iface_nodes: int32 [16, 2, 256], P(('group', 'gx'), 'gy'), may hold values from 0 to 2047
- iface_coords: float32 [3, 16, 2, 256], P(None, ('group', 'gx'), 'gy'), may hold values from 0 to 128
- neighbours: int32 [16, 2, 2, 8], P(('group', 'gx'), 'gy'), may hold values from 0 to 11, as said below
Outputs:
- new_populations: bfloat16 [19, 32, 16, 128], P(None, ('group', 'gx'), 'gy')
- displacement: float32 [3, 64, 8, 128], P(None, ('group', 'gx'), 'gy')
The draws below stay inside these ranges and needn't reach their ends.
Inputs may be any that keep to these rules, and one draw needn't show every extreme that they name: `populations`: each population is positive, between 0.48 and 1.68 times its lattice weight. `elem_matrix`: symmetric. `neighbours`: on devices of structure group 3 + j every entry is g * 4 + t with t < 4, g < 3 and g congruent to j modulo 1.
All inputs are finite; a program needn't handle non-finite values. No bound on the sum of `solid_mask` or of `elem_active` on one device may be relied on, other than what follows from the above.
Results may differ from the reference program's by a relative error of at most 0.0019.
Values may be sent and summed in bfloat16 or wider, within the bound.
No kernel may reach another device: no remote copies, remote signals or barrier semaphores. Data moves between devices by JAX's collectives and lax.ppermute only.
A program may use at most 64 MiB of HBM per device.

```python
import math
import jax
import jax.numpy as jnp
from jax import lax

AX = 2
BY = 8
CZ = 128
SA = 4
SB = 4
SC = 128
FT = 4
ST = 2
NB = 8
TILE = 128
ITERS = 3
SGROUPS = 1
FGROUPS = 3
SPAN_DEVS = 4
COLUMNS = 2
SLABS = 16
NXF = 32
NYF = 16
NXS = 64
NYS = 8
PTS = 512
NI = 256
N_GROUP = 4
N_GX = 4
N_GY = 2


def draw_populations(key, part):
    weights = jnp.array([1.0 / 3.0] + [1.0 / 18.0] * 6 + [1.0 / 36.0] * 12, jnp.float32)
    first, second = jax.random.split(key)
    density = jax.random.uniform(first, (1, NXF, NYF, CZ), jnp.float32, 0.8, 1.2)
    wobble = jax.random.uniform(second, (19, NXF, NYF, CZ), jnp.float32, -0.4, 0.4)
    return (weights[:, None, None, None] * density * (1.0 + wobble)).astype(jnp.bfloat16)


def draw_elem_matrix(key, part):
    first, second = jax.random.split(key)
    raw_values = jax.random.uniform(first, (24, 24), jnp.float32, -0.25, 0.25)
    diagonal = jax.random.uniform(second, (24,), jnp.float32, 6.0, 8.0)
    row_ids = lax.broadcasted_iota(jnp.int32, (24, 24), 0)
    col_ids = lax.broadcasted_iota(jnp.int32, (24, 24), 1)
    symmetric = 0.5 * (raw_values + raw_values.T)
    return jnp.where(row_ids == col_ids, diagonal[:, None], symmetric)


def draw_neighbours(key, part):
    first, second = jax.random.split(key)
    group_of = (jnp.arange(SLABS, dtype=jnp.int32) // SPAN_DEVS)[:, None, None, None]
    slot_of = (group_of - FGROUPS) % SGROUPS
    partners = (FGROUPS - slot_of + SGROUPS - 1) // SGROUPS
    grid_shape = (SLABS, COLUMNS, ST, NB)
    partner_pick = jax.random.randint(first, grid_shape, 0, 65536) % partners
    tile_pick = jax.random.randint(second, grid_shape, 0, FT)
    return ((slot_of + partner_pick * SGROUPS) * FT + tile_pick).astype(jnp.int32)


def with_ends(entries, own_key, least, high):
    extent = entries.shape
    index_at = [jax.random.randint(jax.random.fold_in(own_key, axis), (), 0, extent[axis]) for axis in range(len(extent))]
    entries = entries.at[tuple(index_at)].set(least)
    longest = extent.index(max(extent))
    index_at[longest] = (index_at[longest] + 1) % extent[longest]
    return entries.at[tuple(index_at)].set(high)


def levels(stream_key, extent, cuts, smallest, largest):
    gain = 1.0
    for dim, shards_of in cuts:
        draws = jax.random.uniform(jax.random.fold_in(jax.random.fold_in(stream_key, 6), dim), (shards_of,), jnp.float32, smallest / len(cuts), largest / len(cuts))
        gain = gain * jnp.repeat(jnp.exp(draws), extent[dim] // shards_of).reshape((-1,) + (1,) * (len(extent) - 1 - dim))
    return gain


def centred(key, shape, width, limit, pieces=(), kind=jnp.bfloat16):
    values = jax.random.normal(key, shape, jnp.float32) * width
    if len(pieces) > 0:
        values = levels(key, shape, pieces, -0.22, 0.18) * values
    return jnp.clip(values, min=-limit, max=limit).astype(kind)


def setup_inputs(seed: int = 0) -> dict:
    key_of = jax.random.split(jax.random.key(seed), 11)
    return {
        "populations": draw_populations(jax.random.fold_in(key_of[10], 71), 0),
        "solid_mask": with_ends((jax.random.randint(key_of[1], (NXF, NYF, CZ), 0, 6) < 1).astype(jnp.int32), jax.random.fold_in(key_of[1], 1), 0, 1),
        "wall_cells": with_ends(jax.random.randint(key_of[2], (SLABS, COLUMNS, PTS), 0, AX * BY * CZ), jax.random.fold_in(key_of[2], 1), 0, (AX * BY * CZ) - 1).astype(jnp.int32),
        "body_load": centred(key_of[3], (3, NXS, NYS, SC), 0.5, 3.0, ((1, 16), (2, 2)), jnp.float32),
        "elem_scale": jnp.clip(jnp.exp(math.log(0.5) - 2.3025851 * jax.random.uniform(key_of[4], (NXS, NYS, SC), jnp.float32) ** levels(key_of[4], (NXS, NYS, SC), ((0, 16), (1, 2)), -0.2, 0.2)), 0.05, 0.5),
        "elem_active": with_ends((jax.random.randint(key_of[5], (NXS, NYS, SC), 0, 8) < 7).astype(jnp.int32), jax.random.fold_in(key_of[5], 1), 0, 1),
        "elem_matrix": draw_elem_matrix(jax.random.fold_in(key_of[10], 71), 0),
        "iface_nodes": with_ends(jax.random.randint(key_of[7], (SLABS, COLUMNS, NI), 0, SA * SB * SC), jax.random.fold_in(key_of[7], 1), 0, (SA * SB * SC) - 1).astype(jnp.int32),
        "iface_coords": jnp.clip(128.0 * jax.random.uniform(key_of[8], (3, SLABS, COLUMNS, NI), jnp.float32) ** levels(key_of[8], (3, SLABS, COLUMNS, NI), ((1, 16), (2, 2)), -0.2, 0.2), 0.0, 128.0),
        "neighbours": draw_neighbours(jax.random.fold_in(key_of[10], 71), 0),
    }


velocity = [(0, 0, 0), (1, 0, 0), (-1, 0, 0), (0, 1, 0), (0, -1, 0), (0, 0, 1), (0, 0, -1), (1, 1, 0), (-1, -1, 0), (1, -1, 0), (-1, 1, 0), (1, 0, 1), (-1, 0, -1), (1, 0, -1), (-1, 0, 1), (0, 1, 1), (0, -1, -1), (0, 1, -1), (0, -1, 1)]
opposite = [0, 2, 1, 4, 3, 6, 5, 8, 7, 10, 9, 12, 11, 14, 13, 16, 15, 18, 17]
lattice_weight = [1.0 / 3.0] + [1.0 / 18.0] * 6 + [1.0 / 36.0] * 12
relax_rate = 1.0 / 0.6
wall_gain = 60.0
basis_radius = 24.0
mass_shift = 0.5

def project_onto(vectors, direction):
    summed = jnp.zeros_like(vectors[0])
    for component in range(3):
        if direction[component] != 0:
            summed = summed + float(direction[component]) * vectors[component]
    return summed

def collide(population):
    density = lax.optimization_barrier(jnp.sum(population, axis=0))
    momentum = [jnp.zeros_like(density) for component in range(3)]
    for q in range(19):
        for component in range(3):
            if velocity[q][component] != 0:
                momentum[component] = momentum[component] + float(velocity[q][component]) * population[q]
    velocity_parts = [entry / density for entry in momentum]
    speed_square = velocity_parts[0] * velocity_parts[0] + velocity_parts[1] * velocity_parts[1] + velocity_parts[2] * velocity_parts[2]
    relaxed = []
    for q in range(19):
        project = project_onto(velocity_parts, velocity[q])
        balance = lattice_weight[q] * density * (1.0 + 3.0 * project + 4.5 * project * project - 1.5 * speed_square)
        relaxed.append(population[q] + relax_rate * (balance - population[q]))
    return jnp.stack(relaxed)

def stream_links(moved, fluid_ext):
    span_cells = moved.shape[1] - 2
    across_cells = moved.shape[2] - 2
    deep_cells = moved.shape[3] - 2
    upstream, opened, bounce, reflected = ([], [], [], [])
    for q in range(19):
        shift_x, shift_y, shift_z = velocity[q]
        window = (slice(1 - shift_x, 1 - shift_x + span_cells), slice(1 - shift_y, 1 - shift_y + across_cells), slice(1 - shift_z, 1 - shift_z + deep_cells))
        upstream.append(moved[q][window])
        open_up = fluid_ext[window]
        opened.append(open_up)
        bounce.append(1.0 - open_up)
        reflected.append(moved[opposite[q], 1:span_cells + 1, 1:across_cells + 1, 1:deep_cells + 1])
    return (upstream, opened, bounce, reflected)

def wall_force(bounce, reflected):
    force_parts = [jnp.zeros_like(reflected[0]) for component in range(3)]
    for q in range(19):
        for component in range(3):
            if velocity[q][component] != 0:
                force_parts[component] = force_parts[component] - 2.0 * float(velocity[q][component]) * bounce[q] * reflected[q]
    return jnp.stack(force_parts)

def stream_all(moved, fluid_ext, wall_speed):
    upstream, opened, bounce, reflected = stream_links(moved, fluid_ext)
    inside = fluid_ext[1:-1, 1:-1, 1:-1]
    speed_list = [wall_speed[0], wall_speed[1], wall_speed[2]]
    result = []
    for q in range(19):
        correction = 6.0 * lattice_weight[q] * project_onto(speed_list, velocity[q])
        result.append(inside * (opened[q] * upstream[q] + bounce[q] * (reflected[q] + correction)))
    return jnp.stack(result).astype(jnp.bfloat16)

def basis_weights(received, node_positions, tile_lists):
    tile_count = tile_lists.shape[0]
    tile_width = received.shape[2]
    chosen = received[tile_lists]
    nodes_at = node_positions.reshape(3, tile_count, tile_width)
    distance = jnp.zeros((tile_count, tile_width, tile_lists.shape[1], tile_width), jnp.float32)
    for component in range(3):
        offset = nodes_at[component][:, :, None, None] - chosen[:, None, :, 3 + component, :]
        distance = distance + offset * offset
    kernel = 1.0 / jnp.sqrt(1.0 + distance / (basis_radius * basis_radius))
    column = lax.optimization_barrier(jnp.sum(kernel, axis=1))
    totals = jnp.zeros((received.shape[0], tile_width), jnp.float32).at[tile_lists.reshape(-1)].add(column.reshape(-1, tile_width))
    return (kernel / totals[tile_lists][:, None, :, :], chosen)

def map_tractions(weights, chosen, node_index, nodes_total):
    mapped = jnp.einsum('anbp,abcp->can', weights, chosen[:, :, 0:3, :], precision=lax.Precision.HIGHEST)
    return jnp.zeros((3, nodes_total), jnp.float32).at[:, node_index].add(mapped.reshape(3, -1))

def map_speeds(weights, solution_flat, node_index, tile_lists, tile_slots):
    tile_count = weights.shape[0]
    tile_width = weights.shape[1]
    at_nodes = solution_flat[:, node_index].reshape(3, tile_count, tile_width)
    contrib = jnp.einsum('anbp,can->abcp', weights, at_nodes, precision=lax.Precision.HIGHEST)
    return jnp.zeros((tile_slots, 3, tile_width), jnp.float32).at[tile_lists.reshape(-1)].add(contrib.reshape(-1, 3, tile_width))

def element_sum(widened, matrix):
    span_cells = widened.shape[1] - 2
    across_cells = widened.shape[2] - 2
    deep_cells = widened.shape[3]
    widened_z = jnp.pad(widened, ((0, 0), (0, 0), (0, 0), (0, 1)))
    corners = [(a, b, c) for a in (0, 1) for b in (0, 1) for c in (0, 1)]
    gathered = jnp.concatenate([widened_z[0:3, a:a + span_cells + 1, b:b + across_cells + 1, c:c + deep_cells] for a, b, c in corners], axis=0)
    element_scale = widened_z[3, 0:span_cells + 1, 0:across_cells + 1, 0:deep_cells]
    forces = element_scale * jnp.einsum('ij,jabc->iabc', matrix, gathered, precision=lax.Precision.HIGHEST)
    summed = jnp.zeros((3, span_cells + 2, across_cells + 2, deep_cells + 1), jnp.float32)
    for corner_id, (a, b, c) in enumerate(corners):
        summed = summed.at[:, a:a + span_cells + 1, b:b + across_cells + 1, c:c + deep_cells].add(forces[3 * corner_id:3 * corner_id + 3])
    return summed[:, 1:span_cells + 1, 1:across_cells + 1, 0:deep_cells]

def solve_structure(right_side, operator, products):
    residual = right_side
    image_vec = operator(residual)
    norm_now, curvature = products(residual, image_vec)
    step_size = norm_now / curvature
    direction, image_dir = (residual, image_vec)
    solution = jnp.zeros_like(right_side)
    for iteration in range(ITERS):
        solution = solution + step_size * direction
        residual = residual - step_size * image_dir
        if iteration + 1 < ITERS:
            image_vec = operator(residual)
            norm_next, curvature = products(residual, image_vec)
            beta_ratio = norm_next / norm_now
            step_size = norm_next / (curvature - beta_ratio * norm_next / step_size)
            direction = residual + beta_ratio * direction
            image_dir = image_vec + beta_ratio * image_dir
            norm_now = norm_next
    return solution

def reference(populations, solid_mask, wall_cells, body_load, elem_scale, elem_active, elem_matrix, iface_nodes, iface_coords, neighbours):
    fluid_slabs = FGROUPS * N_GX
    fluid_rows = fluid_slabs * AX
    open_cells = 1.0 - solid_mask[:fluid_rows].astype(jnp.float32)
    open_blocks = open_cells.reshape(fluid_slabs, AX, NYF, CZ)
    slab_ids = jnp.arange(fluid_slabs, dtype=jnp.int32)

    def relax_slab(slab_id):
        slab_pops = lax.dynamic_slice_in_dim(populations, slab_id * AX, AX, 1)
        return collide(slab_pops.astype(jnp.float32)).astype(jnp.bfloat16)
    relaxed_blocks = lax.map(relax_slab, slab_ids)
    relaxed_padded = jnp.pad(relaxed_blocks, ((1, 1), (0, 0), (0, 0), (0, 0), (0, 0)))
    open_padded = jnp.pad(open_blocks, ((1, 1), (0, 0), (0, 0), (0, 0)))

    def slab_extent(slab_id):
        lower_row = lax.dynamic_index_in_dim(relaxed_padded, slab_id, 0, False)[:, AX - 1:AX]
        middle_rows = lax.dynamic_index_in_dim(relaxed_padded, slab_id + 1, 0, False)
        upper_row = lax.dynamic_index_in_dim(relaxed_padded, slab_id + 2, 0, False)[:, 0:1]
        moved = jnp.concatenate([lower_row, middle_rows, upper_row], axis=1)
        moved = jnp.pad(moved, ((0, 0), (0, 0), (1, 1), (1, 1))).astype(jnp.float32)
        open_lower = lax.dynamic_index_in_dim(open_padded, slab_id, 0, False)[AX - 1:AX]
        open_middle = lax.dynamic_index_in_dim(open_padded, slab_id + 1, 0, False)
        open_upper = lax.dynamic_index_in_dim(open_padded, slab_id + 2, 0, False)[0:1]
        fluid_ext = jnp.concatenate([open_lower, open_middle, open_upper], axis=0)
        fluid_ext = jnp.pad(fluid_ext, ((0, 0), (1, 1), (1, 1)))
        return (moved, fluid_ext)
    column_offsets = (jnp.arange(N_GY, dtype=jnp.int32) * BY)[:, None]

    def point_places(slab_id):
        wall_index = lax.dynamic_index_in_dim(wall_cells, slab_id, 0, False)
        span_pos = wall_index // (BY * CZ)
        across_pos = wall_index // CZ % BY + column_offsets
        deep_pos = wall_index % CZ
        return (span_pos, across_pos, deep_pos)

    def traction_slab(slab_id):
        moved, fluid_ext = slab_extent(slab_id)
        upstream, opened, bounce, reflected = stream_links(moved, fluid_ext)
        force_parts = wall_force(bounce, reflected)
        span_pos, across_pos, deep_pos = point_places(slab_id)
        picked = force_parts[:, span_pos, across_pos, deep_pos]
        positions = jnp.stack([(slab_id * AX + span_pos).astype(jnp.float32), across_pos.astype(jnp.float32), deep_pos.astype(jnp.float32)])
        packed = jnp.concatenate([picked, positions], axis=0)
        return packed.reshape(6, N_GY, FT, TILE).transpose(1, 2, 0, 3)
    packets = lax.map(traction_slab, slab_ids)
    packets = packets.reshape(FGROUPS, N_GX, N_GY, FT, 6, TILE)
    packets = jnp.concatenate([packets, jnp.zeros((SGROUPS, N_GX, N_GY, FT, 6, TILE), jnp.float32)], axis=0)
    received = packets.transpose(1, 2, 0, 3, 4, 5).reshape(N_GX, N_GY, N_GROUP * FT, 6, TILE)
    struct_start = FGROUPS * N_GX
    device_count = SGROUPS * N_GX * N_GY
    struct_span = SGROUPS * N_GX * SA
    struct_across = N_GY * SB
    dev_received = jnp.broadcast_to(received[None], (SGROUPS,) + received.shape).reshape((device_count, N_GROUP * FT, 6, TILE))
    dev_nodes = iface_nodes[struct_start:].reshape(device_count, NI)
    dev_positions = iface_coords[:, struct_start:].reshape(3, device_count, NI).transpose(1, 0, 2)
    dev_lists = neighbours[struct_start:].reshape(device_count, ST, NB)

    def forward_device(operands):
        received_one, nodes_one, positions_one, lists_one = operands
        weights, chosen = basis_weights(received_one, positions_one, lists_one)
        return map_tractions(weights, chosen, nodes_one, SA * SB * SC)
    mapped = lax.map(forward_device, (dev_received, dev_nodes, dev_positions, dev_lists))
    mapped = mapped.reshape(SGROUPS, N_GX, N_GY, 3, SA, SB, SC).transpose(3, 0, 1, 4, 2, 5, 6).reshape(3, struct_span, struct_across, SC)
    right_side = body_load[:, struct_start * SA:] + mapped
    stiffness = (elem_scale * elem_active.astype(jnp.float32))[struct_start * SA:]

    def one_block(block):
        widened = jnp.pad(block, ((0, 0), (1, 1), (1, 1), (0, 0)))
        return element_sum(widened, elem_matrix)

    def apply_global(values):
        stacked = jnp.concatenate([values, stiffness[None]], axis=0)
        blocks = stacked.reshape(4, SGROUPS, N_GX * SA, struct_across, SC).transpose(1, 0, 2, 3, 4)
        summed = lax.map(one_block, blocks)
        summed = summed.transpose(1, 0, 2, 3, 4).reshape(3, struct_span, struct_across, SC)
        return mass_shift * values + summed

    def products(first_vec, second_vec):
        return (jnp.sum(first_vec * first_vec), jnp.sum(first_vec * second_vec))
    solution = solve_structure(right_side, apply_global, products)
    dev_solution = solution.reshape(3, SGROUPS, N_GX, SA, N_GY, SB, SC).transpose(1, 2, 4, 0, 3, 5, 6).reshape(device_count, 3, SA * SB * SC)

    def backward_device(operands):
        received_one, nodes_one, positions_one, lists_one, solution_one = operands
        weights, chosen = basis_weights(received_one, positions_one, lists_one)
        return map_speeds(weights, solution_one, nodes_one, lists_one, N_GROUP * FT)
    back_terms = lax.map(backward_device, (dev_received, dev_nodes, dev_positions, dev_lists, dev_solution))
    speeds = back_terms.reshape(SGROUPS, N_GX, N_GY, N_GROUP, FT, 3, TILE).sum(axis=0)
    speeds = speeds.transpose(2, 0, 1, 3, 4, 5)[:FGROUPS].reshape(fluid_slabs, N_GY, FT, 3, TILE)

    def stream_slab(slab_id):
        moved, fluid_ext = slab_extent(slab_id)
        span_pos, across_pos, deep_pos = point_places(slab_id)
        speed_one = lax.dynamic_index_in_dim(speeds, slab_id, 0, False)
        speed_one = speed_one.transpose(2, 0, 1, 3).reshape(3, N_GY, PTS)
        wall_speed = jnp.zeros((3, AX, NYF, CZ), jnp.float32).at[:, span_pos, across_pos, deep_pos].add(wall_gain * speed_one)
        return stream_all(moved, fluid_ext, wall_speed)
    passed = lax.map(stream_slab, slab_ids)
    new_populations = passed.transpose(1, 0, 2, 3, 4).reshape(19, fluid_rows, NYF, CZ)
    new_populations = jnp.pad(new_populations, ((0, 0), (0, NXF - fluid_rows), (0, 0), (0, 0)))
    displacement = jnp.pad(solution, ((0, 0), (struct_start * SA, 0), (0, 0), (0, 0)))
    return (new_populations, displacement)
```

```python
import jax
import jax.numpy as jnp
from jax import lax
from jax.sharding import PartitionSpec as P
from jax.experimental import pallas as pl
from jax.experimental.pallas import tpu as pltpu

TILE = 128
ITERS = 3


velocity = [
    (0, 0, 0),
    (1, 0, 0),
    (-1, 0, 0),
    (0, 1, 0),
    (0, -1, 0),
    (0, 0, 1),
    (0, 0, -1),
    (1, 1, 0),
    (-1, -1, 0),
    (1, -1, 0),
    (-1, 1, 0),
    (1, 0, 1),
    (-1, 0, -1),
    (1, 0, -1),
    (-1, 0, 1),
    (0, 1, 1),
    (0, -1, -1),
    (0, 1, -1),
    (0, -1, 1),
]
opposite = [0, 2, 1, 4, 3, 6, 5, 8, 7, 10, 9, 12, 11, 14, 13, 16, 15, 18, 17]
lattice_weight = [1.0 / 3.0] + [1.0 / 18.0] * 6 + [1.0 / 36.0] * 12
relax_rate = 1.0 / 0.6
wall_gain = 60.0
basis_radius = 24.0
mass_shift = 0.5


def padded(cells, sides, width):
    for axis, dim in sides:
        count = lax.axis_size(axis)
        ends = count - 1
        head = lax.slice_in_dim(cells, 0, width, axis=dim)
        tail = lax.slice_in_dim(cells, cells.shape[dim] - width, cells.shape[dim], axis=dim)
        cells = jnp.concatenate(
            [
                lax.ppermute(tail, axis, [(i, (i + 1) % count) for i in range(ends)]),
                cells,
                lax.ppermute(head, axis, [((i + 1) % count, i) for i in range(ends)]),
            ],
            axis=dim,
        )
    return cells


def passed_along(value, axis, steps):
    count = lax.axis_size(axis)
    pairs = [(source, (source + steps) % count) for source in range(count)]
    return lax.ppermute(value, axis, pairs)


def project_onto(vectors, direction):
    summed = jnp.zeros_like(vectors[0])
    for component in range(3):
        if direction[component] != 0:
            summed = summed + float(direction[component]) * vectors[component]
    return summed


def collide(population):
    density = jnp.sum(population, axis=0)
    momentum = [jnp.zeros_like(density) for component in range(3)]
    for q in range(19):
        for component in range(3):
            if velocity[q][component] != 0:
                momentum[component] = (
                    momentum[component] + float(velocity[q][component]) * population[q]
                )
    velocity_parts = [entry / density for entry in momentum]
    speed_square = (
        velocity_parts[0] * velocity_parts[0]
        + velocity_parts[1] * velocity_parts[1]
        + velocity_parts[2] * velocity_parts[2]
    )
    relaxed = []
    for q in range(19):
        project = project_onto(velocity_parts, velocity[q])
        balance = (
            lattice_weight[q]
            * density
            * (1.0 + 3.0 * project + 4.5 * project * project - 1.5 * speed_square)
        )
        relaxed.append(population[q] + relax_rate * (balance - population[q]))
    return jnp.stack(relaxed)


def stream_links(moved, fluid_ext):
    span_cells = moved.shape[1] - 2
    across_cells = moved.shape[2] - 2
    deep_cells = moved.shape[3] - 2
    upstream, opened, bounce, reflected = ([], [], [], [])
    for q in range(19):
        shift_x, shift_y, shift_z = velocity[q]
        window = (
            slice(1 - shift_x, 1 - shift_x + span_cells),
            slice(1 - shift_y, 1 - shift_y + across_cells),
            slice(1 - shift_z, 1 - shift_z + deep_cells),
        )
        upstream.append(moved[q][window])
        open_up = fluid_ext[window]
        opened.append(open_up)
        bounce.append(1.0 - open_up)
        reflected.append(
            moved[opposite[q], 1 : span_cells + 1, 1 : across_cells + 1, 1 : deep_cells + 1]
        )
    return (upstream, opened, bounce, reflected)


def wall_force(bounce, reflected):
    force_parts = [jnp.zeros_like(reflected[0]) for component in range(3)]
    for q in range(19):
        for component in range(3):
            if velocity[q][component] != 0:
                force_parts[component] = (
                    force_parts[component]
                    - 2.0 * float(velocity[q][component]) * bounce[q] * reflected[q]
                )
    return jnp.stack(force_parts)


def stream_all(moved, fluid_ext, wall_speed):
    upstream, opened, bounce, reflected = stream_links(moved, fluid_ext)
    inside = fluid_ext[1:-1, 1:-1, 1:-1]
    speed_list = [wall_speed[0], wall_speed[1], wall_speed[2]]
    result = []
    for q in range(19):
        correction = 6.0 * lattice_weight[q] * project_onto(speed_list, velocity[q])
        result.append(inside * (opened[q] * upstream[q] + bounce[q] * (reflected[q] + correction)))
    return jnp.stack(result).astype(jnp.bfloat16)


def basis_weights(received, node_positions, tile_lists):
    tile_count = tile_lists.shape[0]
    tile_width = received.shape[2]
    chosen = received[tile_lists]
    nodes_at = node_positions.reshape(3, tile_count, tile_width)
    distance = jnp.zeros((tile_count, tile_width, tile_lists.shape[1], tile_width), jnp.float32)
    for component in range(3):
        offset = nodes_at[component][:, :, None, None] - chosen[:, None, :, 3 + component, :]
        distance = distance + offset * offset
    kernel = 1.0 / jnp.sqrt(1.0 + distance / (basis_radius * basis_radius))
    column = jnp.sum(kernel, axis=1)
    totals = (
        jnp.zeros((received.shape[0], tile_width), jnp.float32)
        .at[tile_lists.reshape(-1)]
        .add(column.reshape(-1, tile_width))
    )
    return (kernel / totals[tile_lists][:, None, :, :], chosen)


def map_tractions(weights, chosen, node_index, nodes_total):
    mapped = jnp.einsum(
        "anbp,abcp->can", weights, chosen[:, :, 0:3, :], precision=lax.Precision.HIGHEST
    )
    return jnp.zeros((3, nodes_total), jnp.float32).at[:, node_index].add(mapped.reshape(3, -1))


def map_speeds(weights, solution_flat, node_index, tile_lists, tile_slots):
    tile_count = weights.shape[0]
    tile_width = weights.shape[1]
    at_nodes = solution_flat[:, node_index].reshape(3, tile_count, tile_width)
    contrib = jnp.einsum("anbp,can->abcp", weights, at_nodes, precision=lax.Precision.HIGHEST)
    return (
        jnp.zeros((tile_slots, 3, tile_width), jnp.float32)
        .at[tile_lists.reshape(-1)]
        .add(contrib.reshape(-1, 3, tile_width))
    )


def element_sum(widened, matrix):
    span_cells = widened.shape[1] - 2
    across_cells = widened.shape[2] - 2
    deep_cells = widened.shape[3]
    widened_z = jnp.pad(widened, ((0, 0), (0, 0), (0, 0), (0, 1)))
    corners = [(a, b, c) for a in (0, 1) for b in (0, 1) for c in (0, 1)]
    gathered = jnp.concatenate(
        [
            widened_z[0:3, a : a + span_cells + 1, b : b + across_cells + 1, c : c + deep_cells]
            for a, b, c in corners
        ],
        axis=0,
    )
    element_scale = widened_z[3, 0 : span_cells + 1, 0 : across_cells + 1, 0:deep_cells]
    forces = element_scale * jnp.einsum(
        "ij,jabc->iabc", matrix, gathered, precision=lax.Precision.HIGHEST
    )
    summed = jnp.zeros((3, span_cells + 2, across_cells + 2, deep_cells + 1), jnp.float32)
    for corner_id, (a, b, c) in enumerate(corners):
        summed = summed.at[
            :, a : a + span_cells + 1, b : b + across_cells + 1, c : c + deep_cells
        ].add(forces[3 * corner_id : 3 * corner_id + 3])
    return summed[:, 1 : span_cells + 1, 1 : across_cells + 1, 0:deep_cells]


def operator_kernel(matrix_ref, values_ref, stiff_ref, out_ref):
    span_cells, across_cells, deep_cells = stiff_ref.shape
    across_at = lax.broadcasted_iota(jnp.int32, (across_cells, deep_cells), 0)
    deep_at = lax.broadcasted_iota(jnp.int32, (across_cells, deep_cells), 1)
    corners = [(a, b, c) for a in (0, 1) for b in (0, 1) for c in (0, 1)]
    for component in range(3):
        out_ref[component, 0:span_cells] = mass_shift * values_ref[component, 0:span_cells]
        out_ref[component, span_cells] = jnp.zeros((across_cells, deep_cells), jnp.float32)

    def ahead(value, across, deep):
        if across:
            value = jnp.where(
                across_at < across_cells - 1, pltpu.roll(value, across_cells - 1, 0), 0.0
            )
        if deep:
            value = jnp.where(deep_at < deep_cells - 1, pltpu.roll(value, deep_cells - 1, 1), 0.0)
        return value

    def behind(value, across, deep):
        if across:
            value = jnp.where(across_at >= 1, pltpu.roll(value, 1, 0), 0.0)
        if deep:
            value = jnp.where(deep_at >= 1, pltpu.roll(value, 1, 1), 0.0)
        return value

    def element_row(row, carry):
        gathered = []
        for a, b, c in corners:
            for component in range(3):
                gathered.append(ahead(values_ref[component, row + a], b, c))
        scale = stiff_ref[row]
        for corner_id, (a, b, c) in enumerate(corners):
            for component in range(3):
                line = 3 * corner_id + component
                force = matrix_ref[line * 24] * gathered[0]
                for other in range(1, 24):
                    force = force + matrix_ref[line * 24 + other] * gathered[other]
                out_ref[component, row + a] += behind(scale * force, b, c)
        return carry

    lax.fori_loop(0, span_cells, element_row, 0)


def partition_operator(values, stiffness, matrix):
    span_cells, across_cells, deep_cells = stiffness.shape
    widened = jnp.pad(values, ((0, 0), (0, 1), (0, 0), (0, 0)))
    cells = span_cells * across_cells * deep_cells
    summed = pl.pallas_call(
        operator_kernel,
        out_shape=jax.ShapeDtypeStruct(widened.shape, jnp.float32),
        in_specs=[
            pl.BlockSpec(memory_space=pltpu.SMEM),
            pl.BlockSpec(memory_space=pltpu.VMEM),
            pl.BlockSpec(memory_space=pltpu.VMEM),
        ],
        out_specs=pl.BlockSpec(memory_space=pltpu.VMEM),
        cost_estimate=pl.CostEstimate(
            flops=2 * 24 * 24 * cells, transcendentals=0, bytes_accessed=28 * cells
        ),
    )(matrix.reshape(-1), widened, stiffness)
    return summed[:, :span_cells]


def whole_partition(block):
    lead = block.shape[:-3]
    count = len(lead)
    every = lax.all_gather(block, "gy", axis=count + 1, tiled=True)
    return lax.all_gather(every, "gx", axis=count, tiled=True)


def own_part(whole, rows, cols):
    start = (0, lax.axis_index("gx") * rows, lax.axis_index("gy") * cols, 0)
    return lax.dynamic_slice(whole, start, (whole.shape[0], rows, cols, whole.shape[3]))


def solve_structure(right_side, operator, products):
    residual = right_side
    image_vec = operator(residual)
    norm_now, curvature = products(residual, image_vec)
    step_size = norm_now / curvature
    direction, image_dir = (residual, image_vec)
    solution = jnp.zeros_like(right_side)
    for iteration in range(ITERS):
        solution = solution + step_size * direction
        residual = residual - step_size * image_dir
        if iteration + 1 < ITERS:
            image_vec = operator(residual)
            norm_next, curvature = products(residual, image_vec)
            beta_ratio = norm_next / norm_now
            step_size = norm_next / (curvature - beta_ratio * norm_next / step_size)
            direction = residual + beta_ratio * direction
            image_dir = image_vec + beta_ratio * image_dir
            norm_now = norm_next
    return solution


def per_device(
    populations,
    solid_mask,
    wall_cells,
    body_load,
    elem_scale,
    elem_active,
    elem_matrix,
    iface_nodes,
    iface_coords,
    neighbours,
):
    group_count = lax.axis_size("group")
    span_devices = lax.axis_size("gx")
    struct_groups = max(1, group_count // 8)
    fluid_groups = group_count - struct_groups
    group_index = lax.axis_index("group")
    slab_index = group_index * span_devices + lax.axis_index("gx")
    column_index = lax.axis_index("gy")
    is_fluid = group_index < fluid_groups
    is_struct = jnp.logical_not(is_fluid)
    span_cells, across_cells, deep_cells = solid_mask.shape
    cell_count = span_cells * across_cells * deep_cells
    fluid_here = jnp.where(is_fluid, 1.0 - solid_mask.astype(jnp.float32), 0.0)
    relaxed_pops = lax.cond(
        is_fluid,
        lambda pops: collide(pops.astype(jnp.float32)).astype(jnp.bfloat16),
        lambda pops: jnp.zeros_like(pops),
        populations,
    )
    marker = fluid_here.astype(jnp.bfloat16)[None]
    widened = padded(
        jnp.concatenate([relaxed_pops, marker], axis=0), ((("group", "gx"), 1), ("gy", 2)), 1
    )
    widened = jnp.pad(widened, ((0, 0), (0, 0), (0, 0), (1, 1))).astype(jnp.float32)
    moved = widened[0:19]
    fluid_ext = widened[19]
    wall_index = wall_cells.reshape(-1)
    point_count = wall_index.shape[0]
    tiles_out = point_count // TILE

    def fluid_pack(operands):
        upstream, opened, bounce, reflected = stream_links(operands[0], operands[1])
        force_parts = wall_force(bounce, reflected).reshape(3, cell_count)
        picked = force_parts[:, wall_index]
        span_pos = wall_index // (across_cells * deep_cells)
        across_pos = wall_index // deep_cells % across_cells + column_index * across_cells
        deep_pos = wall_index % deep_cells
        positions = jnp.stack(
            [
                (slab_index * span_cells + span_pos).astype(jnp.float32),
                across_pos.astype(jnp.float32),
                deep_pos.astype(jnp.float32),
            ]
        )
        packed = jnp.concatenate([picked, positions], axis=0)
        return packed.reshape(6, tiles_out, TILE).transpose(1, 0, 2)

    packed = lax.cond(
        is_fluid,
        fluid_pack,
        lambda operands: jnp.zeros((tiles_out, 6, TILE), jnp.float32),
        (moved, fluid_ext),
    )
    received = lax.all_gather(packed, "group", axis=0, tiled=True)
    node_index = iface_nodes.reshape(-1)
    node_positions = iface_coords.reshape(3, -1)
    tile_lists = neighbours.reshape(neighbours.shape[2], neighbours.shape[3])
    nodes_total = body_load.shape[1] * body_load.shape[2] * body_load.shape[3]
    weight_shape = (tile_lists.shape[0], TILE, tile_lists.shape[1], TILE)

    def struct_map(received_all):
        weights, chosen = basis_weights(received_all, node_positions, tile_lists)
        mapped = map_tractions(weights, chosen, node_index, nodes_total)
        return (weights, body_load + mapped.reshape(body_load.shape))

    def struct_quiet(received_all):
        return (jnp.zeros(weight_shape, jnp.float32), jnp.zeros_like(body_load))

    weights, right_side = lax.cond(is_struct, struct_map, struct_quiet, received)
    stiffness = elem_scale * elem_active.astype(jnp.float32)
    joined = whole_partition(jnp.concatenate([right_side, stiffness[None]], axis=0))
    whole_side = joined[0:3]
    stiffness = joined[3]
    rows, cols = body_load.shape[1], body_load.shape[2]

    def partition_products(first_vec, second_vec):
        pair = (jnp.sum(first_vec * first_vec), jnp.sum(first_vec * second_vec))
        if struct_groups > 1:
            pair = lax.psum(tuple(jnp.where(is_struct, x, 0.0) for x in pair), "group")
        return pair

    def partition_solve(operands):
        side, stiff, matrix = operands
        return solve_structure(
            side, lambda values: partition_operator(values, stiff, matrix), partition_products
        )

    if struct_groups > 1:
        whole_solution = partition_solve((whole_side, stiffness, elem_matrix))
    else:
        whole_solution = lax.cond(
            is_struct,
            partition_solve,
            lambda operands: jnp.zeros_like(operands[0]),
            (whole_side, stiffness, elem_matrix),
        )
    solution = jnp.where(is_struct, own_part(whole_solution, rows, cols), 0.0)
    tile_slots = received.shape[0]

    def struct_back(operands):
        return map_speeds(
            operands[0], operands[1].reshape(3, nodes_total), node_index, tile_lists, tile_slots
        )

    back_terms = lax.cond(
        is_struct,
        struct_back,
        lambda operands: jnp.zeros((tile_slots, 3, TILE), jnp.float32),
        (weights, solution),
    )
    per_group = tile_slots // group_count
    route_count = fluid_groups // struct_groups
    sender_slot = jnp.clip(group_index - fluid_groups, 0, struct_groups - 1)
    own_speeds = jnp.zeros((per_group, 3, TILE), jnp.float32)
    for route_step in range(route_count):
        offset_row = (sender_slot + route_step * struct_groups) * per_group
        outgoing = lax.dynamic_slice_in_dim(back_terms, offset_row, per_group, 0)
        incoming = passed_along(outgoing, "group", (route_step + 1) * struct_groups)
        own_speeds = own_speeds + jnp.where(
            group_index // struct_groups == route_step, incoming, 0.0
        )
    speed_parts = wall_gain * own_speeds.transpose(1, 0, 2).reshape(3, point_count)
    wall_speed = jnp.zeros((3, cell_count), jnp.float32).at[:, wall_index].add(speed_parts)
    wall_speed = wall_speed.reshape(3, span_cells, across_cells, deep_cells)
    new_populations = lax.cond(
        is_fluid,
        lambda operands: stream_all(operands[0], operands[1], operands[2]),
        lambda operands: jnp.zeros(operands[0][:, 1:-1, 1:-1, 1:-1].shape, jnp.bfloat16),
        (moved, fluid_ext, wall_speed),
    )
    return (new_populations, solution)


def solution(mesh):
    placed = (
        P(None, ("group", "gx"), "gy", None),
        P(("group", "gx"), "gy", None),
        P(("group", "gx"), "gy", None),
        P(None, ("group", "gx"), "gy", None),
        P(("group", "gx"), "gy", None),
        P(("group", "gx"), "gy", None),
        P(),
        P(("group", "gx"), "gy", None),
        P(None, ("group", "gx"), "gy", None),
        P(("group", "gx"), "gy", None, None),
    )
    return jax.shard_map(
        per_device,
        mesh=mesh,
        in_specs=placed,
        out_specs=(P(None, ("group", "gx"), "gy", None), P(None, ("group", "gx"), "gy", None)),
        check_vma=False,
    )
```

```python
import jax
import jax.numpy as jnp
import numpy as np
from jax import lax
from jax.sharding import PartitionSpec as P
from jax.experimental import pallas as pl
from jax.experimental.pallas import tpu as pltpu

TILE = 128
ITERS = 3


velocity = [
    (0, 0, 0),
    (1, 0, 0),
    (-1, 0, 0),
    (0, 1, 0),
    (0, -1, 0),
    (0, 0, 1),
    (0, 0, -1),
    (1, 1, 0),
    (-1, -1, 0),
    (1, -1, 0),
    (-1, 1, 0),
    (1, 0, 1),
    (-1, 0, -1),
    (1, 0, -1),
    (-1, 0, 1),
    (0, 1, 1),
    (0, -1, -1),
    (0, 1, -1),
    (0, -1, 1),
]
opposite = [0, 2, 1, 4, 3, 6, 5, 8, 7, 10, 9, 12, 11, 14, 13, 16, 15, 18, 17]
lattice_weight = [1.0 / 3.0] + [1.0 / 18.0] * 6 + [1.0 / 36.0] * 12
relax_rate = 1.0 / 0.6
wall_gain = 60.0
basis_radius = 24.0
mass_shift = 0.5


def halo_exchange(cells):
    span_devices = lax.axis_size(("group", "gx"))
    columns = lax.axis_size("gy")
    rows, cols = cells.shape[1], cells.shape[2]
    row_pick = {1: slice(rows - 1, rows), 0: slice(0, rows), -1: slice(0, 1)}
    col_pick = {1: slice(cols - 1, cols), 0: slice(0, cols), -1: slice(0, 1)}
    received = {}
    for dr in (-1, 0, 1):
        for dc in (-1, 0, 1):
            if dr == 0 and dc == 0:
                received[(dr, dc)] = cells
                continue
            pairs = [
                (r * columns + c, (r + dr) * columns + c + dc)
                for r in range(span_devices)
                for c in range(columns)
                if 0 <= r + dr < span_devices and 0 <= c + dc < columns
            ]
            piece = cells[:, row_pick[dr], col_pick[dc]]
            received[(dr, dc)] = lax.ppermute(piece, ("group", "gx", "gy"), pairs)
    bands = [
        jnp.concatenate([received[(dr, dc)] for dc in (1, 0, -1)], axis=2) for dr in (1, 0, -1)
    ]
    return jnp.concatenate(bands, axis=1)


def passed_along(value, axis, steps):
    count = lax.axis_size(axis)
    pairs = [(source, (source + steps) % count) for source in range(count)]
    return lax.ppermute(value, axis, pairs)


def project_onto(vectors, direction):
    summed = jnp.zeros_like(vectors[0])
    for component in range(3):
        if direction[component] != 0:
            summed = summed + float(direction[component]) * vectors[component]
    return summed


def per_direction(values):
    return jnp.asarray(np.array(values, np.float32).reshape(19, 1, 1, 1))


def collide(population):
    density = jnp.sum(population, axis=0)
    velocity_parts = [
        jnp.sum(per_direction([c[component] for c in velocity]) * population, axis=0) / density
        for component in range(3)
    ]
    speed_square = (
        velocity_parts[0] * velocity_parts[0]
        + velocity_parts[1] * velocity_parts[1]
        + velocity_parts[2] * velocity_parts[2]
    )
    project = project_all(velocity_parts)
    balance = (
        per_direction(lattice_weight)
        * density
        * (1.0 + 3.0 * project + 4.5 * project * project - 1.5 * speed_square)
    )
    return population + relax_rate * (balance - population)


def project_all(vectors):
    summed = per_direction([c[0] for c in velocity]) * vectors[0]
    for component in (1, 2):
        summed = summed + per_direction([c[component] for c in velocity]) * vectors[component]
    return summed


def upstream_of(values, inner):
    for axis in range(3):
        shift = per_direction([c[axis] for c in velocity])
        pick = {
            s: lax.slice_in_dim(values, 1 - s, 1 - s + inner[axis], axis=axis + 1)
            for s in (-1, 0, 1)
        }
        values = jnp.where(shift > 0.5, pick[1], jnp.where(shift < -0.5, pick[-1], pick[0]))
    return values


def stream_links(moved, fluid_ext):
    inner = tuple(size - 2 for size in fluid_ext.shape)
    upstream = upstream_of(moved, inner)
    opened = upstream_of(jnp.broadcast_to(fluid_ext[None], (19,) + fluid_ext.shape), inner)
    bounce = 1.0 - opened
    centre = moved[:, 1 : inner[0] + 1, 1 : inner[1] + 1, 1 : inner[2] + 1]
    paired = centre[1:].reshape((9, 2) + inner)[:, ::-1].reshape((18,) + inner)
    reflected = jnp.concatenate([centre[0:1], paired], axis=0)
    return (upstream, opened, bounce, reflected)


def wall_force(bounce, reflected):
    carried = bounce * reflected
    return jnp.stack(
        [
            jnp.sum(per_direction([-2.0 * c[component] for c in velocity]) * carried, axis=0)
            for component in range(3)
        ]
    )


def stream_all(moved, fluid_ext, wall_speed):
    upstream, opened, bounce, reflected = stream_links(moved, fluid_ext)
    inside = fluid_ext[1:-1, 1:-1, 1:-1]
    speed_list = [wall_speed[0], wall_speed[1], wall_speed[2]]
    correction = per_direction([6.0 * w for w in lattice_weight]) * project_all(speed_list)
    result = inside * (opened * upstream + bounce * (reflected + correction))
    return result.astype(jnp.bfloat16)


def basis_weights(received, node_positions, tile_lists):
    tile_count = tile_lists.shape[0]
    tile_width = received.shape[2]
    chosen = received[tile_lists]
    nodes_at = node_positions.reshape(3, tile_count, tile_width)
    distance = jnp.zeros((tile_count, tile_width, tile_lists.shape[1], tile_width), jnp.float32)
    for component in range(3):
        offset = nodes_at[component][:, :, None, None] - chosen[:, None, :, 3 + component, :]
        distance = distance + offset * offset
    kernel = 1.0 / jnp.sqrt(1.0 + distance / (basis_radius * basis_radius))
    column = jnp.sum(kernel, axis=1)
    totals = (
        jnp.zeros((received.shape[0], tile_width), jnp.float32)
        .at[tile_lists.reshape(-1)]
        .add(column.reshape(-1, tile_width))
    )
    return (kernel / totals[tile_lists][:, None, :, :], chosen)


def map_tractions(weights, chosen, node_index, nodes_total):
    mapped = jnp.einsum(
        "anbp,abcp->can", weights, chosen[:, :, 0:3, :], precision=lax.Precision.HIGHEST
    )
    return jnp.zeros((3, nodes_total), jnp.float32).at[:, node_index].add(mapped.reshape(3, -1))


def map_speeds(weights, solution_flat, node_index, tile_lists, tile_slots):
    tile_count = weights.shape[0]
    tile_width = weights.shape[1]
    at_nodes = solution_flat[:, node_index].reshape(3, tile_count, tile_width)
    contrib = jnp.einsum("anbp,can->abcp", weights, at_nodes, precision=lax.Precision.HIGHEST)
    return (
        jnp.zeros((tile_slots, 3, tile_width), jnp.float32)
        .at[tile_lists.reshape(-1)]
        .add(contrib.reshape(-1, 3, tile_width))
    )


def element_sum(widened, matrix):
    span_cells = widened.shape[1] - 2
    across_cells = widened.shape[2] - 2
    deep_cells = widened.shape[3]
    widened_z = jnp.pad(widened, ((0, 0), (0, 0), (0, 0), (0, 1)))
    corners = [(a, b, c) for a in (0, 1) for b in (0, 1) for c in (0, 1)]
    gathered = jnp.concatenate(
        [
            widened_z[0:3, a : a + span_cells + 1, b : b + across_cells + 1, c : c + deep_cells]
            for a, b, c in corners
        ],
        axis=0,
    )
    element_scale = widened_z[3, 0 : span_cells + 1, 0 : across_cells + 1, 0:deep_cells]
    forces = element_scale * jnp.einsum(
        "ij,jabc->iabc", matrix, gathered, precision=lax.Precision.HIGHEST
    )
    summed = jnp.zeros((3, span_cells + 2, across_cells + 2, deep_cells + 1), jnp.float32)
    for corner_id, (a, b, c) in enumerate(corners):
        summed = summed.at[
            :, a : a + span_cells + 1, b : b + across_cells + 1, c : c + deep_cells
        ].add(forces[3 * corner_id : 3 * corner_id + 3])
    return summed[:, 1 : span_cells + 1, 1 : across_cells + 1, 0:deep_cells]


def operator_kernel(matrix_ref, values_ref, stiff_ref, out_ref):
    span_cells, across_cells, deep_cells = stiff_ref.shape
    across_at = lax.broadcasted_iota(jnp.int32, (across_cells, deep_cells), 0)
    deep_at = lax.broadcasted_iota(jnp.int32, (across_cells, deep_cells), 1)
    corners = [(a, b, c) for a in (0, 1) for b in (0, 1) for c in (0, 1)]
    for component in range(3):
        out_ref[component, 0:span_cells] = mass_shift * values_ref[component, 0:span_cells]
        out_ref[component, span_cells] = jnp.zeros((across_cells, deep_cells), jnp.float32)

    def ahead(value, across, deep):
        if across:
            value = jnp.where(
                across_at < across_cells - 1, pltpu.roll(value, across_cells - 1, 0), 0.0
            )
        if deep:
            value = jnp.where(deep_at < deep_cells - 1, pltpu.roll(value, deep_cells - 1, 1), 0.0)
        return value

    def behind(value, across, deep):
        if across:
            value = jnp.where(across_at >= 1, pltpu.roll(value, 1, 0), 0.0)
        if deep:
            value = jnp.where(deep_at >= 1, pltpu.roll(value, 1, 1), 0.0)
        return value

    def element_row(row, carry):
        gathered = []
        for a, b, c in corners:
            for component in range(3):
                gathered.append(ahead(values_ref[component, row + a], b, c))
        scale = stiff_ref[row]
        for corner_id, (a, b, c) in enumerate(corners):
            for component in range(3):
                line = 3 * corner_id + component
                force = matrix_ref[line * 24] * gathered[0]
                for other in range(1, 24):
                    force = force + matrix_ref[line * 24 + other] * gathered[other]
                out_ref[component, row + a] += behind(scale * force, b, c)
        return carry

    lax.fori_loop(0, span_cells, element_row, 0)


def partition_operator(values, stiffness, matrix):
    span_cells, across_cells, deep_cells = stiffness.shape
    widened = jnp.pad(values, ((0, 0), (0, 1), (0, 0), (0, 0)))
    cells = span_cells * across_cells * deep_cells
    summed = pl.pallas_call(
        operator_kernel,
        out_shape=jax.ShapeDtypeStruct(widened.shape, jnp.float32),
        in_specs=[
            pl.BlockSpec(memory_space=pltpu.SMEM),
            pl.BlockSpec(memory_space=pltpu.VMEM),
            pl.BlockSpec(memory_space=pltpu.VMEM),
        ],
        out_specs=pl.BlockSpec(memory_space=pltpu.VMEM),
        cost_estimate=pl.CostEstimate(
            flops=2 * 24 * 24 * cells, transcendentals=0, bytes_accessed=28 * cells
        ),
    )(matrix.reshape(-1), widened, stiffness)
    return summed[:, :span_cells]


def whole_partition(block):
    lead = block.shape[:-3]
    count = len(lead)
    every = lax.all_gather(block, "gy", axis=count + 1, tiled=True)
    return lax.all_gather(every, "gx", axis=count, tiled=True)


def own_part(whole, rows, cols):
    start = (0, lax.axis_index("gx") * rows, lax.axis_index("gy") * cols, 0)
    return lax.dynamic_slice(whole, start, (whole.shape[0], rows, cols, whole.shape[3]))


def solve_structure(right_side, operator, products):
    residual = right_side
    image_vec = operator(residual)
    norm_now, curvature = products(residual, image_vec)
    step_size = norm_now / curvature
    direction, image_dir = (residual, image_vec)
    solution = jnp.zeros_like(right_side)
    for iteration in range(ITERS):
        solution = solution + step_size * direction
        residual = residual - step_size * image_dir
        if iteration + 1 < ITERS:
            image_vec = operator(residual)
            norm_next, curvature = products(residual, image_vec)
            beta_ratio = norm_next / norm_now
            step_size = norm_next / (curvature - beta_ratio * norm_next / step_size)
            direction = residual + beta_ratio * direction
            image_dir = image_vec + beta_ratio * image_dir
            norm_now = norm_next
    return solution


def per_device(
    populations,
    solid_mask,
    wall_cells,
    body_load,
    elem_scale,
    elem_active,
    elem_matrix,
    iface_nodes,
    iface_coords,
    neighbours,
):
    group_count = lax.axis_size("group")
    span_devices = lax.axis_size("gx")
    struct_groups = max(1, group_count // 8)
    fluid_groups = group_count - struct_groups
    group_index = lax.axis_index("group")
    slab_index = group_index * span_devices + lax.axis_index("gx")
    column_index = lax.axis_index("gy")
    is_fluid = group_index < fluid_groups
    is_struct = jnp.logical_not(is_fluid)
    span_cells, across_cells, deep_cells = solid_mask.shape
    cell_count = span_cells * across_cells * deep_cells
    fluid_here = jnp.where(is_fluid, 1.0 - solid_mask.astype(jnp.float32), 0.0)
    relaxed_pops = jnp.where(
        is_fluid, collide(populations.astype(jnp.float32)), 0.0
    ).astype(jnp.bfloat16)
    marker = fluid_here.astype(jnp.bfloat16)[None]
    widened = halo_exchange(jnp.concatenate([relaxed_pops, marker], axis=0))
    widened = jnp.pad(widened, ((0, 0), (0, 0), (0, 0), (1, 1))).astype(jnp.float32)
    moved = widened[0:19]
    fluid_ext = widened[19]
    wall_index = wall_cells.reshape(-1)
    point_count = wall_index.shape[0]
    tiles_out = point_count // TILE

    def fluid_pack(operands):
        upstream, opened, bounce, reflected = stream_links(operands[0], operands[1])
        force_parts = wall_force(bounce, reflected).reshape(3, cell_count)
        picked = force_parts[:, wall_index]
        span_pos = wall_index // (across_cells * deep_cells)
        across_pos = wall_index // deep_cells % across_cells + column_index * across_cells
        deep_pos = wall_index % deep_cells
        positions = jnp.stack(
            [
                (slab_index * span_cells + span_pos).astype(jnp.float32),
                across_pos.astype(jnp.float32),
                deep_pos.astype(jnp.float32),
            ]
        )
        packed = jnp.concatenate([picked, positions], axis=0)
        return packed.reshape(6, tiles_out, TILE).transpose(1, 0, 2)

    packed = lax.cond(
        is_fluid,
        fluid_pack,
        lambda operands: jnp.zeros((tiles_out, 6, TILE), jnp.float32),
        (moved, fluid_ext),
    )
    received = lax.all_gather(packed, "group", axis=0, tiled=True)
    node_index = iface_nodes.reshape(-1)
    node_positions = iface_coords.reshape(3, -1)
    tile_lists = neighbours.reshape(neighbours.shape[2], neighbours.shape[3])
    nodes_total = body_load.shape[1] * body_load.shape[2] * body_load.shape[3]
    weight_shape = (tile_lists.shape[0], TILE, tile_lists.shape[1], TILE)

    def struct_map(received_all):
        weights, chosen = basis_weights(received_all, node_positions, tile_lists)
        mapped = map_tractions(weights, chosen, node_index, nodes_total)
        return (weights, body_load + mapped.reshape(body_load.shape))

    def struct_quiet(received_all):
        return (jnp.zeros(weight_shape, jnp.float32), jnp.zeros_like(body_load))

    weights, right_side = lax.cond(is_struct, struct_map, struct_quiet, received)
    stiffness = elem_scale * elem_active.astype(jnp.float32)
    joined = whole_partition(jnp.concatenate([right_side, stiffness[None]], axis=0))
    whole_side = joined[0:3]
    stiffness = joined[3]
    rows, cols = body_load.shape[1], body_load.shape[2]

    def partition_products(first_vec, second_vec):
        pair = (jnp.sum(first_vec * first_vec), jnp.sum(first_vec * second_vec))
        if struct_groups > 1:
            pair = lax.psum(tuple(jnp.where(is_struct, x, 0.0) for x in pair), "group")
        return pair

    def partition_solve(operands):
        side, stiff, matrix = operands
        return solve_structure(
            side, lambda values: partition_operator(values, stiff, matrix), partition_products
        )

    if struct_groups > 1:
        whole_solution = partition_solve((whole_side, stiffness, elem_matrix))
    else:
        whole_solution = lax.cond(
            is_struct,
            partition_solve,
            lambda operands: jnp.zeros_like(operands[0]),
            (whole_side, stiffness, elem_matrix),
        )
    solution = jnp.where(is_struct, own_part(whole_solution, rows, cols), 0.0)
    tile_slots = received.shape[0]

    def struct_back(operands):
        return map_speeds(
            operands[0], operands[1].reshape(3, nodes_total), node_index, tile_lists, tile_slots
        )

    back_terms = lax.cond(
        is_struct,
        struct_back,
        lambda operands: jnp.zeros((tile_slots, 3, TILE), jnp.float32),
        (weights, solution),
    )
    per_group = tile_slots // group_count
    route_count = fluid_groups // struct_groups
    sender_slot = jnp.clip(group_index - fluid_groups, 0, struct_groups - 1)
    own_speeds = jnp.zeros((per_group, 3, TILE), jnp.float32)
    for route_step in range(route_count):
        offset_row = (sender_slot + route_step * struct_groups) * per_group
        outgoing = lax.dynamic_slice_in_dim(back_terms, offset_row, per_group, 0)
        incoming = passed_along(outgoing, "group", (route_step + 1) * struct_groups)
        own_speeds = own_speeds + jnp.where(
            group_index // struct_groups == route_step, incoming, 0.0
        )
    speed_parts = wall_gain * own_speeds.transpose(1, 0, 2).reshape(3, point_count)
    wall_speed = jnp.zeros((3, cell_count), jnp.float32).at[:, wall_index].add(speed_parts)
    wall_speed = wall_speed.reshape(3, span_cells, across_cells, deep_cells)
    new_populations = lax.cond(
        is_fluid,
        lambda operands: stream_all(operands[0], operands[1], operands[2]),
        lambda operands: jnp.zeros(operands[0][:, 1:-1, 1:-1, 1:-1].shape, jnp.bfloat16),
        (moved, fluid_ext, wall_speed),
    )
    return (new_populations, solution)


def solution(mesh):
    placed = (
        P(None, ("group", "gx"), "gy", None),
        P(("group", "gx"), "gy", None),
        P(("group", "gx"), "gy", None),
        P(None, ("group", "gx"), "gy", None),
        P(("group", "gx"), "gy", None),
        P(("group", "gx"), "gy", None),
        P(),
        P(("group", "gx"), "gy", None),
        P(None, ("group", "gx"), "gy", None),
        P(("group", "gx"), "gy", None, None),
    )
    return jax.shard_map(
        per_device,
        mesh=mesh,
        in_specs=placed,
        out_specs=(P(None, ("group", "gx"), "gy", None), P(None, ("group", "gx"), "gy", None)),
        check_vma=False,
    )
```

```python
import jax
import jax.numpy as jnp
import numpy as np
from jax import lax
from jax.sharding import PartitionSpec as P
from jax.experimental import pallas as pl
from jax.experimental.pallas import tpu as pltpu

TILE = 128
ITERS = 3


velocity = [
    (0, 0, 0),
    (1, 0, 0),
    (-1, 0, 0),
    (0, 1, 0),
    (0, -1, 0),
    (0, 0, 1),
    (0, 0, -1),
    (1, 1, 0),
    (-1, -1, 0),
    (1, -1, 0),
    (-1, 1, 0),
    (1, 0, 1),
    (-1, 0, -1),
    (1, 0, -1),
    (-1, 0, 1),
    (0, 1, 1),
    (0, -1, -1),
    (0, 1, -1),
    (0, -1, 1),
]
opposite = [0, 2, 1, 4, 3, 6, 5, 8, 7, 10, 9, 12, 11, 14, 13, 16, 15, 18, 17]
lattice_weight = [1.0 / 3.0] + [1.0 / 18.0] * 6 + [1.0 / 36.0] * 12
relax_rate = 1.0 / 0.6
wall_gain = 60.0
basis_radius = 24.0
mass_shift = 0.5


def halo_exchange(cells):
    span_devices = lax.axis_size(("group", "gx"))
    columns = lax.axis_size("gy")
    rows, cols = cells.shape[1], cells.shape[2]
    row_pick = {1: slice(rows - 1, rows), 0: slice(0, rows), -1: slice(0, 1)}
    col_pick = {1: slice(cols - 1, cols), 0: slice(0, cols), -1: slice(0, 1)}
    received = {}
    for dr in (-1, 0, 1):
        for dc in (-1, 0, 1):
            if dr == 0 and dc == 0:
                received[(dr, dc)] = cells
                continue
            pairs = [
                (r * columns + c, (r + dr) * columns + c + dc)
                for r in range(span_devices)
                for c in range(columns)
                if 0 <= r + dr < span_devices and 0 <= c + dc < columns
            ]
            piece = cells[:, row_pick[dr], col_pick[dc]]
            received[(dr, dc)] = lax.ppermute(piece, ("group", "gx", "gy"), pairs)
    bands = [
        jnp.concatenate([received[(dr, dc)] for dc in (1, 0, -1)], axis=2) for dr in (1, 0, -1)
    ]
    return jnp.concatenate(bands, axis=1)


def passed_along(value, axis, steps):
    count = lax.axis_size(axis)
    pairs = [(source, (source + steps) % count) for source in range(count)]
    return lax.ppermute(value, axis, pairs)


def project_onto(vectors, direction):
    summed = jnp.zeros_like(vectors[0])
    for component in range(3):
        if direction[component] != 0:
            summed = summed + float(direction[component]) * vectors[component]
    return summed


def per_direction(values):
    return jnp.asarray(np.array(values, np.float32).reshape(19, 1, 1, 1))


def collide(population):
    density = jnp.sum(population, axis=0)
    velocity_parts = [
        jnp.sum(per_direction([c[component] for c in velocity]) * population, axis=0) / density
        for component in range(3)
    ]
    speed_square = (
        velocity_parts[0] * velocity_parts[0]
        + velocity_parts[1] * velocity_parts[1]
        + velocity_parts[2] * velocity_parts[2]
    )
    project = project_all(velocity_parts)
    balance = (
        per_direction(lattice_weight)
        * density
        * (1.0 + 3.0 * project + 4.5 * project * project - 1.5 * speed_square)
    )
    return population + relax_rate * (balance - population)


def project_all(vectors):
    summed = per_direction([c[0] for c in velocity]) * vectors[0]
    for component in (1, 2):
        summed = summed + per_direction([c[component] for c in velocity]) * vectors[component]
    return summed


def upstream_of(values, inner):
    for axis in range(3):
        shift = per_direction([c[axis] for c in velocity])
        pick = {
            s: lax.slice_in_dim(values, 1 - s, 1 - s + inner[axis], axis=axis + 1)
            for s in (-1, 0, 1)
        }
        values = jnp.where(shift > 0.5, pick[1], jnp.where(shift < -0.5, pick[-1], pick[0]))
    return values


def stream_links(moved, fluid_ext):
    inner = tuple(size - 2 for size in fluid_ext.shape)
    upstream = upstream_of(moved, inner)
    opened = upstream_of(jnp.broadcast_to(fluid_ext[None], (19,) + fluid_ext.shape), inner)
    bounce = 1.0 - opened
    centre = moved[:, 1 : inner[0] + 1, 1 : inner[1] + 1, 1 : inner[2] + 1]
    paired = centre[1:].reshape((9, 2) + inner)[:, ::-1].reshape((18,) + inner)
    reflected = jnp.concatenate([centre[0:1], paired], axis=0)
    return (upstream, opened, bounce, reflected)


def wall_force(bounce, reflected):
    carried = bounce * reflected
    return jnp.stack(
        [
            jnp.sum(per_direction([-2.0 * c[component] for c in velocity]) * carried, axis=0)
            for component in range(3)
        ]
    )


def stream_all(moved, fluid_ext, wall_speed):
    upstream, opened, bounce, reflected = stream_links(moved, fluid_ext)
    inside = fluid_ext[1:-1, 1:-1, 1:-1]
    speed_list = [wall_speed[0], wall_speed[1], wall_speed[2]]
    correction = per_direction([6.0 * w for w in lattice_weight]) * project_all(speed_list)
    result = inside * (opened * upstream + bounce * (reflected + correction))
    return result.astype(jnp.bfloat16)


def basis_weights(received, node_positions, tile_lists):
    tile_count = tile_lists.shape[0]
    tile_width = received.shape[2]
    chosen = received[tile_lists]
    nodes_at = node_positions.reshape(3, tile_count, tile_width)
    distance = jnp.zeros((tile_count, tile_width, tile_lists.shape[1], tile_width), jnp.float32)
    for component in range(3):
        offset = nodes_at[component][:, :, None, None] - chosen[:, None, :, 3 + component, :]
        distance = distance + offset * offset
    kernel = 1.0 / jnp.sqrt(1.0 + distance / (basis_radius * basis_radius))
    column = jnp.sum(kernel, axis=1)
    totals = (
        jnp.zeros((received.shape[0], tile_width), jnp.float32)
        .at[tile_lists.reshape(-1)]
        .add(column.reshape(-1, tile_width))
    )
    return (kernel / totals[tile_lists][:, None, :, :], chosen)


def map_tractions(weights, chosen, node_index, nodes_total):
    mapped = jnp.einsum(
        "anbp,abcp->can", weights, chosen[:, :, 0:3, :], precision=lax.Precision.HIGHEST
    )
    return jnp.zeros((3, nodes_total), jnp.float32).at[:, node_index].add(mapped.reshape(3, -1))


def map_speeds(weights, solution_flat, node_index, tile_lists, tile_slots):
    tile_count = weights.shape[0]
    tile_width = weights.shape[1]
    at_nodes = solution_flat[:, node_index].reshape(3, tile_count, tile_width)
    contrib = jnp.einsum("anbp,can->abcp", weights, at_nodes, precision=lax.Precision.HIGHEST)
    return (
        jnp.zeros((tile_slots, 3, tile_width), jnp.float32)
        .at[tile_lists.reshape(-1)]
        .add(contrib.reshape(-1, 3, tile_width))
    )


def element_sum(widened, matrix):
    span_cells = widened.shape[1] - 2
    across_cells = widened.shape[2] - 2
    deep_cells = widened.shape[3]
    widened_z = jnp.pad(widened, ((0, 0), (0, 0), (0, 0), (0, 1)))
    corners = [(a, b, c) for a in (0, 1) for b in (0, 1) for c in (0, 1)]
    gathered = jnp.concatenate(
        [
            widened_z[0:3, a : a + span_cells + 1, b : b + across_cells + 1, c : c + deep_cells]
            for a, b, c in corners
        ],
        axis=0,
    )
    element_scale = widened_z[3, 0 : span_cells + 1, 0 : across_cells + 1, 0:deep_cells]
    forces = element_scale * jnp.einsum(
        "ij,jabc->iabc", matrix, gathered, precision=lax.Precision.HIGHEST
    )
    summed = jnp.zeros((3, span_cells + 2, across_cells + 2, deep_cells + 1), jnp.float32)
    for corner_id, (a, b, c) in enumerate(corners):
        summed = summed.at[
            :, a : a + span_cells + 1, b : b + across_cells + 1, c : c + deep_cells
        ].add(forces[3 * corner_id : 3 * corner_id + 3])
    return summed[:, 1 : span_cells + 1, 1 : across_cells + 1, 0:deep_cells]


def apply_rows(matrix_ref, values_ref, stiff_ref, out_ref):
    span_cells, across_cells, deep_cells = stiff_ref.shape
    step = 2 if span_cells % 2 == 0 else 1
    shape = (step, across_cells, deep_cells)
    across_at = lax.broadcasted_iota(jnp.int32, shape, 1)
    deep_at = lax.broadcasted_iota(jnp.int32, shape, 2)
    corners = [(a, b, c) for a in (0, 1) for b in (0, 1) for c in (0, 1)]
    for component in range(3):
        out_ref[component, 0:span_cells] = mass_shift * values_ref[component, 0:span_cells]
        out_ref[component, span_cells] = jnp.zeros((across_cells, deep_cells), jnp.float32)

    def ahead(value, across, deep):
        if across:
            value = jnp.where(
                across_at < across_cells - 1, pltpu.roll(value, across_cells - 1, 1), 0.0
            )
        if deep:
            value = jnp.where(deep_at < deep_cells - 1, pltpu.roll(value, deep_cells - 1, 2), 0.0)
        return value

    def behind(value, across, deep):
        if across:
            value = jnp.where(across_at >= 1, pltpu.roll(value, 1, 1), 0.0)
        if deep:
            value = jnp.where(deep_at >= 1, pltpu.roll(value, 1, 2), 0.0)
        return value

    def element_rows(block, carry):
        row = block * step
        gathered = []
        for a, b, c in corners:
            for component in range(3):
                gathered.append(ahead(values_ref[component, pl.ds(row + a, step)], b, c))
        scale = stiff_ref[pl.ds(row, step)]
        for corner_id, (a, b, c) in enumerate(corners):
            for component in range(3):
                line = 3 * corner_id + component
                force = matrix_ref[line * 24] * gathered[0]
                for other in range(1, 24):
                    force = force + matrix_ref[line * 24 + other] * gathered[other]
                out_ref[component, pl.ds(row + a, step)] += behind(scale * force, b, c)
        return carry

    lax.fori_loop(0, span_cells // step, element_rows, 0)


def operator_kernel(matrix_ref, values_ref, stiff_ref, out_ref):
    apply_rows(matrix_ref, values_ref, stiff_ref, out_ref)


def whole_sum(value):
    value = jnp.sum(value, axis=(0, 1))
    value = jnp.sum(value, axis=0, keepdims=True)
    return jnp.sum(value, axis=1, keepdims=True)


def solve_kernel(matrix_ref, side_ref, stiff_ref, out_ref, ahead_ref, image_ref, dir_ref, img_ref):
    span_cells = stiff_ref.shape[0]
    residual = side_ref[...]
    ahead_ref[:, 0:span_cells] = residual
    ahead_ref[:, span_cells : span_cells + 1] = jnp.zeros_like(residual[:, 0:1])
    apply_rows(matrix_ref, ahead_ref, stiff_ref, image_ref)
    image_vec = image_ref[:, 0:span_cells]
    norm_now = whole_sum(residual * residual)
    step_size = norm_now / whole_sum(residual * image_vec)
    dir_ref[...] = residual
    img_ref[...] = image_vec
    out_ref[...] = jnp.zeros_like(residual)
    for iteration in range(ITERS):
        out_ref[...] = out_ref[...] + step_size * dir_ref[...]
        residual = residual - step_size * img_ref[...]
        if iteration + 1 < ITERS:
            ahead_ref[:, 0:span_cells] = residual
            apply_rows(matrix_ref, ahead_ref, stiff_ref, image_ref)
            image_vec = image_ref[:, 0:span_cells]
            norm_next = whole_sum(residual * residual)
            curvature = whole_sum(residual * image_vec)
            beta_ratio = norm_next / norm_now
            step_size = norm_next / (curvature - beta_ratio * norm_next / step_size)
            dir_ref[...] = residual + beta_ratio * dir_ref[...]
            img_ref[...] = image_vec + beta_ratio * img_ref[...]
            norm_now = norm_next


def partition_solve_kernel(side, stiffness, matrix):
    span_cells, across_cells, deep_cells = stiffness.shape
    cells = span_cells * across_cells * deep_cells
    wide = (3, span_cells + 1, across_cells, deep_cells)
    return pl.pallas_call(
        solve_kernel,
        out_shape=jax.ShapeDtypeStruct(side.shape, jnp.float32),
        in_specs=[
            pl.BlockSpec(memory_space=pltpu.SMEM),
            pl.BlockSpec(memory_space=pltpu.VMEM),
            pl.BlockSpec(memory_space=pltpu.VMEM),
        ],
        out_specs=pl.BlockSpec(memory_space=pltpu.VMEM),
        scratch_shapes=[
            pltpu.VMEM(wide, jnp.float32),
            pltpu.VMEM(wide, jnp.float32),
            pltpu.VMEM(side.shape, jnp.float32),
            pltpu.VMEM(side.shape, jnp.float32),
        ],
        cost_estimate=pl.CostEstimate(
            flops=ITERS * 2 * 24 * 24 * cells, transcendentals=0, bytes_accessed=28 * cells
        ),
    )(matrix.reshape(-1), side, stiffness)


def partition_operator(values, stiffness, matrix):
    span_cells, across_cells, deep_cells = stiffness.shape
    widened = jnp.pad(values, ((0, 0), (0, 1), (0, 0), (0, 0)))
    cells = span_cells * across_cells * deep_cells
    summed = pl.pallas_call(
        operator_kernel,
        out_shape=jax.ShapeDtypeStruct(widened.shape, jnp.float32),
        in_specs=[
            pl.BlockSpec(memory_space=pltpu.SMEM),
            pl.BlockSpec(memory_space=pltpu.VMEM),
            pl.BlockSpec(memory_space=pltpu.VMEM),
        ],
        out_specs=pl.BlockSpec(memory_space=pltpu.VMEM),
        cost_estimate=pl.CostEstimate(
            flops=2 * 24 * 24 * cells, transcendentals=0, bytes_accessed=28 * cells
        ),
    )(matrix.reshape(-1), widened, stiffness)
    return summed[:, :span_cells]


def whole_partition(block):
    lead = block.shape[:-3]
    count = len(lead)
    every = lax.all_gather(block, "gy", axis=count + 1, tiled=True)
    return lax.all_gather(every, "gx", axis=count, tiled=True)


def own_part(whole, rows, cols):
    start = (0, lax.axis_index("gx") * rows, lax.axis_index("gy") * cols, 0)
    return lax.dynamic_slice(whole, start, (whole.shape[0], rows, cols, whole.shape[3]))


def solve_structure(right_side, operator, products):
    residual = right_side
    image_vec = operator(residual)
    norm_now, curvature = products(residual, image_vec)
    step_size = norm_now / curvature
    direction, image_dir = (residual, image_vec)
    solution = jnp.zeros_like(right_side)
    for iteration in range(ITERS):
        solution = solution + step_size * direction
        residual = residual - step_size * image_dir
        if iteration + 1 < ITERS:
            image_vec = operator(residual)
            norm_next, curvature = products(residual, image_vec)
            beta_ratio = norm_next / norm_now
            step_size = norm_next / (curvature - beta_ratio * norm_next / step_size)
            direction = residual + beta_ratio * direction
            image_dir = image_vec + beta_ratio * image_dir
            norm_now = norm_next
    return solution


def per_device(
    populations,
    solid_mask,
    wall_cells,
    body_load,
    elem_scale,
    elem_active,
    elem_matrix,
    iface_nodes,
    iface_coords,
    neighbours,
):
    group_count = lax.axis_size("group")
    span_devices = lax.axis_size("gx")
    struct_groups = max(1, group_count // 8)
    fluid_groups = group_count - struct_groups
    group_index = lax.axis_index("group")
    slab_index = group_index * span_devices + lax.axis_index("gx")
    column_index = lax.axis_index("gy")
    is_fluid = group_index < fluid_groups
    is_struct = jnp.logical_not(is_fluid)
    span_cells, across_cells, deep_cells = solid_mask.shape
    cell_count = span_cells * across_cells * deep_cells
    fluid_here = jnp.where(is_fluid, 1.0 - solid_mask.astype(jnp.float32), 0.0)
    relaxed_pops = jnp.where(
        is_fluid, collide(populations.astype(jnp.float32)), 0.0
    ).astype(jnp.bfloat16)
    marker = fluid_here.astype(jnp.bfloat16)[None]
    widened = halo_exchange(jnp.concatenate([relaxed_pops, marker], axis=0))
    widened = jnp.pad(widened, ((0, 0), (0, 0), (0, 0), (1, 1))).astype(jnp.float32)
    moved = widened[0:19]
    fluid_ext = widened[19]
    wall_index = wall_cells.reshape(-1)
    point_count = wall_index.shape[0]
    tiles_out = point_count // TILE

    def fluid_pack(operands):
        upstream, opened, bounce, reflected = stream_links(operands[0], operands[1])
        force_parts = wall_force(bounce, reflected).reshape(3, cell_count)
        picked = force_parts[:, wall_index]
        span_pos = wall_index // (across_cells * deep_cells)
        across_pos = wall_index // deep_cells % across_cells + column_index * across_cells
        deep_pos = wall_index % deep_cells
        positions = jnp.stack(
            [
                (slab_index * span_cells + span_pos).astype(jnp.float32),
                across_pos.astype(jnp.float32),
                deep_pos.astype(jnp.float32),
            ]
        )
        packed = jnp.concatenate([picked, positions], axis=0)
        return packed.reshape(6, tiles_out, TILE).transpose(1, 0, 2)

    packed = lax.cond(
        is_fluid,
        fluid_pack,
        lambda operands: jnp.zeros((tiles_out, 6, TILE), jnp.float32),
        (moved, fluid_ext),
    )
    received = lax.all_gather(packed, "group", axis=0, tiled=True)
    node_index = iface_nodes.reshape(-1)
    node_positions = iface_coords.reshape(3, -1)
    tile_lists = neighbours.reshape(neighbours.shape[2], neighbours.shape[3])
    nodes_total = body_load.shape[1] * body_load.shape[2] * body_load.shape[3]
    weight_shape = (tile_lists.shape[0], TILE, tile_lists.shape[1], TILE)

    def struct_map(received_all):
        weights, chosen = basis_weights(received_all, node_positions, tile_lists)
        mapped = map_tractions(weights, chosen, node_index, nodes_total)
        return (weights, body_load + mapped.reshape(body_load.shape))

    def struct_quiet(received_all):
        return (jnp.zeros(weight_shape, jnp.float32), jnp.zeros_like(body_load))

    weights, right_side = lax.cond(is_struct, struct_map, struct_quiet, received)
    stiffness = elem_scale * elem_active.astype(jnp.float32)
    joined = whole_partition(jnp.concatenate([right_side, stiffness[None]], axis=0))
    whole_side = joined[0:3]
    stiffness = joined[3]
    rows, cols = body_load.shape[1], body_load.shape[2]

    def partition_products(first_vec, second_vec):
        pair = (jnp.sum(first_vec * first_vec), jnp.sum(first_vec * second_vec))
        if struct_groups > 1:
            pair = lax.psum(tuple(jnp.where(is_struct, x, 0.0) for x in pair), "group")
        return pair

    def partition_solve(operands):
        side, stiff, matrix = operands
        return solve_structure(
            side, lambda values: partition_operator(values, stiff, matrix), partition_products
        )

    if struct_groups > 1:
        whole_solution = partition_solve((whole_side, stiffness, elem_matrix))
    else:
        whole_solution = lax.cond(
            is_struct,
            lambda operands: partition_solve_kernel(*operands),
            lambda operands: jnp.zeros_like(operands[0]),
            (whole_side, stiffness, elem_matrix),
        )
    solution = jnp.where(is_struct, own_part(whole_solution, rows, cols), 0.0)
    tile_slots = received.shape[0]

    def struct_back(operands):
        return map_speeds(
            operands[0], operands[1].reshape(3, nodes_total), node_index, tile_lists, tile_slots
        )

    back_terms = lax.cond(
        is_struct,
        struct_back,
        lambda operands: jnp.zeros((tile_slots, 3, TILE), jnp.float32),
        (weights, solution),
    )
    per_group = tile_slots // group_count
    route_count = fluid_groups // struct_groups
    sender_slot = jnp.clip(group_index - fluid_groups, 0, struct_groups - 1)
    own_speeds = jnp.zeros((per_group, 3, TILE), jnp.float32)
    for route_step in range(route_count):
        offset_row = (sender_slot + route_step * struct_groups) * per_group
        outgoing = lax.dynamic_slice_in_dim(back_terms, offset_row, per_group, 0)
        incoming = passed_along(outgoing, "group", (route_step + 1) * struct_groups)
        own_speeds = own_speeds + jnp.where(
            group_index // struct_groups == route_step, incoming, 0.0
        )
    speed_parts = wall_gain * own_speeds.transpose(1, 0, 2).reshape(3, point_count)
    wall_speed = jnp.zeros((3, cell_count), jnp.float32).at[:, wall_index].add(speed_parts)
    wall_speed = wall_speed.reshape(3, span_cells, across_cells, deep_cells)
    new_populations = lax.cond(
        is_fluid,
        lambda operands: stream_all(operands[0], operands[1], operands[2]),
        lambda operands: jnp.zeros(operands[0][:, 1:-1, 1:-1, 1:-1].shape, jnp.bfloat16),
        (moved, fluid_ext, wall_speed),
    )
    return (new_populations, solution)


def solution(mesh):
    placed = (
        P(None, ("group", "gx"), "gy", None),
        P(("group", "gx"), "gy", None),
        P(("group", "gx"), "gy", None),
        P(None, ("group", "gx"), "gy", None),
        P(("group", "gx"), "gy", None),
        P(("group", "gx"), "gy", None),
        P(),
        P(("group", "gx"), "gy", None),
        P(None, ("group", "gx"), "gy", None),
        P(("group", "gx"), "gy", None, None),
    )
    return jax.shard_map(
        per_device,
        mesh=mesh,
        in_specs=placed,
        out_specs=(P(None, ("group", "gx"), "gy", None), P(None, ("group", "gx"), "gy", None)),
        check_vma=False,
    )
```

```python
import jax
import jax.numpy as jnp
import numpy as np
from jax import lax
from jax.sharding import PartitionSpec as P
from jax.experimental import pallas as pl
from jax.experimental.pallas import tpu as pltpu

TILE = 128
ITERS = 3


velocity = [
    (0, 0, 0),
    (1, 0, 0),
    (-1, 0, 0),
    (0, 1, 0),
    (0, -1, 0),
    (0, 0, 1),
    (0, 0, -1),
    (1, 1, 0),
    (-1, -1, 0),
    (1, -1, 0),
    (-1, 1, 0),
    (1, 0, 1),
    (-1, 0, -1),
    (1, 0, -1),
    (-1, 0, 1),
    (0, 1, 1),
    (0, -1, -1),
    (0, 1, -1),
    (0, -1, 1),
]
opposite = [0, 2, 1, 4, 3, 6, 5, 8, 7, 10, 9, 12, 11, 14, 13, 16, 15, 18, 17]
lattice_weight = [1.0 / 3.0] + [1.0 / 18.0] * 6 + [1.0 / 36.0] * 12
relax_rate = 1.0 / 0.6
wall_gain = 60.0
basis_radius = 24.0
mass_shift = 0.5


def halo_exchange(cells, span_devices):
    columns = lax.axis_size("gy")
    rows, cols = cells.shape[1], cells.shape[2]
    row_pick = {1: slice(rows - 1, rows), 0: slice(0, rows), -1: slice(0, 1)}
    col_pick = {1: slice(cols - 1, cols), 0: slice(0, cols), -1: slice(0, 1)}
    received = {}
    for dr in (-1, 0, 1):
        for dc in (-1, 0, 1):
            if dr == 0 and dc == 0:
                received[(dr, dc)] = cells
                continue
            pairs = [
                (r * columns + c, (r + dr) * columns + c + dc)
                for r in range(span_devices)
                for c in range(columns)
                if 0 <= r + dr < span_devices and 0 <= c + dc < columns
            ]
            piece = cells[:, row_pick[dr], col_pick[dc]]
            received[(dr, dc)] = lax.ppermute(piece, ("group", "gx", "gy"), pairs)
    bands = [
        jnp.concatenate([received[(dr, dc)] for dc in (1, 0, -1)], axis=2) for dr in (1, 0, -1)
    ]
    return jnp.concatenate(bands, axis=1)


def passed_along(value, axis, steps):
    count = lax.axis_size(axis)
    pairs = [(source, (source + steps) % count) for source in range(count)]
    return lax.ppermute(value, axis, pairs)


def project_onto(vectors, direction):
    summed = jnp.zeros_like(vectors[0])
    for component in range(3):
        if direction[component] != 0:
            summed = summed + float(direction[component]) * vectors[component]
    return summed


def per_direction(values):
    return jnp.asarray(np.array(values, np.float32).reshape(19, 1, 1, 1))


def collide(population):
    density = jnp.sum(population, axis=0)
    velocity_parts = [
        jnp.sum(per_direction([c[component] for c in velocity]) * population, axis=0) / density
        for component in range(3)
    ]
    speed_square = (
        velocity_parts[0] * velocity_parts[0]
        + velocity_parts[1] * velocity_parts[1]
        + velocity_parts[2] * velocity_parts[2]
    )
    project = project_all(velocity_parts)
    balance = (
        per_direction(lattice_weight)
        * density
        * (1.0 + 3.0 * project + 4.5 * project * project - 1.5 * speed_square)
    )
    return population + relax_rate * (balance - population)


def project_all(vectors):
    summed = per_direction([c[0] for c in velocity]) * vectors[0]
    for component in (1, 2):
        summed = summed + per_direction([c[component] for c in velocity]) * vectors[component]
    return summed


def upstream_of(values, inner):
    for axis in range(3):
        shift = per_direction([c[axis] for c in velocity])
        pick = {
            s: lax.slice_in_dim(values, 1 - s, 1 - s + inner[axis], axis=axis + 1)
            for s in (-1, 0, 1)
        }
        values = jnp.where(shift > 0.5, pick[1], jnp.where(shift < -0.5, pick[-1], pick[0]))
    return values


def stream_links(moved, fluid_ext):
    inner = tuple(size - 2 for size in fluid_ext.shape)
    upstream = upstream_of(moved, inner)
    opened = upstream_of(jnp.broadcast_to(fluid_ext[None], (19,) + fluid_ext.shape), inner)
    bounce = 1.0 - opened
    centre = moved[:, 1 : inner[0] + 1, 1 : inner[1] + 1, 1 : inner[2] + 1]
    paired = centre[1:].reshape((9, 2) + inner)[:, ::-1].reshape((18,) + inner)
    reflected = jnp.concatenate([centre[0:1], paired], axis=0)
    return (upstream, opened, bounce, reflected)


def local_force(relaxed, fluid_ext):
    inner = relaxed.shape[1:]
    opened = upstream_of(jnp.broadcast_to(fluid_ext[None], (19,) + fluid_ext.shape), inner)
    paired = relaxed[1:].reshape((9, 2) + inner)[:, ::-1].reshape((18,) + inner)
    reflected = jnp.concatenate([relaxed[0:1], paired], axis=0)
    return wall_force(1.0 - opened, reflected)


def wall_force(bounce, reflected):
    carried = bounce * reflected
    return jnp.stack(
        [
            jnp.sum(per_direction([-2.0 * c[component] for c in velocity]) * carried, axis=0)
            for component in range(3)
        ]
    )


def stream_all(moved, fluid_ext, wall_speed):
    upstream, opened, bounce, reflected = stream_links(moved, fluid_ext)
    inside = fluid_ext[1:-1, 1:-1, 1:-1]
    speed_list = [wall_speed[0], wall_speed[1], wall_speed[2]]
    correction = per_direction([6.0 * w for w in lattice_weight]) * project_all(speed_list)
    result = inside * (opened * upstream + bounce * (reflected + correction))
    return result.astype(jnp.bfloat16)


def basis_weights(received, node_positions, tile_lists):
    tile_count = tile_lists.shape[0]
    tile_width = received.shape[2]
    chosen = received[tile_lists]
    nodes_at = node_positions.reshape(3, tile_count, tile_width)
    distance = jnp.zeros((tile_count, tile_width, tile_lists.shape[1], tile_width), jnp.float32)
    for component in range(3):
        offset = nodes_at[component][:, :, None, None] - chosen[:, None, :, 3 + component, :]
        distance = distance + offset * offset
    kernel = 1.0 / jnp.sqrt(1.0 + distance / (basis_radius * basis_radius))
    column = jnp.sum(kernel, axis=1)
    totals = (
        jnp.zeros((received.shape[0], tile_width), jnp.float32)
        .at[tile_lists.reshape(-1)]
        .add(column.reshape(-1, tile_width))
    )
    return (kernel / totals[tile_lists][:, None, :, :], chosen)


def map_tractions(weights, chosen, node_index, nodes_total):
    mapped = jnp.einsum(
        "anbp,abcp->can", weights, chosen[:, :, 0:3, :], precision=lax.Precision.HIGHEST
    )
    return jnp.zeros((3, nodes_total), jnp.float32).at[:, node_index].add(mapped.reshape(3, -1))


def map_speeds(weights, solution_flat, node_index, tile_lists, tile_slots):
    tile_count = weights.shape[0]
    tile_width = weights.shape[1]
    at_nodes = solution_flat[:, node_index].reshape(3, tile_count, tile_width)
    contrib = jnp.einsum("anbp,can->abcp", weights, at_nodes, precision=lax.Precision.HIGHEST)
    return (
        jnp.zeros((tile_slots, 3, tile_width), jnp.float32)
        .at[tile_lists.reshape(-1)]
        .add(contrib.reshape(-1, 3, tile_width))
    )


def element_sum(widened, matrix):
    span_cells = widened.shape[1] - 2
    across_cells = widened.shape[2] - 2
    deep_cells = widened.shape[3]
    widened_z = jnp.pad(widened, ((0, 0), (0, 0), (0, 0), (0, 1)))
    corners = [(a, b, c) for a in (0, 1) for b in (0, 1) for c in (0, 1)]
    gathered = jnp.concatenate(
        [
            widened_z[0:3, a : a + span_cells + 1, b : b + across_cells + 1, c : c + deep_cells]
            for a, b, c in corners
        ],
        axis=0,
    )
    element_scale = widened_z[3, 0 : span_cells + 1, 0 : across_cells + 1, 0:deep_cells]
    forces = element_scale * jnp.einsum(
        "ij,jabc->iabc", matrix, gathered, precision=lax.Precision.HIGHEST
    )
    summed = jnp.zeros((3, span_cells + 2, across_cells + 2, deep_cells + 1), jnp.float32)
    for corner_id, (a, b, c) in enumerate(corners):
        summed = summed.at[
            :, a : a + span_cells + 1, b : b + across_cells + 1, c : c + deep_cells
        ].add(forces[3 * corner_id : 3 * corner_id + 3])
    return summed[:, 1 : span_cells + 1, 1 : across_cells + 1, 0:deep_cells]


def apply_rows(matrix_ref, values_ref, stiff_ref, out_ref):
    span_cells, across_cells, deep_cells = stiff_ref.shape
    step = 2 if span_cells % 2 == 0 else 1
    shape = (step, across_cells, deep_cells)
    across_at = lax.broadcasted_iota(jnp.int32, shape, 1)
    deep_at = lax.broadcasted_iota(jnp.int32, shape, 2)
    corners = [(a, b, c) for a in (0, 1) for b in (0, 1) for c in (0, 1)]
    for component in range(3):
        out_ref[component, 0:span_cells] = mass_shift * values_ref[component, 0:span_cells]
        out_ref[component, span_cells] = jnp.zeros((across_cells, deep_cells), jnp.float32)

    def ahead(value, across, deep):
        if across:
            value = jnp.where(
                across_at < across_cells - 1, pltpu.roll(value, across_cells - 1, 1), 0.0
            )
        if deep:
            value = jnp.where(deep_at < deep_cells - 1, pltpu.roll(value, deep_cells - 1, 2), 0.0)
        return value

    def behind(value, across, deep):
        if across:
            value = jnp.where(across_at >= 1, pltpu.roll(value, 1, 1), 0.0)
        if deep:
            value = jnp.where(deep_at >= 1, pltpu.roll(value, 1, 2), 0.0)
        return value

    def element_rows(block, carry):
        row = block * step
        gathered = []
        for a, b, c in corners:
            for component in range(3):
                gathered.append(ahead(values_ref[component, pl.ds(row + a, step)], b, c))
        scale = stiff_ref[pl.ds(row, step)]
        for corner_id, (a, b, c) in enumerate(corners):
            for component in range(3):
                line = 3 * corner_id + component
                force = matrix_ref[line * 24] * gathered[0]
                for other in range(1, 24):
                    force = force + matrix_ref[line * 24 + other] * gathered[other]
                out_ref[component, pl.ds(row + a, step)] += behind(scale * force, b, c)
        return carry

    lax.fori_loop(0, span_cells // step, element_rows, 0)


def operator_kernel(matrix_ref, values_ref, stiff_ref, out_ref):
    apply_rows(matrix_ref, values_ref, stiff_ref, out_ref)


def whole_sum(value):
    value = jnp.sum(value, axis=(0, 1))
    value = jnp.sum(value, axis=0, keepdims=True)
    return jnp.sum(value, axis=1, keepdims=True)


def solve_kernel(matrix_ref, side_ref, stiff_ref, out_ref, ahead_ref, image_ref, dir_ref, img_ref):
    span_cells = stiff_ref.shape[0]
    residual = side_ref[...]
    ahead_ref[:, 0:span_cells] = residual
    ahead_ref[:, span_cells : span_cells + 1] = jnp.zeros_like(residual[:, 0:1])
    apply_rows(matrix_ref, ahead_ref, stiff_ref, image_ref)
    image_vec = image_ref[:, 0:span_cells]
    norm_now = whole_sum(residual * residual)
    step_size = norm_now / whole_sum(residual * image_vec)
    dir_ref[...] = residual
    img_ref[...] = image_vec
    out_ref[...] = jnp.zeros_like(residual)
    for iteration in range(ITERS):
        out_ref[...] = out_ref[...] + step_size * dir_ref[...]
        residual = residual - step_size * img_ref[...]
        if iteration + 1 < ITERS:
            ahead_ref[:, 0:span_cells] = residual
            apply_rows(matrix_ref, ahead_ref, stiff_ref, image_ref)
            image_vec = image_ref[:, 0:span_cells]
            norm_next = whole_sum(residual * residual)
            curvature = whole_sum(residual * image_vec)
            beta_ratio = norm_next / norm_now
            step_size = norm_next / (curvature - beta_ratio * norm_next / step_size)
            dir_ref[...] = residual + beta_ratio * dir_ref[...]
            img_ref[...] = image_vec + beta_ratio * img_ref[...]
            norm_now = norm_next


def partition_solve_kernel(side, stiffness, matrix):
    span_cells, across_cells, deep_cells = stiffness.shape
    cells = span_cells * across_cells * deep_cells
    wide = (3, span_cells + 1, across_cells, deep_cells)
    return pl.pallas_call(
        solve_kernel,
        out_shape=jax.ShapeDtypeStruct(side.shape, jnp.float32),
        in_specs=[
            pl.BlockSpec(memory_space=pltpu.SMEM),
            pl.BlockSpec(memory_space=pltpu.VMEM),
            pl.BlockSpec(memory_space=pltpu.VMEM),
        ],
        out_specs=pl.BlockSpec(memory_space=pltpu.VMEM),
        scratch_shapes=[
            pltpu.VMEM(wide, jnp.float32),
            pltpu.VMEM(wide, jnp.float32),
            pltpu.VMEM(side.shape, jnp.float32),
            pltpu.VMEM(side.shape, jnp.float32),
        ],
        cost_estimate=pl.CostEstimate(
            flops=ITERS * 2 * 24 * 24 * cells, transcendentals=0, bytes_accessed=28 * cells
        ),
    )(matrix.reshape(-1), side, stiffness)


def partition_operator(values, stiffness, matrix):
    span_cells, across_cells, deep_cells = stiffness.shape
    widened = jnp.pad(values, ((0, 0), (0, 1), (0, 0), (0, 0)))
    cells = span_cells * across_cells * deep_cells
    summed = pl.pallas_call(
        operator_kernel,
        out_shape=jax.ShapeDtypeStruct(widened.shape, jnp.float32),
        in_specs=[
            pl.BlockSpec(memory_space=pltpu.SMEM),
            pl.BlockSpec(memory_space=pltpu.VMEM),
            pl.BlockSpec(memory_space=pltpu.VMEM),
        ],
        out_specs=pl.BlockSpec(memory_space=pltpu.VMEM),
        cost_estimate=pl.CostEstimate(
            flops=2 * 24 * 24 * cells, transcendentals=0, bytes_accessed=28 * cells
        ),
    )(matrix.reshape(-1), widened, stiffness)
    return summed[:, :span_cells]


def whole_partition(block):
    lead = block.shape[:-3]
    count = len(lead)
    every = lax.all_gather(block, "gy", axis=count + 1, tiled=True)
    return lax.all_gather(every, "gx", axis=count, tiled=True)


def own_part(whole, rows, cols):
    start = (0, lax.axis_index("gx") * rows, lax.axis_index("gy") * cols, 0)
    return lax.dynamic_slice(whole, start, (whole.shape[0], rows, cols, whole.shape[3]))


def solve_structure(right_side, operator, products):
    residual = right_side
    image_vec = operator(residual)
    norm_now, curvature = products(residual, image_vec)
    step_size = norm_now / curvature
    direction, image_dir = (residual, image_vec)
    solution = jnp.zeros_like(right_side)
    for iteration in range(ITERS):
        solution = solution + step_size * direction
        residual = residual - step_size * image_dir
        if iteration + 1 < ITERS:
            image_vec = operator(residual)
            norm_next, curvature = products(residual, image_vec)
            beta_ratio = norm_next / norm_now
            step_size = norm_next / (curvature - beta_ratio * norm_next / step_size)
            direction = residual + beta_ratio * direction
            image_dir = image_vec + beta_ratio * image_dir
            norm_now = norm_next
    return solution


def per_device(
    populations,
    solid_mask,
    wall_cells,
    body_load,
    elem_scale,
    elem_active,
    elem_matrix,
    iface_nodes,
    iface_coords,
    neighbours,
):
    group_count = lax.axis_size("group")
    span_devices = lax.axis_size("gx")
    struct_groups = max(1, group_count // 8)
    fluid_groups = group_count - struct_groups
    group_index = lax.axis_index("group")
    slab_index = group_index * span_devices + lax.axis_index("gx")
    column_index = lax.axis_index("gy")
    is_fluid = group_index < fluid_groups
    is_struct = jnp.logical_not(is_fluid)
    span_cells, across_cells, deep_cells = solid_mask.shape
    cell_count = span_cells * across_cells * deep_cells
    fluid_here = jnp.where(is_fluid, 1.0 - solid_mask.astype(jnp.float32), 0.0)
    relaxed_pops = jnp.where(
        is_fluid, collide(populations.astype(jnp.float32)), 0.0
    ).astype(jnp.bfloat16)
    fluid_slabs = fluid_groups * span_devices
    marker = fluid_here.astype(jnp.bfloat16)[None]
    fluid_ext = halo_exchange(marker, fluid_slabs)[0]
    fluid_ext = jnp.pad(fluid_ext, ((0, 0), (0, 0), (1, 1))).astype(jnp.float32)
    wall_index = wall_cells.reshape(-1)
    point_count = wall_index.shape[0]
    tiles_out = point_count // TILE

    def fluid_pack(operands):
        force_parts = local_force(operands[0], operands[1]).reshape(3, cell_count)
        picked = force_parts[:, wall_index]
        span_pos = wall_index // (across_cells * deep_cells)
        across_pos = wall_index // deep_cells % across_cells + column_index * across_cells
        deep_pos = wall_index % deep_cells
        positions = jnp.stack(
            [
                (slab_index * span_cells + span_pos).astype(jnp.float32),
                across_pos.astype(jnp.float32),
                deep_pos.astype(jnp.float32),
            ]
        )
        packed = jnp.concatenate([picked, positions], axis=0)
        return packed.reshape(6, tiles_out, TILE).transpose(1, 0, 2)

    packed = lax.cond(
        is_fluid,
        fluid_pack,
        lambda operands: jnp.zeros((tiles_out, 6, TILE), jnp.float32),
        (relaxed_pops.astype(jnp.float32), fluid_ext),
    )
    received = lax.all_gather(packed, "group", axis=0, tiled=True)
    relaxed_pops, received = lax.optimization_barrier((relaxed_pops, received))
    moved = halo_exchange(relaxed_pops, fluid_slabs)
    moved = jnp.pad(moved, ((0, 0), (0, 0), (0, 0), (1, 1))).astype(jnp.float32)
    node_index = iface_nodes.reshape(-1)
    node_positions = iface_coords.reshape(3, -1)
    tile_lists = neighbours.reshape(neighbours.shape[2], neighbours.shape[3])
    nodes_total = body_load.shape[1] * body_load.shape[2] * body_load.shape[3]
    weight_shape = (tile_lists.shape[0], TILE, tile_lists.shape[1], TILE)

    def struct_map(received_all):
        weights, chosen = basis_weights(received_all, node_positions, tile_lists)
        mapped = map_tractions(weights, chosen, node_index, nodes_total)
        return (weights, body_load + mapped.reshape(body_load.shape))

    def struct_quiet(received_all):
        return (jnp.zeros(weight_shape, jnp.float32), jnp.zeros_like(body_load))

    weights, right_side = lax.cond(is_struct, struct_map, struct_quiet, received)
    stiffness = elem_scale * elem_active.astype(jnp.float32)
    joined = whole_partition(jnp.concatenate([right_side, stiffness[None]], axis=0))
    whole_side = joined[0:3]
    stiffness = joined[3]
    rows, cols = body_load.shape[1], body_load.shape[2]

    def partition_products(first_vec, second_vec):
        pair = (jnp.sum(first_vec * first_vec), jnp.sum(first_vec * second_vec))
        if struct_groups > 1:
            pair = lax.psum(tuple(jnp.where(is_struct, x, 0.0) for x in pair), "group")
        return pair

    def partition_solve(operands):
        side, stiff, matrix = operands
        return solve_structure(
            side, lambda values: partition_operator(values, stiff, matrix), partition_products
        )

    if struct_groups > 1:
        whole_solution = partition_solve((whole_side, stiffness, elem_matrix))
    else:
        whole_solution = lax.cond(
            is_struct,
            lambda operands: partition_solve_kernel(*operands),
            lambda operands: jnp.zeros_like(operands[0]),
            (whole_side, stiffness, elem_matrix),
        )
    solution = jnp.where(is_struct, own_part(whole_solution, rows, cols), 0.0)
    tile_slots = received.shape[0]

    def struct_back(operands):
        return map_speeds(
            operands[0], operands[1].reshape(3, nodes_total), node_index, tile_lists, tile_slots
        )

    back_terms = lax.cond(
        is_struct,
        struct_back,
        lambda operands: jnp.zeros((tile_slots, 3, TILE), jnp.float32),
        (weights, solution),
    )
    back_terms, moved = lax.optimization_barrier((back_terms, moved))
    per_group = tile_slots // group_count
    route_count = fluid_groups // struct_groups
    sender_slot = jnp.clip(group_index - fluid_groups, 0, struct_groups - 1)
    own_speeds = jnp.zeros((per_group, 3, TILE), jnp.float32)
    for route_step in range(route_count):
        offset_row = (sender_slot + route_step * struct_groups) * per_group
        outgoing = lax.dynamic_slice_in_dim(back_terms, offset_row, per_group, 0)
        incoming = passed_along(outgoing, "group", (route_step + 1) * struct_groups)
        own_speeds = own_speeds + jnp.where(
            group_index // struct_groups == route_step, incoming, 0.0
        )
    speed_parts = wall_gain * own_speeds.transpose(1, 0, 2).reshape(3, point_count)
    wall_speed = jnp.zeros((3, cell_count), jnp.float32).at[:, wall_index].add(speed_parts)
    wall_speed = wall_speed.reshape(3, span_cells, across_cells, deep_cells)
    new_populations = lax.cond(
        is_fluid,
        lambda operands: stream_all(operands[0], operands[1], operands[2]),
        lambda operands: jnp.zeros(operands[0][:, 1:-1, 1:-1, 1:-1].shape, jnp.bfloat16),
        (moved, fluid_ext, wall_speed),
    )
    return (new_populations, solution)


def solution(mesh):
    placed = (
        P(None, ("group", "gx"), "gy", None),
        P(("group", "gx"), "gy", None),
        P(("group", "gx"), "gy", None),
        P(None, ("group", "gx"), "gy", None),
        P(("group", "gx"), "gy", None),
        P(("group", "gx"), "gy", None),
        P(),
        P(("group", "gx"), "gy", None),
        P(None, ("group", "gx"), "gy", None),
        P(("group", "gx"), "gy", None, None),
    )
    return jax.shard_map(
        per_device,
        mesh=mesh,
        in_specs=placed,
        out_specs=(P(None, ("group", "gx"), "gy", None), P(None, ("group", "gx"), "gy", None)),
        check_vma=False,
    )
```

```python
import jax
import jax.numpy as jnp
import numpy as np
from jax import lax
from jax.sharding import PartitionSpec as P
from jax.experimental import pallas as pl
from jax.experimental.pallas import tpu as pltpu

TILE = 128
ITERS = 3


velocity = [
    (0, 0, 0),
    (1, 0, 0),
    (-1, 0, 0),
    (0, 1, 0),
    (0, -1, 0),
    (0, 0, 1),
    (0, 0, -1),
    (1, 1, 0),
    (-1, -1, 0),
    (1, -1, 0),
    (-1, 1, 0),
    (1, 0, 1),
    (-1, 0, -1),
    (1, 0, -1),
    (-1, 0, 1),
    (0, 1, 1),
    (0, -1, -1),
    (0, 1, -1),
    (0, -1, 1),
]
opposite = [0, 2, 1, 4, 3, 6, 5, 8, 7, 10, 9, 12, 11, 14, 13, 16, 15, 18, 17]
lattice_weight = [1.0 / 3.0] + [1.0 / 18.0] * 6 + [1.0 / 36.0] * 12
relax_rate = 1.0 / 0.6
wall_gain = 60.0
basis_radius = 24.0
mass_shift = 0.5


def halo_exchange(cells, span_devices):
    columns = lax.axis_size("gy")
    axes = ("group", "gx", "gy")

    def shifted(piece, dr, dc):
        pairs = [
            (r * columns + c, (r + dr) * columns + c + dc)
            for r in range(span_devices)
            for c in range(columns)
            if 0 <= r + dr < span_devices and 0 <= c + dc < columns
        ]
        return lax.ppermute(piece, axes, pairs)

    cols = cells.shape[2]
    cells = jnp.concatenate(
        [shifted(cells[:, :, cols - 1 :], 0, 1), cells, shifted(cells[:, :, :1], 0, -1)], axis=2
    )
    rows = cells.shape[1]
    return jnp.concatenate(
        [shifted(cells[:, rows - 1 :], 1, 0), cells, shifted(cells[:, :1], -1, 0)], axis=1
    )


def passed_along(value, axis, steps):
    count = lax.axis_size(axis)
    pairs = [(source, (source + steps) % count) for source in range(count)]
    return lax.ppermute(value, axis, pairs)


def project_onto(vectors, direction):
    summed = jnp.zeros_like(vectors[0])
    for component in range(3):
        if direction[component] != 0:
            summed = summed + float(direction[component]) * vectors[component]
    return summed


def per_direction(values):
    return jnp.asarray(np.array(values, np.float32).reshape(19, 1, 1, 1))


def collide(population):
    density = jnp.sum(population, axis=0)
    velocity_parts = [
        jnp.sum(per_direction([c[component] for c in velocity]) * population, axis=0) / density
        for component in range(3)
    ]
    speed_square = (
        velocity_parts[0] * velocity_parts[0]
        + velocity_parts[1] * velocity_parts[1]
        + velocity_parts[2] * velocity_parts[2]
    )
    project = project_all(velocity_parts)
    balance = (
        per_direction(lattice_weight)
        * density
        * (1.0 + 3.0 * project + 4.5 * project * project - 1.5 * speed_square)
    )
    return population + relax_rate * (balance - population)


def project_all(vectors):
    summed = per_direction([c[0] for c in velocity]) * vectors[0]
    for component in (1, 2):
        summed = summed + per_direction([c[component] for c in velocity]) * vectors[component]
    return summed


def upstream_of(values, inner):
    for axis in range(3):
        shift = per_direction([c[axis] for c in velocity])
        pick = {
            s: lax.slice_in_dim(values, 1 - s, 1 - s + inner[axis], axis=axis + 1)
            for s in (-1, 0, 1)
        }
        values = jnp.where(shift > 0.5, pick[1], jnp.where(shift < -0.5, pick[-1], pick[0]))
    return values


def stream_links(moved, fluid_ext):
    inner = tuple(size - 2 for size in fluid_ext.shape)
    upstream = upstream_of(moved, inner)
    opened = upstream_of(jnp.broadcast_to(fluid_ext[None], (19,) + fluid_ext.shape), inner)
    bounce = 1.0 - opened
    centre = moved[:, 1 : inner[0] + 1, 1 : inner[1] + 1, 1 : inner[2] + 1]
    paired = centre[1:].reshape((9, 2) + inner)[:, ::-1].reshape((18,) + inner)
    reflected = jnp.concatenate([centre[0:1], paired], axis=0)
    return (upstream, opened, bounce, reflected)


def wall_force(bounce, reflected):
    carried = bounce * reflected
    return jnp.stack(
        [
            jnp.sum(per_direction([-2.0 * c[component] for c in velocity]) * carried, axis=0)
            for component in range(3)
        ]
    )


def stream_all(moved, fluid_ext, wall_speed):
    upstream, opened, bounce, reflected = stream_links(moved, fluid_ext)
    inside = fluid_ext[1:-1, 1:-1, 1:-1]
    speed_list = [wall_speed[0], wall_speed[1], wall_speed[2]]
    correction = per_direction([6.0 * w for w in lattice_weight]) * project_all(speed_list)
    result = inside * (opened * upstream + bounce * (reflected + correction))
    return result.astype(jnp.bfloat16)


def basis_weights(received, node_positions, tile_lists):
    tile_count = tile_lists.shape[0]
    tile_width = received.shape[2]
    chosen = received[tile_lists]
    nodes_at = node_positions.reshape(3, tile_count, tile_width)
    distance = jnp.zeros((tile_count, tile_width, tile_lists.shape[1], tile_width), jnp.float32)
    for component in range(3):
        offset = nodes_at[component][:, :, None, None] - chosen[:, None, :, 3 + component, :]
        distance = distance + offset * offset
    kernel = 1.0 / jnp.sqrt(1.0 + distance / (basis_radius * basis_radius))
    column = jnp.sum(kernel, axis=1)
    totals = (
        jnp.zeros((received.shape[0], tile_width), jnp.float32)
        .at[tile_lists.reshape(-1)]
        .add(column.reshape(-1, tile_width))
    )
    return (kernel / totals[tile_lists][:, None, :, :], chosen)


def map_tractions(weights, chosen, node_index, nodes_total):
    mapped = jnp.einsum(
        "anbp,abcp->can", weights, chosen[:, :, 0:3, :], precision=lax.Precision.HIGHEST
    )
    return jnp.zeros((3, nodes_total), jnp.float32).at[:, node_index].add(mapped.reshape(3, -1))


def map_speeds(weights, solution_flat, node_index, tile_lists, tile_slots):
    tile_count = weights.shape[0]
    tile_width = weights.shape[1]
    at_nodes = solution_flat[:, node_index].reshape(3, tile_count, tile_width)
    contrib = jnp.einsum("anbp,can->abcp", weights, at_nodes, precision=lax.Precision.HIGHEST)
    return (
        jnp.zeros((tile_slots, 3, tile_width), jnp.float32)
        .at[tile_lists.reshape(-1)]
        .add(contrib.reshape(-1, 3, tile_width))
    )


def element_sum(widened, matrix):
    span_cells = widened.shape[1] - 2
    across_cells = widened.shape[2] - 2
    deep_cells = widened.shape[3]
    widened_z = jnp.pad(widened, ((0, 0), (0, 0), (0, 0), (0, 1)))
    corners = [(a, b, c) for a in (0, 1) for b in (0, 1) for c in (0, 1)]
    gathered = jnp.concatenate(
        [
            widened_z[0:3, a : a + span_cells + 1, b : b + across_cells + 1, c : c + deep_cells]
            for a, b, c in corners
        ],
        axis=0,
    )
    element_scale = widened_z[3, 0 : span_cells + 1, 0 : across_cells + 1, 0:deep_cells]
    forces = element_scale * jnp.einsum(
        "ij,jabc->iabc", matrix, gathered, precision=lax.Precision.HIGHEST
    )
    summed = jnp.zeros((3, span_cells + 2, across_cells + 2, deep_cells + 1), jnp.float32)
    for corner_id, (a, b, c) in enumerate(corners):
        summed = summed.at[
            :, a : a + span_cells + 1, b : b + across_cells + 1, c : c + deep_cells
        ].add(forces[3 * corner_id : 3 * corner_id + 3])
    return summed[:, 1 : span_cells + 1, 1 : across_cells + 1, 0:deep_cells]


def apply_rows(matrix_ref, values_ref, stiff_ref, out_ref):
    span_cells, across_cells, deep_cells = stiff_ref.shape
    step = 2 if span_cells % 2 == 0 else 1
    shape = (step, across_cells, deep_cells)
    across_at = lax.broadcasted_iota(jnp.int32, shape, 1)
    deep_at = lax.broadcasted_iota(jnp.int32, shape, 2)
    corners = [(a, b, c) for a in (0, 1) for b in (0, 1) for c in (0, 1)]
    for component in range(3):
        out_ref[component, 0:span_cells] = mass_shift * values_ref[component, 0:span_cells]
        out_ref[component, span_cells] = jnp.zeros((across_cells, deep_cells), jnp.float32)

    def ahead(value, across, deep):
        if across:
            value = jnp.where(
                across_at < across_cells - 1, pltpu.roll(value, across_cells - 1, 1), 0.0
            )
        if deep:
            value = jnp.where(deep_at < deep_cells - 1, pltpu.roll(value, deep_cells - 1, 2), 0.0)
        return value

    def behind(value, across, deep):
        if across:
            value = jnp.where(across_at >= 1, pltpu.roll(value, 1, 1), 0.0)
        if deep:
            value = jnp.where(deep_at >= 1, pltpu.roll(value, 1, 2), 0.0)
        return value

    def element_rows(block, carry):
        row = block * step
        gathered = []
        for a, b, c in corners:
            for component in range(3):
                gathered.append(ahead(values_ref[component, pl.ds(row + a, step)], b, c))
        scale = stiff_ref[pl.ds(row, step)]
        for corner_id, (a, b, c) in enumerate(corners):
            for component in range(3):
                line = 3 * corner_id + component
                force = matrix_ref[line * 24] * gathered[0]
                for other in range(1, 24):
                    force = force + matrix_ref[line * 24 + other] * gathered[other]
                out_ref[component, pl.ds(row + a, step)] += behind(scale * force, b, c)
        return carry

    lax.fori_loop(0, span_cells // step, element_rows, 0)


def operator_kernel(matrix_ref, values_ref, stiff_ref, out_ref):
    apply_rows(matrix_ref, values_ref, stiff_ref, out_ref)


def whole_sum(value):
    value = jnp.sum(value, axis=(0, 1))
    value = jnp.sum(value, axis=0, keepdims=True)
    return jnp.sum(value, axis=1, keepdims=True)


def solve_kernel(matrix_ref, side_ref, stiff_ref, out_ref, ahead_ref, image_ref, dir_ref, img_ref):
    span_cells = stiff_ref.shape[0]
    residual = side_ref[...]
    ahead_ref[:, 0:span_cells] = residual
    ahead_ref[:, span_cells : span_cells + 1] = jnp.zeros_like(residual[:, 0:1])
    apply_rows(matrix_ref, ahead_ref, stiff_ref, image_ref)
    image_vec = image_ref[:, 0:span_cells]
    norm_now = whole_sum(residual * residual)
    step_size = norm_now / whole_sum(residual * image_vec)
    dir_ref[...] = residual
    img_ref[...] = image_vec
    out_ref[...] = jnp.zeros_like(residual)
    for iteration in range(ITERS):
        out_ref[...] = out_ref[...] + step_size * dir_ref[...]
        residual = residual - step_size * img_ref[...]
        if iteration + 1 < ITERS:
            ahead_ref[:, 0:span_cells] = residual
            apply_rows(matrix_ref, ahead_ref, stiff_ref, image_ref)
            image_vec = image_ref[:, 0:span_cells]
            norm_next = whole_sum(residual * residual)
            curvature = whole_sum(residual * image_vec)
            beta_ratio = norm_next / norm_now
            step_size = norm_next / (curvature - beta_ratio * norm_next / step_size)
            dir_ref[...] = residual + beta_ratio * dir_ref[...]
            img_ref[...] = image_vec + beta_ratio * img_ref[...]
            norm_now = norm_next


def partition_solve_kernel(side, stiffness, matrix):
    span_cells, across_cells, deep_cells = stiffness.shape
    cells = span_cells * across_cells * deep_cells
    wide = (3, span_cells + 1, across_cells, deep_cells)
    return pl.pallas_call(
        solve_kernel,
        out_shape=jax.ShapeDtypeStruct(side.shape, jnp.float32),
        in_specs=[
            pl.BlockSpec(memory_space=pltpu.SMEM),
            pl.BlockSpec(memory_space=pltpu.VMEM),
            pl.BlockSpec(memory_space=pltpu.VMEM),
        ],
        out_specs=pl.BlockSpec(memory_space=pltpu.VMEM),
        scratch_shapes=[
            pltpu.VMEM(wide, jnp.float32),
            pltpu.VMEM(wide, jnp.float32),
            pltpu.VMEM(side.shape, jnp.float32),
            pltpu.VMEM(side.shape, jnp.float32),
        ],
        cost_estimate=pl.CostEstimate(
            flops=ITERS * 2 * 24 * 24 * cells, transcendentals=0, bytes_accessed=28 * cells
        ),
    )(matrix.reshape(-1), side, stiffness)


def partition_operator(values, stiffness, matrix):
    span_cells, across_cells, deep_cells = stiffness.shape
    widened = jnp.pad(values, ((0, 0), (0, 1), (0, 0), (0, 0)))
    cells = span_cells * across_cells * deep_cells
    summed = pl.pallas_call(
        operator_kernel,
        out_shape=jax.ShapeDtypeStruct(widened.shape, jnp.float32),
        in_specs=[
            pl.BlockSpec(memory_space=pltpu.SMEM),
            pl.BlockSpec(memory_space=pltpu.VMEM),
            pl.BlockSpec(memory_space=pltpu.VMEM),
        ],
        out_specs=pl.BlockSpec(memory_space=pltpu.VMEM),
        cost_estimate=pl.CostEstimate(
            flops=2 * 24 * 24 * cells, transcendentals=0, bytes_accessed=28 * cells
        ),
    )(matrix.reshape(-1), widened, stiffness)
    return summed[:, :span_cells]


def whole_partition(block):
    lead = block.shape[:-3]
    count = len(lead)
    every = lax.all_gather(block, "gy", axis=count + 1, tiled=True)
    return lax.all_gather(every, "gx", axis=count, tiled=True)


def own_part(whole, rows, cols):
    start = (0, lax.axis_index("gx") * rows, lax.axis_index("gy") * cols, 0)
    return lax.dynamic_slice(whole, start, (whole.shape[0], rows, cols, whole.shape[3]))


def solve_structure(right_side, operator, products):
    residual = right_side
    image_vec = operator(residual)
    norm_now, curvature = products(residual, image_vec)
    step_size = norm_now / curvature
    direction, image_dir = (residual, image_vec)
    solution = jnp.zeros_like(right_side)
    for iteration in range(ITERS):
        solution = solution + step_size * direction
        residual = residual - step_size * image_dir
        if iteration + 1 < ITERS:
            image_vec = operator(residual)
            norm_next, curvature = products(residual, image_vec)
            beta_ratio = norm_next / norm_now
            step_size = norm_next / (curvature - beta_ratio * norm_next / step_size)
            direction = residual + beta_ratio * direction
            image_dir = image_vec + beta_ratio * image_dir
            norm_now = norm_next
    return solution


def per_device(
    populations,
    solid_mask,
    wall_cells,
    body_load,
    elem_scale,
    elem_active,
    elem_matrix,
    iface_nodes,
    iface_coords,
    neighbours,
):
    group_count = lax.axis_size("group")
    span_devices = lax.axis_size("gx")
    struct_groups = max(1, group_count // 8)
    fluid_groups = group_count - struct_groups
    group_index = lax.axis_index("group")
    slab_index = group_index * span_devices + lax.axis_index("gx")
    column_index = lax.axis_index("gy")
    is_fluid = group_index < fluid_groups
    is_struct = jnp.logical_not(is_fluid)
    span_cells, across_cells, deep_cells = solid_mask.shape
    cell_count = span_cells * across_cells * deep_cells
    fluid_here = jnp.where(is_fluid, 1.0 - solid_mask.astype(jnp.float32), 0.0)
    relaxed_pops = jnp.where(
        is_fluid, collide(populations.astype(jnp.float32)), 0.0
    ).astype(jnp.bfloat16)
    marker = fluid_here.astype(jnp.bfloat16)[None]
    widened = halo_exchange(
        jnp.concatenate([relaxed_pops, marker], axis=0), fluid_groups * span_devices
    )
    widened = jnp.pad(widened, ((0, 0), (0, 0), (0, 0), (1, 1))).astype(jnp.float32)
    moved = widened[0:19]
    fluid_ext = widened[19]
    wall_index = wall_cells.reshape(-1)
    point_count = wall_index.shape[0]
    tiles_out = point_count // TILE

    def fluid_pack(operands):
        upstream, opened, bounce, reflected = stream_links(operands[0], operands[1])
        force_parts = wall_force(bounce, reflected).reshape(3, cell_count)
        picked = force_parts[:, wall_index]
        span_pos = wall_index // (across_cells * deep_cells)
        across_pos = wall_index // deep_cells % across_cells + column_index * across_cells
        deep_pos = wall_index % deep_cells
        positions = jnp.stack(
            [
                (slab_index * span_cells + span_pos).astype(jnp.float32),
                across_pos.astype(jnp.float32),
                deep_pos.astype(jnp.float32),
            ]
        )
        packed = jnp.concatenate([picked, positions], axis=0)
        return packed.reshape(6, tiles_out, TILE).transpose(1, 0, 2)

    packed = lax.cond(
        is_fluid,
        fluid_pack,
        lambda operands: jnp.zeros((tiles_out, 6, TILE), jnp.float32),
        (moved, fluid_ext),
    )
    received = lax.all_gather(packed, "group", axis=0, tiled=True)
    node_index = iface_nodes.reshape(-1)
    node_positions = iface_coords.reshape(3, -1)
    tile_lists = neighbours.reshape(neighbours.shape[2], neighbours.shape[3])
    nodes_total = body_load.shape[1] * body_load.shape[2] * body_load.shape[3]
    weight_shape = (tile_lists.shape[0], TILE, tile_lists.shape[1], TILE)

    def struct_map(received_all):
        weights, chosen = basis_weights(received_all, node_positions, tile_lists)
        mapped = map_tractions(weights, chosen, node_index, nodes_total)
        return (weights, body_load + mapped.reshape(body_load.shape))

    def struct_quiet(received_all):
        return (jnp.zeros(weight_shape, jnp.float32), jnp.zeros_like(body_load))

    weights, right_side = lax.cond(is_struct, struct_map, struct_quiet, received)
    stiffness = elem_scale * elem_active.astype(jnp.float32)
    joined = whole_partition(jnp.concatenate([right_side, stiffness[None]], axis=0))
    whole_side = joined[0:3]
    stiffness = joined[3]
    rows, cols = body_load.shape[1], body_load.shape[2]

    def partition_products(first_vec, second_vec):
        pair = (jnp.sum(first_vec * first_vec), jnp.sum(first_vec * second_vec))
        if struct_groups > 1:
            pair = lax.psum(tuple(jnp.where(is_struct, x, 0.0) for x in pair), "group")
        return pair

    def partition_solve(operands):
        side, stiff, matrix = operands
        return solve_structure(
            side, lambda values: partition_operator(values, stiff, matrix), partition_products
        )

    if struct_groups > 1:
        whole_solution = partition_solve((whole_side, stiffness, elem_matrix))
    else:
        whole_solution = lax.cond(
            is_struct,
            lambda operands: partition_solve_kernel(*operands),
            lambda operands: jnp.zeros_like(operands[0]),
            (whole_side, stiffness, elem_matrix),
        )
    solution = jnp.where(is_struct, own_part(whole_solution, rows, cols), 0.0)
    tile_slots = received.shape[0]

    def struct_back(operands):
        return map_speeds(
            operands[0], operands[1].reshape(3, nodes_total), node_index, tile_lists, tile_slots
        )

    back_terms = lax.cond(
        is_struct,
        struct_back,
        lambda operands: jnp.zeros((tile_slots, 3, TILE), jnp.float32),
        (weights, solution),
    )
    per_group = tile_slots // group_count
    route_count = fluid_groups // struct_groups
    sender_slot = jnp.clip(group_index - fluid_groups, 0, struct_groups - 1)
    own_speeds = jnp.zeros((per_group, 3, TILE), jnp.float32)
    for route_step in range(route_count):
        offset_row = (sender_slot + route_step * struct_groups) * per_group
        outgoing = lax.dynamic_slice_in_dim(back_terms, offset_row, per_group, 0)
        incoming = passed_along(outgoing, "group", (route_step + 1) * struct_groups)
        own_speeds = own_speeds + jnp.where(
            group_index // struct_groups == route_step, incoming, 0.0
        )
    speed_parts = wall_gain * own_speeds.transpose(1, 0, 2).reshape(3, point_count)
    wall_speed = jnp.zeros((3, cell_count), jnp.float32).at[:, wall_index].add(speed_parts)
    wall_speed = wall_speed.reshape(3, span_cells, across_cells, deep_cells)
    new_populations = lax.cond(
        is_fluid,
        lambda operands: stream_all(operands[0], operands[1], operands[2]),
        lambda operands: jnp.zeros(operands[0][:, 1:-1, 1:-1, 1:-1].shape, jnp.bfloat16),
        (moved, fluid_ext, wall_speed),
    )
    return (new_populations, solution)


def solution(mesh):
    placed = (
        P(None, ("group", "gx"), "gy", None),
        P(("group", "gx"), "gy", None),
        P(("group", "gx"), "gy", None),
        P(None, ("group", "gx"), "gy", None),
        P(("group", "gx"), "gy", None),
        P(("group", "gx"), "gy", None),
        P(),
        P(("group", "gx"), "gy", None),
        P(None, ("group", "gx"), "gy", None),
        P(("group", "gx"), "gy", None, None),
    )
    return jax.shard_map(
        per_device,
        mesh=mesh,
        in_specs=placed,
        out_specs=(P(None, ("group", "gx"), "gy", None), P(None, ("group", "gx"), "gy", None)),
        check_vma=False,
    )
```

```python
import jax
import jax.numpy as jnp
import numpy as np
from jax import lax
from jax.sharding import PartitionSpec as P
from jax.experimental import pallas as pl
from jax.experimental.pallas import tpu as pltpu

TILE = 128
ITERS = 3


velocity = [
    (0, 0, 0),
    (1, 0, 0),
    (-1, 0, 0),
    (0, 1, 0),
    (0, -1, 0),
    (0, 0, 1),
    (0, 0, -1),
    (1, 1, 0),
    (-1, -1, 0),
    (1, -1, 0),
    (-1, 1, 0),
    (1, 0, 1),
    (-1, 0, -1),
    (1, 0, -1),
    (-1, 0, 1),
    (0, 1, 1),
    (0, -1, -1),
    (0, 1, -1),
    (0, -1, 1),
]
opposite = [0, 2, 1, 4, 3, 6, 5, 8, 7, 10, 9, 12, 11, 14, 13, 16, 15, 18, 17]
lattice_weight = [1.0 / 3.0] + [1.0 / 18.0] * 6 + [1.0 / 36.0] * 12
relax_rate = 1.0 / 0.6
wall_gain = 60.0
basis_radius = 24.0
mass_shift = 0.5


def halo_exchange(cells, span_devices):
    columns = lax.axis_size("gy")
    axes = ("group", "gx", "gy")

    def shifted(piece, dr, dc):
        pairs = [
            (r * columns + c, (r + dr) * columns + c + dc)
            for r in range(span_devices)
            for c in range(columns)
            if 0 <= r + dr < span_devices and 0 <= c + dc < columns
        ]
        return lax.ppermute(piece, axes, pairs)

    cols = cells.shape[2]
    column = lax.axis_index("gy")
    edges = jnp.concatenate([cells[:, :, :1], cells[:, :, cols - 1 :]], axis=2)
    every = lax.all_gather(edges, "gy", axis=0)
    from_left = lax.dynamic_index_in_dim(every, jnp.maximum(column - 1, 0), 0, False)
    from_right = lax.dynamic_index_in_dim(every, jnp.minimum(column + 1, columns - 1), 0, False)
    cells = jnp.concatenate(
        [
            jnp.where(column > 0, from_left[:, :, 1:], 0.0).astype(cells.dtype),
            cells,
            jnp.where(column < columns - 1, from_right[:, :, :1], 0.0).astype(cells.dtype),
        ],
        axis=2,
    )
    rows = cells.shape[1]
    return jnp.concatenate(
        [shifted(cells[:, rows - 1 :], 1, 0), cells, shifted(cells[:, :1], -1, 0)], axis=1
    )


def passed_along(value, axis, steps):
    count = lax.axis_size(axis)
    pairs = [(source, (source + steps) % count) for source in range(count)]
    return lax.ppermute(value, axis, pairs)


def project_onto(vectors, direction):
    summed = jnp.zeros_like(vectors[0])
    for component in range(3):
        if direction[component] != 0:
            summed = summed + float(direction[component]) * vectors[component]
    return summed


def per_direction(values):
    return jnp.asarray(np.array(values, np.float32).reshape(19, 1, 1, 1))


def collide(population):
    density = jnp.sum(population, axis=0)
    velocity_parts = [
        jnp.sum(per_direction([c[component] for c in velocity]) * population, axis=0) / density
        for component in range(3)
    ]
    speed_square = (
        velocity_parts[0] * velocity_parts[0]
        + velocity_parts[1] * velocity_parts[1]
        + velocity_parts[2] * velocity_parts[2]
    )
    project = project_all(velocity_parts)
    balance = (
        per_direction(lattice_weight)
        * density
        * (1.0 + 3.0 * project + 4.5 * project * project - 1.5 * speed_square)
    )
    return population + relax_rate * (balance - population)


def project_all(vectors):
    summed = per_direction([c[0] for c in velocity]) * vectors[0]
    for component in (1, 2):
        summed = summed + per_direction([c[component] for c in velocity]) * vectors[component]
    return summed


def upstream_of(values, inner):
    for axis in range(3):
        shift = per_direction([c[axis] for c in velocity])
        pick = {
            s: lax.slice_in_dim(values, 1 - s, 1 - s + inner[axis], axis=axis + 1)
            for s in (-1, 0, 1)
        }
        values = jnp.where(shift > 0.5, pick[1], jnp.where(shift < -0.5, pick[-1], pick[0]))
    return values


def stream_links(moved, fluid_ext):
    inner = tuple(size - 2 for size in fluid_ext.shape)
    upstream = upstream_of(moved, inner)
    opened = upstream_of(jnp.broadcast_to(fluid_ext[None], (19,) + fluid_ext.shape), inner)
    bounce = 1.0 - opened
    centre = moved[:, 1 : inner[0] + 1, 1 : inner[1] + 1, 1 : inner[2] + 1]
    paired = centre[1:].reshape((9, 2) + inner)[:, ::-1].reshape((18,) + inner)
    reflected = jnp.concatenate([centre[0:1], paired], axis=0)
    return (upstream, opened, bounce, reflected)


def wall_force(bounce, reflected):
    carried = bounce * reflected
    return jnp.stack(
        [
            jnp.sum(per_direction([-2.0 * c[component] for c in velocity]) * carried, axis=0)
            for component in range(3)
        ]
    )


def stream_all(moved, fluid_ext, wall_speed):
    upstream, opened, bounce, reflected = stream_links(moved, fluid_ext)
    inside = fluid_ext[1:-1, 1:-1, 1:-1]
    speed_list = [wall_speed[0], wall_speed[1], wall_speed[2]]
    correction = per_direction([6.0 * w for w in lattice_weight]) * project_all(speed_list)
    result = inside * (opened * upstream + bounce * (reflected + correction))
    return result.astype(jnp.bfloat16)


def basis_weights(received, node_positions, tile_lists):
    tile_count = tile_lists.shape[0]
    tile_width = received.shape[2]
    chosen = received[tile_lists]
    nodes_at = node_positions.reshape(3, tile_count, tile_width)
    distance = jnp.zeros((tile_count, tile_width, tile_lists.shape[1], tile_width), jnp.float32)
    for component in range(3):
        offset = nodes_at[component][:, :, None, None] - chosen[:, None, :, 3 + component, :]
        distance = distance + offset * offset
    kernel = 1.0 / jnp.sqrt(1.0 + distance / (basis_radius * basis_radius))
    column = jnp.sum(kernel, axis=1)
    totals = (
        jnp.zeros((received.shape[0], tile_width), jnp.float32)
        .at[tile_lists.reshape(-1)]
        .add(column.reshape(-1, tile_width))
    )
    return (kernel / totals[tile_lists][:, None, :, :], chosen)


def map_tractions(weights, chosen, node_index, nodes_total):
    mapped = jnp.einsum(
        "anbp,abcp->can", weights, chosen[:, :, 0:3, :], precision=lax.Precision.HIGHEST
    )
    return jnp.zeros((3, nodes_total), jnp.float32).at[:, node_index].add(mapped.reshape(3, -1))


def map_speeds(weights, solution_flat, node_index, tile_lists, tile_slots):
    tile_count = weights.shape[0]
    tile_width = weights.shape[1]
    at_nodes = solution_flat[:, node_index].reshape(3, tile_count, tile_width)
    contrib = jnp.einsum("anbp,can->abcp", weights, at_nodes, precision=lax.Precision.HIGHEST)
    return (
        jnp.zeros((tile_slots, 3, tile_width), jnp.float32)
        .at[tile_lists.reshape(-1)]
        .add(contrib.reshape(-1, 3, tile_width))
    )


def element_sum(widened, matrix):
    span_cells = widened.shape[1] - 2
    across_cells = widened.shape[2] - 2
    deep_cells = widened.shape[3]
    widened_z = jnp.pad(widened, ((0, 0), (0, 0), (0, 0), (0, 1)))
    corners = [(a, b, c) for a in (0, 1) for b in (0, 1) for c in (0, 1)]
    gathered = jnp.concatenate(
        [
            widened_z[0:3, a : a + span_cells + 1, b : b + across_cells + 1, c : c + deep_cells]
            for a, b, c in corners
        ],
        axis=0,
    )
    element_scale = widened_z[3, 0 : span_cells + 1, 0 : across_cells + 1, 0:deep_cells]
    forces = element_scale * jnp.einsum(
        "ij,jabc->iabc", matrix, gathered, precision=lax.Precision.HIGHEST
    )
    summed = jnp.zeros((3, span_cells + 2, across_cells + 2, deep_cells + 1), jnp.float32)
    for corner_id, (a, b, c) in enumerate(corners):
        summed = summed.at[
            :, a : a + span_cells + 1, b : b + across_cells + 1, c : c + deep_cells
        ].add(forces[3 * corner_id : 3 * corner_id + 3])
    return summed[:, 1 : span_cells + 1, 1 : across_cells + 1, 0:deep_cells]


def apply_rows(matrix_ref, values_ref, stiff_ref, out_ref):
    span_cells, across_cells, deep_cells = stiff_ref.shape
    step = 2 if span_cells % 2 == 0 else 1
    shape = (step, across_cells, deep_cells)
    across_at = lax.broadcasted_iota(jnp.int32, shape, 1)
    deep_at = lax.broadcasted_iota(jnp.int32, shape, 2)
    corners = [(a, b, c) for a in (0, 1) for b in (0, 1) for c in (0, 1)]
    for component in range(3):
        out_ref[component, 0:span_cells] = mass_shift * values_ref[component, 0:span_cells]
        out_ref[component, span_cells] = jnp.zeros((across_cells, deep_cells), jnp.float32)

    def ahead(value, across, deep):
        if across:
            value = jnp.where(
                across_at < across_cells - 1, pltpu.roll(value, across_cells - 1, 1), 0.0
            )
        if deep:
            value = jnp.where(deep_at < deep_cells - 1, pltpu.roll(value, deep_cells - 1, 2), 0.0)
        return value

    def behind(value, across, deep):
        if across:
            value = jnp.where(across_at >= 1, pltpu.roll(value, 1, 1), 0.0)
        if deep:
            value = jnp.where(deep_at >= 1, pltpu.roll(value, 1, 2), 0.0)
        return value

    def element_rows(block, carry):
        row = block * step
        gathered = []
        for a, b, c in corners:
            for component in range(3):
                gathered.append(ahead(values_ref[component, pl.ds(row + a, step)], b, c))
        scale = stiff_ref[pl.ds(row, step)]
        for corner_id, (a, b, c) in enumerate(corners):
            for component in range(3):
                line = 3 * corner_id + component
                force = matrix_ref[line * 24] * gathered[0]
                for other in range(1, 24):
                    force = force + matrix_ref[line * 24 + other] * gathered[other]
                out_ref[component, pl.ds(row + a, step)] += behind(scale * force, b, c)
        return carry

    lax.fori_loop(0, span_cells // step, element_rows, 0)


def operator_kernel(matrix_ref, values_ref, stiff_ref, out_ref):
    apply_rows(matrix_ref, values_ref, stiff_ref, out_ref)


def whole_sum(value):
    value = jnp.sum(value, axis=(0, 1))
    value = jnp.sum(value, axis=0, keepdims=True)
    return jnp.sum(value, axis=1, keepdims=True)


def solve_kernel(matrix_ref, side_ref, stiff_ref, out_ref, ahead_ref, image_ref, dir_ref, img_ref):
    span_cells = stiff_ref.shape[0]
    residual = side_ref[...]
    ahead_ref[:, 0:span_cells] = residual
    ahead_ref[:, span_cells : span_cells + 1] = jnp.zeros_like(residual[:, 0:1])
    apply_rows(matrix_ref, ahead_ref, stiff_ref, image_ref)
    image_vec = image_ref[:, 0:span_cells]
    norm_now = whole_sum(residual * residual)
    step_size = norm_now / whole_sum(residual * image_vec)
    dir_ref[...] = residual
    img_ref[...] = image_vec
    out_ref[...] = jnp.zeros_like(residual)
    for iteration in range(ITERS):
        out_ref[...] = out_ref[...] + step_size * dir_ref[...]
        residual = residual - step_size * img_ref[...]
        if iteration + 1 < ITERS:
            ahead_ref[:, 0:span_cells] = residual
            apply_rows(matrix_ref, ahead_ref, stiff_ref, image_ref)
            image_vec = image_ref[:, 0:span_cells]
            norm_next = whole_sum(residual * residual)
            curvature = whole_sum(residual * image_vec)
            beta_ratio = norm_next / norm_now
            step_size = norm_next / (curvature - beta_ratio * norm_next / step_size)
            dir_ref[...] = residual + beta_ratio * dir_ref[...]
            img_ref[...] = image_vec + beta_ratio * img_ref[...]
            norm_now = norm_next


def partition_solve_kernel(side, stiffness, matrix):
    span_cells, across_cells, deep_cells = stiffness.shape
    cells = span_cells * across_cells * deep_cells
    wide = (3, span_cells + 1, across_cells, deep_cells)
    return pl.pallas_call(
        solve_kernel,
        out_shape=jax.ShapeDtypeStruct(side.shape, jnp.float32),
        in_specs=[
            pl.BlockSpec(memory_space=pltpu.SMEM),
            pl.BlockSpec(memory_space=pltpu.VMEM),
            pl.BlockSpec(memory_space=pltpu.VMEM),
        ],
        out_specs=pl.BlockSpec(memory_space=pltpu.VMEM),
        scratch_shapes=[
            pltpu.VMEM(wide, jnp.float32),
            pltpu.VMEM(wide, jnp.float32),
            pltpu.VMEM(side.shape, jnp.float32),
            pltpu.VMEM(side.shape, jnp.float32),
        ],
        cost_estimate=pl.CostEstimate(
            flops=ITERS * 2 * 24 * 24 * cells, transcendentals=0, bytes_accessed=28 * cells
        ),
    )(matrix.reshape(-1), side, stiffness)


def partition_operator(values, stiffness, matrix):
    span_cells, across_cells, deep_cells = stiffness.shape
    widened = jnp.pad(values, ((0, 0), (0, 1), (0, 0), (0, 0)))
    cells = span_cells * across_cells * deep_cells
    summed = pl.pallas_call(
        operator_kernel,
        out_shape=jax.ShapeDtypeStruct(widened.shape, jnp.float32),
        in_specs=[
            pl.BlockSpec(memory_space=pltpu.SMEM),
            pl.BlockSpec(memory_space=pltpu.VMEM),
            pl.BlockSpec(memory_space=pltpu.VMEM),
        ],
        out_specs=pl.BlockSpec(memory_space=pltpu.VMEM),
        cost_estimate=pl.CostEstimate(
            flops=2 * 24 * 24 * cells, transcendentals=0, bytes_accessed=28 * cells
        ),
    )(matrix.reshape(-1), widened, stiffness)
    return summed[:, :span_cells]


def whole_partition(block):
    lead = block.shape[:-3]
    count = len(lead)
    every = lax.all_gather(block, "gy", axis=count + 1, tiled=True)
    return lax.all_gather(every, "gx", axis=count, tiled=True)


def own_part(whole, rows, cols):
    start = (0, lax.axis_index("gx") * rows, lax.axis_index("gy") * cols, 0)
    return lax.dynamic_slice(whole, start, (whole.shape[0], rows, cols, whole.shape[3]))


def solve_structure(right_side, operator, products):
    residual = right_side
    image_vec = operator(residual)
    norm_now, curvature = products(residual, image_vec)
    step_size = norm_now / curvature
    direction, image_dir = (residual, image_vec)
    solution = jnp.zeros_like(right_side)
    for iteration in range(ITERS):
        solution = solution + step_size * direction
        residual = residual - step_size * image_dir
        if iteration + 1 < ITERS:
            image_vec = operator(residual)
            norm_next, curvature = products(residual, image_vec)
            beta_ratio = norm_next / norm_now
            step_size = norm_next / (curvature - beta_ratio * norm_next / step_size)
            direction = residual + beta_ratio * direction
            image_dir = image_vec + beta_ratio * image_dir
            norm_now = norm_next
    return solution


def per_device(
    populations,
    solid_mask,
    wall_cells,
    body_load,
    elem_scale,
    elem_active,
    elem_matrix,
    iface_nodes,
    iface_coords,
    neighbours,
):
    group_count = lax.axis_size("group")
    span_devices = lax.axis_size("gx")
    struct_groups = max(1, group_count // 8)
    fluid_groups = group_count - struct_groups
    group_index = lax.axis_index("group")
    slab_index = group_index * span_devices + lax.axis_index("gx")
    column_index = lax.axis_index("gy")
    is_fluid = group_index < fluid_groups
    is_struct = jnp.logical_not(is_fluid)
    span_cells, across_cells, deep_cells = solid_mask.shape
    cell_count = span_cells * across_cells * deep_cells
    fluid_here = jnp.where(is_fluid, 1.0 - solid_mask.astype(jnp.float32), 0.0)
    relaxed_pops = jnp.where(
        is_fluid, collide(populations.astype(jnp.float32)), 0.0
    ).astype(jnp.bfloat16)
    marker = fluid_here.astype(jnp.bfloat16)[None]
    widened = halo_exchange(
        jnp.concatenate([relaxed_pops, marker], axis=0), fluid_groups * span_devices
    )
    widened = jnp.pad(widened, ((0, 0), (0, 0), (0, 0), (1, 1))).astype(jnp.float32)
    moved = widened[0:19]
    fluid_ext = widened[19]
    wall_index = wall_cells.reshape(-1)
    point_count = wall_index.shape[0]
    tiles_out = point_count // TILE

    def fluid_pack(operands):
        upstream, opened, bounce, reflected = stream_links(operands[0], operands[1])
        force_parts = wall_force(bounce, reflected).reshape(3, cell_count)
        picked = force_parts[:, wall_index]
        span_pos = wall_index // (across_cells * deep_cells)
        across_pos = wall_index // deep_cells % across_cells + column_index * across_cells
        deep_pos = wall_index % deep_cells
        positions = jnp.stack(
            [
                (slab_index * span_cells + span_pos).astype(jnp.float32),
                across_pos.astype(jnp.float32),
                deep_pos.astype(jnp.float32),
            ]
        )
        packed = jnp.concatenate([picked, positions], axis=0)
        return packed.reshape(6, tiles_out, TILE).transpose(1, 0, 2)

    packed = lax.cond(
        is_fluid,
        fluid_pack,
        lambda operands: jnp.zeros((tiles_out, 6, TILE), jnp.float32),
        (moved, fluid_ext),
    )
    received = lax.all_gather(packed, "group", axis=0, tiled=True)
    node_index = iface_nodes.reshape(-1)
    node_positions = iface_coords.reshape(3, -1)
    tile_lists = neighbours.reshape(neighbours.shape[2], neighbours.shape[3])
    nodes_total = body_load.shape[1] * body_load.shape[2] * body_load.shape[3]
    weight_shape = (tile_lists.shape[0], TILE, tile_lists.shape[1], TILE)

    def struct_map(received_all):
        weights, chosen = basis_weights(received_all, node_positions, tile_lists)
        mapped = map_tractions(weights, chosen, node_index, nodes_total)
        return (weights, body_load + mapped.reshape(body_load.shape))

    def struct_quiet(received_all):
        return (jnp.zeros(weight_shape, jnp.float32), jnp.zeros_like(body_load))

    weights, right_side = lax.cond(is_struct, struct_map, struct_quiet, received)
    stiffness = elem_scale * elem_active.astype(jnp.float32)
    joined = whole_partition(jnp.concatenate([right_side, stiffness[None]], axis=0))
    whole_side = joined[0:3]
    stiffness = joined[3]
    rows, cols = body_load.shape[1], body_load.shape[2]

    def partition_products(first_vec, second_vec):
        pair = (jnp.sum(first_vec * first_vec), jnp.sum(first_vec * second_vec))
        if struct_groups > 1:
            pair = lax.psum(tuple(jnp.where(is_struct, x, 0.0) for x in pair), "group")
        return pair

    def partition_solve(operands):
        side, stiff, matrix = operands
        return solve_structure(
            side, lambda values: partition_operator(values, stiff, matrix), partition_products
        )

    if struct_groups > 1:
        whole_solution = partition_solve((whole_side, stiffness, elem_matrix))
    else:
        whole_solution = lax.cond(
            is_struct,
            lambda operands: partition_solve_kernel(*operands),
            lambda operands: jnp.zeros_like(operands[0]),
            (whole_side, stiffness, elem_matrix),
        )
    solution = jnp.where(is_struct, own_part(whole_solution, rows, cols), 0.0)
    tile_slots = received.shape[0]

    def struct_back(operands):
        return map_speeds(
            operands[0], operands[1].reshape(3, nodes_total), node_index, tile_lists, tile_slots
        )

    back_terms = lax.cond(
        is_struct,
        struct_back,
        lambda operands: jnp.zeros((tile_slots, 3, TILE), jnp.float32),
        (weights, solution),
    )
    per_group = tile_slots // group_count
    route_count = fluid_groups // struct_groups
    sender_slot = jnp.clip(group_index - fluid_groups, 0, struct_groups - 1)
    own_speeds = jnp.zeros((per_group, 3, TILE), jnp.float32)
    for route_step in range(route_count):
        offset_row = (sender_slot + route_step * struct_groups) * per_group
        outgoing = lax.dynamic_slice_in_dim(back_terms, offset_row, per_group, 0)
        incoming = passed_along(outgoing, "group", (route_step + 1) * struct_groups)
        own_speeds = own_speeds + jnp.where(
            group_index // struct_groups == route_step, incoming, 0.0
        )
    speed_parts = wall_gain * own_speeds.transpose(1, 0, 2).reshape(3, point_count)
    wall_speed = jnp.zeros((3, cell_count), jnp.float32).at[:, wall_index].add(speed_parts)
    wall_speed = wall_speed.reshape(3, span_cells, across_cells, deep_cells)
    new_populations = lax.cond(
        is_fluid,
        lambda operands: stream_all(operands[0], operands[1], operands[2]),
        lambda operands: jnp.zeros(operands[0][:, 1:-1, 1:-1, 1:-1].shape, jnp.bfloat16),
        (moved, fluid_ext, wall_speed),
    )
    return (new_populations, solution)


def solution(mesh):
    placed = (
        P(None, ("group", "gx"), "gy", None),
        P(("group", "gx"), "gy", None),
        P(("group", "gx"), "gy", None),
        P(None, ("group", "gx"), "gy", None),
        P(("group", "gx"), "gy", None),
        P(("group", "gx"), "gy", None),
        P(),
        P(("group", "gx"), "gy", None),
        P(None, ("group", "gx"), "gy", None),
        P(("group", "gx"), "gy", None, None),
    )
    return jax.shard_map(
        per_device,
        mesh=mesh,
        in_specs=placed,
        out_specs=(P(None, ("group", "gx"), "gy", None), P(None, ("group", "gx"), "gy", None)),
        check_vma=False,
    )
```

```python
import jax
import jax.numpy as jnp
import numpy as np
from jax import lax
from jax.sharding import PartitionSpec as P
from jax.experimental import pallas as pl
from jax.experimental.pallas import tpu as pltpu

TILE = 128
ITERS = 3


velocity = [
    (0, 0, 0),
    (1, 0, 0),
    (-1, 0, 0),
    (0, 1, 0),
    (0, -1, 0),
    (0, 0, 1),
    (0, 0, -1),
    (1, 1, 0),
    (-1, -1, 0),
    (1, -1, 0),
    (-1, 1, 0),
    (1, 0, 1),
    (-1, 0, -1),
    (1, 0, -1),
    (-1, 0, 1),
    (0, 1, 1),
    (0, -1, -1),
    (0, 1, -1),
    (0, -1, 1),
]
opposite = [0, 2, 1, 4, 3, 6, 5, 8, 7, 10, 9, 12, 11, 14, 13, 16, 15, 18, 17]
lattice_weight = [1.0 / 3.0] + [1.0 / 18.0] * 6 + [1.0 / 36.0] * 12
relax_rate = 1.0 / 0.6
wall_gain = 60.0
basis_radius = 24.0
mass_shift = 0.5


def halo_exchange(cells, span_devices):
    columns = lax.axis_size("gy")
    axes = ("group", "gx", "gy")

    def shifted(piece, dr, dc):
        pairs = [
            (r * columns + c, (r + dr) * columns + c + dc)
            for r in range(span_devices)
            for c in range(columns)
            if 0 <= r + dr < span_devices and 0 <= c + dc < columns
        ]
        return lax.ppermute(piece, axes, pairs)

    cols = cells.shape[2]
    column = lax.axis_index("gy")
    edges = jnp.concatenate([cells[:, :, :1], cells[:, :, cols - 1 :]], axis=2)
    every = lax.all_gather(edges, "gy", axis=0)
    from_left = lax.dynamic_index_in_dim(every, jnp.maximum(column - 1, 0), 0, False)
    from_right = lax.dynamic_index_in_dim(every, jnp.minimum(column + 1, columns - 1), 0, False)
    cells = jnp.concatenate(
        [
            jnp.where(column > 0, from_left[:, :, 1:], 0.0).astype(cells.dtype),
            cells,
            jnp.where(column < columns - 1, from_right[:, :, :1], 0.0).astype(cells.dtype),
        ],
        axis=2,
    )
    rows = cells.shape[1]
    return jnp.concatenate(
        [shifted(cells[:, rows - 1 :], 1, 0), cells, shifted(cells[:, :1], -1, 0)], axis=1
    )


def passed_along(value, axis, steps):
    count = lax.axis_size(axis)
    pairs = [(source, (source + steps) % count) for source in range(count)]
    return lax.ppermute(value, axis, pairs)


def project_onto(vectors, direction):
    summed = jnp.zeros_like(vectors[0])
    for component in range(3):
        if direction[component] != 0:
            summed = summed + float(direction[component]) * vectors[component]
    return summed


def per_direction(values):
    return jnp.asarray(np.array(values, np.float32).reshape(19, 1, 1, 1))


def collide(population):
    density = jnp.sum(population, axis=0)
    velocity_parts = [
        jnp.sum(per_direction([c[component] for c in velocity]) * population, axis=0) / density
        for component in range(3)
    ]
    speed_square = (
        velocity_parts[0] * velocity_parts[0]
        + velocity_parts[1] * velocity_parts[1]
        + velocity_parts[2] * velocity_parts[2]
    )
    project = project_all(velocity_parts)
    balance = (
        per_direction(lattice_weight)
        * density
        * (1.0 + 3.0 * project + 4.5 * project * project - 1.5 * speed_square)
    )
    return population + relax_rate * (balance - population)


def project_all(vectors):
    summed = per_direction([c[0] for c in velocity]) * vectors[0]
    for component in (1, 2):
        summed = summed + per_direction([c[component] for c in velocity]) * vectors[component]
    return summed


def upstream_of(values, inner):
    for axis in range(3):
        shift = per_direction([c[axis] for c in velocity])
        pick = {
            s: lax.slice_in_dim(values, 1 - s, 1 - s + inner[axis], axis=axis + 1)
            for s in (-1, 0, 1)
        }
        values = jnp.where(shift > 0.5, pick[1], jnp.where(shift < -0.5, pick[-1], pick[0]))
    return values


def stream_links(moved, fluid_ext):
    inner = tuple(size - 2 for size in fluid_ext.shape)
    upstream = upstream_of(moved, inner)
    opened = upstream_of(jnp.broadcast_to(fluid_ext[None], (19,) + fluid_ext.shape), inner)
    bounce = 1.0 - opened
    centre = moved[:, 1 : inner[0] + 1, 1 : inner[1] + 1, 1 : inner[2] + 1]
    paired = centre[1:].reshape((9, 2) + inner)[:, ::-1].reshape((18,) + inner)
    reflected = jnp.concatenate([centre[0:1], paired], axis=0)
    return (upstream, opened, bounce, reflected)


def wall_force(bounce, reflected):
    carried = bounce * reflected
    return jnp.stack(
        [
            jnp.sum(per_direction([-2.0 * c[component] for c in velocity]) * carried, axis=0)
            for component in range(3)
        ]
    )


def stream_all(moved, fluid_ext, wall_speed):
    upstream, opened, bounce, reflected = stream_links(moved, fluid_ext)
    inside = fluid_ext[1:-1, 1:-1, 1:-1]
    speed_list = [wall_speed[0], wall_speed[1], wall_speed[2]]
    correction = per_direction([6.0 * w for w in lattice_weight]) * project_all(speed_list)
    result = inside * (opened * upstream + bounce * (reflected + correction))
    return result.astype(jnp.bfloat16)


def slot_table(tile_lists, tile_slots):
    slots = lax.broadcasted_iota(jnp.int32, (tile_slots, tile_lists.size), 0)
    return (slots == tile_lists.reshape(1, -1)).astype(jnp.float32)


def basis_weights(received, node_positions, tile_lists):
    tile_count = tile_lists.shape[0]
    tile_width = received.shape[2]
    chosen = received[tile_lists]
    nodes_at = node_positions.reshape(3, tile_count, tile_width)
    distance = jnp.zeros((tile_count, tile_width, tile_lists.shape[1], tile_width), jnp.float32)
    for component in range(3):
        offset = nodes_at[component][:, :, None, None] - chosen[:, None, :, 3 + component, :]
        distance = distance + offset * offset
    kernel = 1.0 / jnp.sqrt(1.0 + distance / (basis_radius * basis_radius))
    column = jnp.sum(kernel, axis=1).reshape(-1, tile_width)
    table = slot_table(tile_lists, received.shape[0])
    exact = lax.Precision.HIGHEST
    totals = jnp.einsum("tk,kp->tp", table, column, precision=exact)
    listed = jnp.einsum("tk,tp->kp", table, totals, precision=exact)
    listed = listed.reshape(tile_count, tile_lists.shape[1], tile_width)
    return (kernel / listed[:, None, :, :], chosen)


def map_tractions(weights, chosen, node_index, base):
    mapped = jnp.einsum(
        "anbp,abcp->can", weights, chosen[:, :, 0:3, :], precision=lax.Precision.HIGHEST
    )
    return base.at[0:3, node_index].add(mapped.reshape(3, -1))


def map_speeds(weights, solution_flat, node_index, tile_lists, tile_slots):
    tile_count = weights.shape[0]
    tile_width = weights.shape[1]
    at_nodes = solution_flat[:, node_index].reshape(3, tile_count, tile_width)
    contrib = jnp.einsum("anbp,can->abcp", weights, at_nodes, precision=lax.Precision.HIGHEST)
    return jnp.einsum(
        "tk,kcp->tcp",
        slot_table(tile_lists, tile_slots),
        contrib.reshape(-1, 3, tile_width),
        precision=lax.Precision.HIGHEST,
    )


def apply_rows(matrix_ref, values_ref, stiff_ref, out_ref):
    span_cells, across_cells, deep_cells = stiff_ref.shape
    step = 2 if span_cells % 2 == 0 else 1
    shape = (step, across_cells, deep_cells)
    across_at = lax.broadcasted_iota(jnp.int32, shape, 1)
    deep_at = lax.broadcasted_iota(jnp.int32, shape, 2)
    corners = [(a, b, c) for a in (0, 1) for b in (0, 1) for c in (0, 1)]
    for component in range(3):
        out_ref[component, 0:span_cells] = mass_shift * values_ref[component, 0:span_cells]
        out_ref[component, span_cells] = jnp.zeros((across_cells, deep_cells), jnp.float32)

    def ahead(value, across, deep):
        if across:
            value = jnp.where(
                across_at < across_cells - 1, pltpu.roll(value, across_cells - 1, 1), 0.0
            )
        if deep:
            value = jnp.where(deep_at < deep_cells - 1, pltpu.roll(value, deep_cells - 1, 2), 0.0)
        return value

    def behind(value, across, deep):
        if across:
            value = jnp.where(across_at >= 1, pltpu.roll(value, 1, 1), 0.0)
        if deep:
            value = jnp.where(deep_at >= 1, pltpu.roll(value, 1, 2), 0.0)
        return value

    def element_rows(block, carry):
        row = block * step
        gathered = []
        for a, b, c in corners:
            for component in range(3):
                gathered.append(ahead(values_ref[component, pl.ds(row + a, step)], b, c))
        scale = stiff_ref[pl.ds(row, step)]
        for corner_id, (a, b, c) in enumerate(corners):
            for component in range(3):
                line = 3 * corner_id + component
                force = matrix_ref[line * 24] * gathered[0]
                for other in range(1, 24):
                    force = force + matrix_ref[line * 24 + other] * gathered[other]
                out_ref[component, pl.ds(row + a, step)] += behind(scale * force, b, c)
        return carry

    lax.fori_loop(0, span_cells // step, element_rows, 0)


def operator_kernel(matrix_ref, values_ref, stiff_ref, out_ref):
    apply_rows(matrix_ref, values_ref, stiff_ref, out_ref)


def whole_sum(value):
    value = jnp.sum(value, axis=(0, 1))
    value = jnp.sum(value, axis=0, keepdims=True)
    return jnp.sum(value, axis=1, keepdims=True)


def solve_kernel(matrix_ref, side_ref, stiff_ref, out_ref, ahead_ref, image_ref, dir_ref, img_ref):
    span_cells = stiff_ref.shape[0]
    residual = side_ref[...]
    ahead_ref[:, 0:span_cells] = residual
    ahead_ref[:, span_cells : span_cells + 1] = jnp.zeros_like(residual[:, 0:1])
    apply_rows(matrix_ref, ahead_ref, stiff_ref, image_ref)
    image_vec = image_ref[:, 0:span_cells]
    norm_now = whole_sum(residual * residual)
    step_size = norm_now / whole_sum(residual * image_vec)
    dir_ref[...] = residual
    img_ref[...] = image_vec
    out_ref[...] = jnp.zeros_like(residual)
    for iteration in range(ITERS):
        out_ref[...] = out_ref[...] + step_size * dir_ref[...]
        residual = residual - step_size * img_ref[...]
        if iteration + 1 < ITERS:
            ahead_ref[:, 0:span_cells] = residual
            apply_rows(matrix_ref, ahead_ref, stiff_ref, image_ref)
            image_vec = image_ref[:, 0:span_cells]
            norm_next = whole_sum(residual * residual)
            curvature = whole_sum(residual * image_vec)
            beta_ratio = norm_next / norm_now
            step_size = norm_next / (curvature - beta_ratio * norm_next / step_size)
            dir_ref[...] = residual + beta_ratio * dir_ref[...]
            img_ref[...] = image_vec + beta_ratio * img_ref[...]
            norm_now = norm_next


def partition_solve_kernel(side, stiffness, matrix):
    span_cells, across_cells, deep_cells = stiffness.shape
    cells = span_cells * across_cells * deep_cells
    wide = (3, span_cells + 1, across_cells, deep_cells)
    return pl.pallas_call(
        solve_kernel,
        out_shape=jax.ShapeDtypeStruct(side.shape, jnp.float32),
        in_specs=[
            pl.BlockSpec(memory_space=pltpu.SMEM),
            pl.BlockSpec(memory_space=pltpu.VMEM),
            pl.BlockSpec(memory_space=pltpu.VMEM),
        ],
        out_specs=pl.BlockSpec(memory_space=pltpu.VMEM),
        scratch_shapes=[
            pltpu.VMEM(wide, jnp.float32),
            pltpu.VMEM(wide, jnp.float32),
            pltpu.VMEM(side.shape, jnp.float32),
            pltpu.VMEM(side.shape, jnp.float32),
        ],
        cost_estimate=pl.CostEstimate(
            flops=ITERS * 2 * 24 * 24 * cells, transcendentals=0, bytes_accessed=28 * cells
        ),
    )(matrix.reshape(-1), side, stiffness)


def partition_operator(values, stiffness, matrix):
    span_cells, across_cells, deep_cells = stiffness.shape
    widened = jnp.pad(values, ((0, 0), (0, 1), (0, 0), (0, 0)))
    cells = span_cells * across_cells * deep_cells
    summed = pl.pallas_call(
        operator_kernel,
        out_shape=jax.ShapeDtypeStruct(widened.shape, jnp.float32),
        in_specs=[
            pl.BlockSpec(memory_space=pltpu.SMEM),
            pl.BlockSpec(memory_space=pltpu.VMEM),
            pl.BlockSpec(memory_space=pltpu.VMEM),
        ],
        out_specs=pl.BlockSpec(memory_space=pltpu.VMEM),
        cost_estimate=pl.CostEstimate(
            flops=2 * 24 * 24 * cells, transcendentals=0, bytes_accessed=28 * cells
        ),
    )(matrix.reshape(-1), widened, stiffness)
    return summed[:, :span_cells]


def whole_partition(block):
    lead = block.shape[:-3]
    count = len(lead)
    every = lax.all_gather(block, "gy", axis=count + 1, tiled=True)
    return lax.all_gather(every, "gx", axis=count, tiled=True)


def own_part(whole, rows, cols):
    start = (0, lax.axis_index("gx") * rows, lax.axis_index("gy") * cols, 0)
    return lax.dynamic_slice(whole, start, (whole.shape[0], rows, cols, whole.shape[3]))


def solve_structure(right_side, operator, products):
    residual = right_side
    image_vec = operator(residual)
    norm_now, curvature = products(residual, image_vec)
    step_size = norm_now / curvature
    direction, image_dir = (residual, image_vec)
    solution = jnp.zeros_like(right_side)
    for iteration in range(ITERS):
        solution = solution + step_size * direction
        residual = residual - step_size * image_dir
        if iteration + 1 < ITERS:
            image_vec = operator(residual)
            norm_next, curvature = products(residual, image_vec)
            beta_ratio = norm_next / norm_now
            step_size = norm_next / (curvature - beta_ratio * norm_next / step_size)
            direction = residual + beta_ratio * direction
            image_dir = image_vec + beta_ratio * image_dir
            norm_now = norm_next
    return solution


def per_device(
    populations,
    solid_mask,
    wall_cells,
    body_load,
    elem_scale,
    elem_active,
    elem_matrix,
    iface_nodes,
    iface_coords,
    neighbours,
):
    group_count = lax.axis_size("group")
    span_devices = lax.axis_size("gx")
    struct_groups = max(1, group_count // 8)
    fluid_groups = group_count - struct_groups
    group_index = lax.axis_index("group")
    slab_index = group_index * span_devices + lax.axis_index("gx")
    column_index = lax.axis_index("gy")
    is_fluid = group_index < fluid_groups
    is_struct = jnp.logical_not(is_fluid)
    span_cells, across_cells, deep_cells = solid_mask.shape
    cell_count = span_cells * across_cells * deep_cells
    fluid_here = jnp.where(is_fluid, 1.0 - solid_mask.astype(jnp.float32), 0.0)
    relaxed_pops = jnp.where(
        is_fluid, collide(populations.astype(jnp.float32)), 0.0
    ).astype(jnp.bfloat16)
    marker = fluid_here.astype(jnp.bfloat16)[None]
    widened = halo_exchange(
        jnp.concatenate([relaxed_pops, marker], axis=0), fluid_groups * span_devices
    )
    widened = jnp.pad(widened, ((0, 0), (0, 0), (0, 0), (1, 1))).astype(jnp.float32)
    moved = widened[0:19]
    fluid_ext = widened[19]
    wall_index = wall_cells.reshape(-1)
    point_count = wall_index.shape[0]
    tiles_out = point_count // TILE

    def fluid_pack(operands):
        upstream, opened, bounce, reflected = stream_links(operands[0], operands[1])
        force_parts = wall_force(bounce, reflected).reshape(3, cell_count)
        picked = force_parts[:, wall_index]
        span_pos = wall_index // (across_cells * deep_cells)
        across_pos = wall_index // deep_cells % across_cells + column_index * across_cells
        deep_pos = wall_index % deep_cells
        positions = jnp.stack(
            [
                (slab_index * span_cells + span_pos).astype(jnp.float32),
                across_pos.astype(jnp.float32),
                deep_pos.astype(jnp.float32),
            ]
        )
        packed = jnp.concatenate([picked, positions], axis=0)
        return packed.reshape(6, tiles_out, TILE).transpose(1, 0, 2)

    packed = lax.cond(
        is_fluid,
        fluid_pack,
        lambda operands: jnp.zeros((tiles_out, 6, TILE), jnp.float32),
        (moved, fluid_ext),
    )
    received = lax.all_gather(packed, "group", axis=0, tiled=True)
    node_index = iface_nodes.reshape(-1)
    node_positions = iface_coords.reshape(3, -1)
    tile_lists = neighbours.reshape(neighbours.shape[2], neighbours.shape[3])
    nodes_total = body_load.shape[1] * body_load.shape[2] * body_load.shape[3]
    weight_shape = (tile_lists.shape[0], TILE, tile_lists.shape[1], TILE)

    stiffness = elem_scale * elem_active.astype(jnp.float32)
    base = jnp.concatenate([body_load, stiffness[None]], axis=0).reshape(4, nodes_total)

    def struct_map(operands):
        received_all, flat = operands
        weights, chosen = basis_weights(received_all, node_positions, tile_lists)
        return (weights, map_tractions(weights, chosen, node_index, flat))

    def struct_quiet(operands):
        return (jnp.zeros(weight_shape, jnp.float32), operands[1])

    weights, joined = lax.cond(is_struct, struct_map, struct_quiet, (received, base))
    joined = whole_partition(joined.reshape((4,) + body_load.shape[1:]))
    whole_side = joined[0:3]
    stiffness = joined[3]
    rows, cols = body_load.shape[1], body_load.shape[2]

    def partition_products(first_vec, second_vec):
        pair = (jnp.sum(first_vec * first_vec), jnp.sum(first_vec * second_vec))
        if struct_groups > 1:
            pair = lax.psum(tuple(jnp.where(is_struct, x, 0.0) for x in pair), "group")
        return pair

    def partition_solve(operands):
        side, stiff, matrix = operands
        return solve_structure(
            side, lambda values: partition_operator(values, stiff, matrix), partition_products
        )

    if struct_groups > 1:
        whole_solution = partition_solve((whole_side, stiffness, elem_matrix))
    else:
        whole_solution = lax.cond(
            is_struct,
            lambda operands: partition_solve_kernel(*operands),
            lambda operands: jnp.zeros_like(operands[0]),
            (whole_side, stiffness, elem_matrix),
        )
    solution = jnp.where(is_struct, own_part(whole_solution, rows, cols), 0.0)
    tile_slots = received.shape[0]

    def struct_back(operands):
        return map_speeds(
            operands[0], operands[1].reshape(3, nodes_total), node_index, tile_lists, tile_slots
        )

    back_terms = lax.cond(
        is_struct,
        struct_back,
        lambda operands: jnp.zeros((tile_slots, 3, TILE), jnp.float32),
        (weights, solution),
    )
    per_group = tile_slots // group_count
    route_count = fluid_groups // struct_groups
    sender_slot = jnp.clip(group_index - fluid_groups, 0, struct_groups - 1)
    own_speeds = jnp.zeros((per_group, 3, TILE), jnp.float32)
    for route_step in range(route_count):
        offset_row = (sender_slot + route_step * struct_groups) * per_group
        outgoing = lax.dynamic_slice_in_dim(back_terms, offset_row, per_group, 0)
        incoming = passed_along(outgoing, "group", (route_step + 1) * struct_groups)
        own_speeds = own_speeds + jnp.where(
            group_index // struct_groups == route_step, incoming, 0.0
        )
    speed_parts = wall_gain * own_speeds.transpose(1, 0, 2).reshape(3, point_count)
    wall_speed = jnp.zeros((3, cell_count), jnp.float32).at[:, wall_index].add(speed_parts)
    wall_speed = wall_speed.reshape(3, span_cells, across_cells, deep_cells)
    new_populations = lax.cond(
        is_fluid,
        lambda operands: stream_all(operands[0], operands[1], operands[2]),
        lambda operands: jnp.zeros(operands[0][:, 1:-1, 1:-1, 1:-1].shape, jnp.bfloat16),
        (moved, fluid_ext, wall_speed),
    )
    return (new_populations, solution)


def solution(mesh):
    placed = (
        P(None, ("group", "gx"), "gy", None),
        P(("group", "gx"), "gy", None),
        P(("group", "gx"), "gy", None),
        P(None, ("group", "gx"), "gy", None),
        P(("group", "gx"), "gy", None),
        P(("group", "gx"), "gy", None),
        P(),
        P(("group", "gx"), "gy", None),
        P(None, ("group", "gx"), "gy", None),
        P(("group", "gx"), "gy", None, None),
    )
    return jax.shard_map(
        per_device,
        mesh=mesh,
        in_specs=placed,
        out_specs=(P(None, ("group", "gx"), "gy", None), P(None, ("group", "gx"), "gy", None)),
        check_vma=False,
    )
```

```python
import jax
import jax.numpy as jnp
import numpy as np
from jax import lax
from jax.sharding import PartitionSpec as P
from jax.experimental import pallas as pl
from jax.experimental.pallas import tpu as pltpu

TILE = 128
ITERS = 3


velocity = [
    (0, 0, 0),
    (1, 0, 0),
    (-1, 0, 0),
    (0, 1, 0),
    (0, -1, 0),
    (0, 0, 1),
    (0, 0, -1),
    (1, 1, 0),
    (-1, -1, 0),
    (1, -1, 0),
    (-1, 1, 0),
    (1, 0, 1),
    (-1, 0, -1),
    (1, 0, -1),
    (-1, 0, 1),
    (0, 1, 1),
    (0, -1, -1),
    (0, 1, -1),
    (0, -1, 1),
]
opposite = [0, 2, 1, 4, 3, 6, 5, 8, 7, 10, 9, 12, 11, 14, 13, 16, 15, 18, 17]
lattice_weight = [1.0 / 3.0] + [1.0 / 18.0] * 6 + [1.0 / 36.0] * 12
relax_rate = 1.0 / 0.6
wall_gain = 60.0
basis_radius = 24.0
mass_shift = 0.5


def halo_exchange(cells, span_devices):
    columns = lax.axis_size("gy")
    axes = ("group", "gx", "gy")

    def shifted(piece, dr, dc):
        pairs = [
            (r * columns + c, (r + dr) * columns + c + dc)
            for r in range(span_devices)
            for c in range(columns)
            if 0 <= r + dr < span_devices and 0 <= c + dc < columns
        ]
        return lax.ppermute(piece, axes, pairs)

    cols = cells.shape[2]
    column = lax.axis_index("gy")
    edges = jnp.concatenate([cells[:, :, :1], cells[:, :, cols - 1 :]], axis=2)
    every = lax.all_gather(edges, "gy", axis=0)
    from_left = lax.dynamic_index_in_dim(every, jnp.maximum(column - 1, 0), 0, False)
    from_right = lax.dynamic_index_in_dim(every, jnp.minimum(column + 1, columns - 1), 0, False)
    cells = jnp.concatenate(
        [
            jnp.where(column > 0, from_left[:, :, 1:], 0.0).astype(cells.dtype),
            cells,
            jnp.where(column < columns - 1, from_right[:, :, :1], 0.0).astype(cells.dtype),
        ],
        axis=2,
    )
    rows = cells.shape[1]
    return jnp.concatenate(
        [shifted(cells[:, rows - 1 :], 1, 0), cells, shifted(cells[:, :1], -1, 0)], axis=1
    )


def passed_along(value, axis, steps):
    count = lax.axis_size(axis)
    pairs = [(source, (source + steps) % count) for source in range(count)]
    return lax.ppermute(value, axis, pairs)


def project_onto(vectors, direction):
    summed = jnp.zeros_like(vectors[0])
    for component in range(3):
        if direction[component] != 0:
            summed = summed + float(direction[component]) * vectors[component]
    return summed


def per_direction(values):
    return jnp.asarray(np.array(values, np.float32).reshape(19, 1, 1, 1))


def collide(population):
    density = jnp.sum(population, axis=0)
    velocity_parts = [
        jnp.sum(per_direction([c[component] for c in velocity]) * population, axis=0) / density
        for component in range(3)
    ]
    speed_square = (
        velocity_parts[0] * velocity_parts[0]
        + velocity_parts[1] * velocity_parts[1]
        + velocity_parts[2] * velocity_parts[2]
    )
    project = project_all(velocity_parts)
    balance = (
        per_direction(lattice_weight)
        * density
        * (1.0 + 3.0 * project + 4.5 * project * project - 1.5 * speed_square)
    )
    return population + relax_rate * (balance - population)


def project_all(vectors):
    summed = per_direction([c[0] for c in velocity]) * vectors[0]
    for component in (1, 2):
        summed = summed + per_direction([c[component] for c in velocity]) * vectors[component]
    return summed


def upstream_of(values, inner):
    for axis in range(3):
        shift = per_direction([c[axis] for c in velocity])
        pick = {
            s: lax.slice_in_dim(values, 1 - s, 1 - s + inner[axis], axis=axis + 1)
            for s in (-1, 0, 1)
        }
        values = jnp.where(shift > 0.5, pick[1], jnp.where(shift < -0.5, pick[-1], pick[0]))
    return values


def stream_links(moved, fluid_ext):
    inner = tuple(size - 2 for size in fluid_ext.shape)
    upstream = upstream_of(moved, inner)
    opened = upstream_of(jnp.broadcast_to(fluid_ext[None], (19,) + fluid_ext.shape), inner)
    bounce = 1.0 - opened
    centre = moved[:, 1 : inner[0] + 1, 1 : inner[1] + 1, 1 : inner[2] + 1]
    paired = centre[1:].reshape((9, 2) + inner)[:, ::-1].reshape((18,) + inner)
    reflected = jnp.concatenate([centre[0:1], paired], axis=0)
    return (upstream, opened, bounce, reflected)


def wall_force(bounce, reflected):
    carried = bounce * reflected
    return jnp.stack(
        [
            jnp.sum(per_direction([-2.0 * c[component] for c in velocity]) * carried, axis=0)
            for component in range(3)
        ]
    )


def stream_all(moved, fluid_ext, wall_speed):
    upstream, opened, bounce, reflected = stream_links(moved, fluid_ext)
    inside = fluid_ext[1:-1, 1:-1, 1:-1]
    speed_list = [wall_speed[0], wall_speed[1], wall_speed[2]]
    correction = per_direction([6.0 * w for w in lattice_weight]) * project_all(speed_list)
    result = inside * (opened * upstream + bounce * (reflected + correction))
    return result.astype(jnp.bfloat16)


def slot_table(tile_lists, tile_slots):
    slots = lax.broadcasted_iota(jnp.int32, (tile_slots, tile_lists.size), 0)
    return (slots == tile_lists.reshape(1, -1)).astype(jnp.float32)


def basis_weights(received, node_positions, tile_lists):
    tile_count = tile_lists.shape[0]
    tile_width = received.shape[2]
    chosen = received[tile_lists]
    nodes_at = node_positions.reshape(3, tile_count, tile_width)
    distance = jnp.zeros((tile_count, tile_width, tile_lists.shape[1], tile_width), jnp.float32)
    for component in range(3):
        offset = nodes_at[component][:, :, None, None] - chosen[:, None, :, 3 + component, :]
        distance = distance + offset * offset
    kernel = 1.0 / jnp.sqrt(1.0 + distance / (basis_radius * basis_radius))
    column = jnp.sum(kernel, axis=1).reshape(-1, tile_width)
    table = slot_table(tile_lists, received.shape[0])
    exact = lax.Precision.HIGHEST
    totals = jnp.einsum("tk,kp->tp", table, column, precision=exact)
    listed = jnp.einsum("tk,tp->kp", table, totals, precision=exact)
    listed = listed.reshape(tile_count, tile_lists.shape[1], tile_width)
    return (kernel / listed[:, None, :, :], chosen)


def map_tractions(weights, chosen, node_index, base):
    mapped = jnp.einsum(
        "anbp,abcp->can", weights, chosen[:, :, 0:3, :], precision=lax.Precision.HIGHEST
    )
    return base.at[:, node_index].add(mapped.reshape(3, -1))


def map_speeds(weights, solution_flat, node_index, tile_lists, tile_slots):
    tile_count = weights.shape[0]
    tile_width = weights.shape[1]
    at_nodes = solution_flat[:, node_index].reshape(3, tile_count, tile_width)
    contrib = jnp.einsum("anbp,can->abcp", weights, at_nodes, precision=lax.Precision.HIGHEST)
    return jnp.einsum(
        "tk,kcp->tcp",
        slot_table(tile_lists, tile_slots),
        contrib.reshape(-1, 3, tile_width),
        precision=lax.Precision.HIGHEST,
    )


def apply_rows(matrix_ref, values_ref, stiff_ref, out_ref):
    span_cells, across_cells, deep_cells = stiff_ref.shape
    step = 2 if span_cells % 2 == 0 else 1
    shape = (step, across_cells, deep_cells)
    across_at = lax.broadcasted_iota(jnp.int32, shape, 1)
    deep_at = lax.broadcasted_iota(jnp.int32, shape, 2)
    corners = [(a, b, c) for a in (0, 1) for b in (0, 1) for c in (0, 1)]
    for component in range(3):
        out_ref[component, 0:span_cells] = mass_shift * values_ref[component, 0:span_cells]
        out_ref[component, span_cells] = jnp.zeros((across_cells, deep_cells), jnp.float32)

    def ahead(value, across, deep):
        if across:
            value = jnp.where(
                across_at < across_cells - 1, pltpu.roll(value, across_cells - 1, 1), 0.0
            )
        if deep:
            value = jnp.where(deep_at < deep_cells - 1, pltpu.roll(value, deep_cells - 1, 2), 0.0)
        return value

    def behind(value, across, deep):
        if across:
            value = jnp.where(across_at >= 1, pltpu.roll(value, 1, 1), 0.0)
        if deep:
            value = jnp.where(deep_at >= 1, pltpu.roll(value, 1, 2), 0.0)
        return value

    def element_rows(block, carry):
        row = block * step
        gathered = []
        for a, b, c in corners:
            for component in range(3):
                gathered.append(ahead(values_ref[component, pl.ds(row + a, step)], b, c))
        scale = stiff_ref[pl.ds(row, step)]
        for corner_id, (a, b, c) in enumerate(corners):
            for component in range(3):
                line = 3 * corner_id + component
                force = matrix_ref[line * 24] * gathered[0]
                for other in range(1, 24):
                    force = force + matrix_ref[line * 24 + other] * gathered[other]
                out_ref[component, pl.ds(row + a, step)] += behind(scale * force, b, c)
        return carry

    lax.fori_loop(0, span_cells // step, element_rows, 0)


def operator_kernel(matrix_ref, values_ref, stiff_ref, out_ref):
    apply_rows(matrix_ref, values_ref, stiff_ref, out_ref)


def whole_sum(value):
    value = jnp.sum(value, axis=(0, 1))
    value = jnp.sum(value, axis=0, keepdims=True)
    return jnp.sum(value, axis=1, keepdims=True)


def solve_kernel(matrix_ref, side_ref, stiff_ref, out_ref, ahead_ref, image_ref, dir_ref, img_ref):
    span_cells = stiff_ref.shape[0]
    residual = side_ref[...]
    ahead_ref[:, 0:span_cells] = residual
    ahead_ref[:, span_cells : span_cells + 1] = jnp.zeros_like(residual[:, 0:1])
    apply_rows(matrix_ref, ahead_ref, stiff_ref, image_ref)
    image_vec = image_ref[:, 0:span_cells]
    norm_now = whole_sum(residual * residual)
    step_size = norm_now / whole_sum(residual * image_vec)
    dir_ref[...] = residual
    img_ref[...] = image_vec
    out_ref[...] = jnp.zeros_like(residual)
    for iteration in range(ITERS):
        out_ref[...] = out_ref[...] + step_size * dir_ref[...]
        residual = residual - step_size * img_ref[...]
        if iteration + 1 < ITERS:
            ahead_ref[:, 0:span_cells] = residual
            apply_rows(matrix_ref, ahead_ref, stiff_ref, image_ref)
            image_vec = image_ref[:, 0:span_cells]
            norm_next = whole_sum(residual * residual)
            curvature = whole_sum(residual * image_vec)
            beta_ratio = norm_next / norm_now
            step_size = norm_next / (curvature - beta_ratio * norm_next / step_size)
            dir_ref[...] = residual + beta_ratio * dir_ref[...]
            img_ref[...] = image_vec + beta_ratio * img_ref[...]
            norm_now = norm_next


def partition_solve_kernel(side, stiffness, matrix):
    span_cells, across_cells, deep_cells = stiffness.shape
    cells = span_cells * across_cells * deep_cells
    wide = (3, span_cells + 1, across_cells, deep_cells)
    return pl.pallas_call(
        solve_kernel,
        out_shape=jax.ShapeDtypeStruct(side.shape, jnp.float32),
        in_specs=[
            pl.BlockSpec(memory_space=pltpu.SMEM),
            pl.BlockSpec(memory_space=pltpu.VMEM),
            pl.BlockSpec(memory_space=pltpu.VMEM),
        ],
        out_specs=pl.BlockSpec(memory_space=pltpu.VMEM),
        scratch_shapes=[
            pltpu.VMEM(wide, jnp.float32),
            pltpu.VMEM(wide, jnp.float32),
            pltpu.VMEM(side.shape, jnp.float32),
            pltpu.VMEM(side.shape, jnp.float32),
        ],
        cost_estimate=pl.CostEstimate(
            flops=ITERS * 2 * 24 * 24 * cells, transcendentals=0, bytes_accessed=28 * cells
        ),
    )(matrix.reshape(-1), side, stiffness)


def partition_operator(values, stiffness, matrix):
    span_cells, across_cells, deep_cells = stiffness.shape
    widened = jnp.pad(values, ((0, 0), (0, 1), (0, 0), (0, 0)))
    cells = span_cells * across_cells * deep_cells
    summed = pl.pallas_call(
        operator_kernel,
        out_shape=jax.ShapeDtypeStruct(widened.shape, jnp.float32),
        in_specs=[
            pl.BlockSpec(memory_space=pltpu.SMEM),
            pl.BlockSpec(memory_space=pltpu.VMEM),
            pl.BlockSpec(memory_space=pltpu.VMEM),
        ],
        out_specs=pl.BlockSpec(memory_space=pltpu.VMEM),
        cost_estimate=pl.CostEstimate(
            flops=2 * 24 * 24 * cells, transcendentals=0, bytes_accessed=28 * cells
        ),
    )(matrix.reshape(-1), widened, stiffness)
    return summed[:, :span_cells]


def whole_partition(block):
    lead = block.shape[:-3]
    count = len(lead)
    every = lax.all_gather(block, "gy", axis=count + 1, tiled=True)
    return lax.all_gather(every, "gx", axis=count, tiled=True)


def own_part(whole, rows, cols):
    start = (0, lax.axis_index("gx") * rows, lax.axis_index("gy") * cols, 0)
    return lax.dynamic_slice(whole, start, (whole.shape[0], rows, cols, whole.shape[3]))


def solve_structure(right_side, operator, products):
    residual = right_side
    image_vec = operator(residual)
    norm_now, curvature = products(residual, image_vec)
    step_size = norm_now / curvature
    direction, image_dir = (residual, image_vec)
    solution = jnp.zeros_like(right_side)
    for iteration in range(ITERS):
        solution = solution + step_size * direction
        residual = residual - step_size * image_dir
        if iteration + 1 < ITERS:
            image_vec = operator(residual)
            norm_next, curvature = products(residual, image_vec)
            beta_ratio = norm_next / norm_now
            step_size = norm_next / (curvature - beta_ratio * norm_next / step_size)
            direction = residual + beta_ratio * direction
            image_dir = image_vec + beta_ratio * image_dir
            norm_now = norm_next
    return solution


def per_device(
    populations,
    solid_mask,
    wall_cells,
    body_load,
    elem_scale,
    elem_active,
    elem_matrix,
    iface_nodes,
    iface_coords,
    neighbours,
):
    group_count = lax.axis_size("group")
    span_devices = lax.axis_size("gx")
    struct_groups = max(1, group_count // 8)
    fluid_groups = group_count - struct_groups
    group_index = lax.axis_index("group")
    slab_index = group_index * span_devices + lax.axis_index("gx")
    column_index = lax.axis_index("gy")
    is_fluid = group_index < fluid_groups
    is_struct = jnp.logical_not(is_fluid)
    span_cells, across_cells, deep_cells = solid_mask.shape
    cell_count = span_cells * across_cells * deep_cells
    fluid_here = jnp.where(is_fluid, 1.0 - solid_mask.astype(jnp.float32), 0.0)
    relaxed_pops = jnp.where(
        is_fluid, collide(populations.astype(jnp.float32)), 0.0
    ).astype(jnp.bfloat16)
    marker = fluid_here.astype(jnp.bfloat16)[None]
    widened = halo_exchange(
        jnp.concatenate([relaxed_pops, marker], axis=0), fluid_groups * span_devices
    )
    widened = jnp.pad(widened, ((0, 0), (0, 0), (0, 0), (1, 1))).astype(jnp.float32)
    moved = widened[0:19]
    fluid_ext = widened[19]
    wall_index = wall_cells.reshape(-1)
    point_count = wall_index.shape[0]
    tiles_out = point_count // TILE

    def fluid_pack(operands):
        upstream, opened, bounce, reflected = stream_links(operands[0], operands[1])
        force_parts = wall_force(bounce, reflected).reshape(3, cell_count)
        picked = force_parts[:, wall_index]
        span_pos = wall_index // (across_cells * deep_cells)
        across_pos = wall_index // deep_cells % across_cells + column_index * across_cells
        deep_pos = wall_index % deep_cells
        positions = jnp.stack(
            [
                (slab_index * span_cells + span_pos).astype(jnp.float32),
                across_pos.astype(jnp.float32),
                deep_pos.astype(jnp.float32),
            ]
        )
        packed = jnp.concatenate([picked, positions], axis=0)
        return packed.reshape(6, tiles_out, TILE).transpose(1, 0, 2)

    packed = lax.cond(
        is_fluid,
        fluid_pack,
        lambda operands: jnp.zeros((tiles_out, 6, TILE), jnp.float32),
        (moved, fluid_ext),
    )
    received = lax.all_gather(packed, "group", axis=0, tiled=True)
    node_index = iface_nodes.reshape(-1)
    node_positions = iface_coords.reshape(3, -1)
    tile_lists = neighbours.reshape(neighbours.shape[2], neighbours.shape[3])
    nodes_total = body_load.shape[1] * body_load.shape[2] * body_load.shape[3]
    weight_shape = (tile_lists.shape[0], TILE, tile_lists.shape[1], TILE)

    stiffness = elem_scale * elem_active.astype(jnp.float32)

    def struct_map(operands):
        received_all, flat = operands
        weights, chosen = basis_weights(received_all, node_positions, tile_lists)
        return (weights, map_tractions(weights, chosen, node_index, flat))

    def struct_quiet(operands):
        return (jnp.zeros(weight_shape, jnp.float32), operands[1])

    weights, right_side = lax.cond(
        is_struct, struct_map, struct_quiet, (received, body_load.reshape(3, nodes_total))
    )
    right_side = right_side.reshape(body_load.shape)
    joined = whole_partition(jnp.concatenate([right_side, stiffness[None]], axis=0))
    whole_side = joined[0:3]
    stiffness = joined[3]
    rows, cols = body_load.shape[1], body_load.shape[2]

    def partition_products(first_vec, second_vec):
        pair = (jnp.sum(first_vec * first_vec), jnp.sum(first_vec * second_vec))
        if struct_groups > 1:
            pair = lax.psum(tuple(jnp.where(is_struct, x, 0.0) for x in pair), "group")
        return pair

    def partition_solve(operands):
        side, stiff, matrix = operands
        return solve_structure(
            side, lambda values: partition_operator(values, stiff, matrix), partition_products
        )

    if struct_groups > 1:
        whole_solution = partition_solve((whole_side, stiffness, elem_matrix))
    else:
        whole_solution = lax.cond(
            is_struct,
            lambda operands: partition_solve_kernel(*operands),
            lambda operands: jnp.zeros_like(operands[0]),
            (whole_side, stiffness, elem_matrix),
        )
    solution = jnp.where(is_struct, own_part(whole_solution, rows, cols), 0.0)
    tile_slots = received.shape[0]

    def struct_back(operands):
        return map_speeds(
            operands[0], operands[1].reshape(3, nodes_total), node_index, tile_lists, tile_slots
        )

    back_terms = lax.cond(
        is_struct,
        struct_back,
        lambda operands: jnp.zeros((tile_slots, 3, TILE), jnp.float32),
        (weights, solution),
    )
    per_group = tile_slots // group_count
    route_count = fluid_groups // struct_groups
    sender_slot = jnp.clip(group_index - fluid_groups, 0, struct_groups - 1)
    own_speeds = jnp.zeros((per_group, 3, TILE), jnp.float32)
    for route_step in range(route_count):
        offset_row = (sender_slot + route_step * struct_groups) * per_group
        outgoing = lax.dynamic_slice_in_dim(back_terms, offset_row, per_group, 0)
        incoming = passed_along(outgoing, "group", (route_step + 1) * struct_groups)
        own_speeds = own_speeds + jnp.where(
            group_index // struct_groups == route_step, incoming, 0.0
        )
    speed_parts = wall_gain * own_speeds.transpose(1, 0, 2).reshape(3, point_count)
    wall_speed = jnp.zeros((3, cell_count), jnp.float32).at[:, wall_index].add(speed_parts)
    wall_speed = wall_speed.reshape(3, span_cells, across_cells, deep_cells)
    new_populations = lax.cond(
        is_fluid,
        lambda operands: stream_all(operands[0], operands[1], operands[2]),
        lambda operands: jnp.zeros(operands[0][:, 1:-1, 1:-1, 1:-1].shape, jnp.bfloat16),
        (moved, fluid_ext, wall_speed),
    )
    return (new_populations, solution)


def solution(mesh):
    placed = (
        P(None, ("group", "gx"), "gy", None),
        P(("group", "gx"), "gy", None),
        P(("group", "gx"), "gy", None),
        P(None, ("group", "gx"), "gy", None),
        P(("group", "gx"), "gy", None),
        P(("group", "gx"), "gy", None),
        P(),
        P(("group", "gx"), "gy", None),
        P(None, ("group", "gx"), "gy", None),
        P(("group", "gx"), "gy", None, None),
    )
    return jax.shard_map(
        per_device,
        mesh=mesh,
        in_specs=placed,
        out_specs=(P(None, ("group", "gx"), "gy", None), P(None, ("group", "gx"), "gy", None)),
        check_vma=False,
    )
```

```python
import jax
import jax.numpy as jnp
import numpy as np
from jax import lax
from jax.sharding import PartitionSpec as P
from jax.experimental import pallas as pl
from jax.experimental.pallas import tpu as pltpu

TILE = 128
ITERS = 3


velocity = [
    (0, 0, 0),
    (1, 0, 0),
    (-1, 0, 0),
    (0, 1, 0),
    (0, -1, 0),
    (0, 0, 1),
    (0, 0, -1),
    (1, 1, 0),
    (-1, -1, 0),
    (1, -1, 0),
    (-1, 1, 0),
    (1, 0, 1),
    (-1, 0, -1),
    (1, 0, -1),
    (-1, 0, 1),
    (0, 1, 1),
    (0, -1, -1),
    (0, 1, -1),
    (0, -1, 1),
]
opposite = [0, 2, 1, 4, 3, 6, 5, 8, 7, 10, 9, 12, 11, 14, 13, 16, 15, 18, 17]
lattice_weight = [1.0 / 3.0] + [1.0 / 18.0] * 6 + [1.0 / 36.0] * 12
relax_rate = 1.0 / 0.6
wall_gain = 60.0
basis_radius = 24.0
mass_shift = 0.5


def halo_exchange(cells, span_devices):
    columns = lax.axis_size("gy")
    axes = ("group", "gx", "gy")

    def shifted(piece, dr, dc):
        pairs = [
            (r * columns + c, (r + dr) * columns + c + dc)
            for r in range(span_devices)
            for c in range(columns)
            if 0 <= r + dr < span_devices and 0 <= c + dc < columns
        ]
        return lax.ppermute(piece, axes, pairs)

    cols = cells.shape[2]
    column = lax.axis_index("gy")
    edges = jnp.concatenate([cells[:, :, :1], cells[:, :, cols - 1 :]], axis=2)
    every = lax.all_gather(edges, "gy", axis=0)
    from_left = lax.dynamic_index_in_dim(every, jnp.maximum(column - 1, 0), 0, False)
    from_right = lax.dynamic_index_in_dim(every, jnp.minimum(column + 1, columns - 1), 0, False)
    cells = jnp.concatenate(
        [
            jnp.where(column > 0, from_left[:, :, 1:], 0.0).astype(cells.dtype),
            cells,
            jnp.where(column < columns - 1, from_right[:, :, :1], 0.0).astype(cells.dtype),
        ],
        axis=2,
    )
    rows = cells.shape[1]
    return jnp.concatenate(
        [shifted(cells[:, rows - 1 :], 1, 0), cells, shifted(cells[:, :1], -1, 0)], axis=1
    )


def passed_along(value, axis, steps):
    count = lax.axis_size(axis)
    pairs = [(source, (source + steps) % count) for source in range(count)]
    return lax.ppermute(value, axis, pairs)


def project_onto(vectors, direction):
    summed = jnp.zeros_like(vectors[0])
    for component in range(3):
        if direction[component] != 0:
            summed = summed + float(direction[component]) * vectors[component]
    return summed


def per_direction(values):
    return jnp.asarray(np.array(values, np.float32).reshape(19, 1, 1, 1))


def collide(population):
    density = jnp.sum(population, axis=0)
    velocity_parts = [
        jnp.sum(per_direction([c[component] for c in velocity]) * population, axis=0) / density
        for component in range(3)
    ]
    speed_square = (
        velocity_parts[0] * velocity_parts[0]
        + velocity_parts[1] * velocity_parts[1]
        + velocity_parts[2] * velocity_parts[2]
    )
    project = project_all(velocity_parts)
    balance = (
        per_direction(lattice_weight)
        * density
        * (1.0 + 3.0 * project + 4.5 * project * project - 1.5 * speed_square)
    )
    return population + relax_rate * (balance - population)


def project_all(vectors):
    summed = per_direction([c[0] for c in velocity]) * vectors[0]
    for component in (1, 2):
        summed = summed + per_direction([c[component] for c in velocity]) * vectors[component]
    return summed


def upstream_of(values, inner):
    for axis in range(3):
        shift = per_direction([c[axis] for c in velocity])
        pick = {
            s: lax.slice_in_dim(values, 1 - s, 1 - s + inner[axis], axis=axis + 1)
            for s in (-1, 0, 1)
        }
        values = jnp.where(shift > 0.5, pick[1], jnp.where(shift < -0.5, pick[-1], pick[0]))
    return values


def stream_links(moved, fluid_ext):
    inner = tuple(size - 2 for size in fluid_ext.shape)
    upstream = upstream_of(moved, inner)
    opened = upstream_of(jnp.broadcast_to(fluid_ext[None], (19,) + fluid_ext.shape), inner)
    bounce = 1.0 - opened
    centre = moved[:, 1 : inner[0] + 1, 1 : inner[1] + 1, 1 : inner[2] + 1]
    paired = centre[1:].reshape((9, 2) + inner)[:, ::-1].reshape((18,) + inner)
    reflected = jnp.concatenate([centre[0:1], paired], axis=0)
    return (upstream, opened, bounce, reflected)


def wall_force(bounce, reflected):
    carried = bounce * reflected
    return jnp.stack(
        [
            jnp.sum(per_direction([-2.0 * c[component] for c in velocity]) * carried, axis=0)
            for component in range(3)
        ]
    )


def stream_all(moved, fluid_ext, wall_speed):
    upstream, opened, bounce, reflected = stream_links(moved, fluid_ext)
    inside = fluid_ext[1:-1, 1:-1, 1:-1]
    speed_list = [wall_speed[0], wall_speed[1], wall_speed[2]]
    correction = per_direction([6.0 * w for w in lattice_weight]) * project_all(speed_list)
    result = inside * (opened * upstream + bounce * (reflected + correction))
    return result.astype(jnp.bfloat16)


def slot_table(tile_lists, tile_slots):
    slots = lax.broadcasted_iota(jnp.int32, (tile_slots, tile_lists.size), 0)
    return (slots == tile_lists.reshape(1, -1)).astype(jnp.float32)


def basis_weights(received, node_positions, tile_lists):
    tile_count = tile_lists.shape[0]
    tile_width = received.shape[2]
    chosen = received[tile_lists]
    nodes_at = node_positions.reshape(3, tile_count, tile_width)
    distance = jnp.zeros((tile_count, tile_width, tile_lists.shape[1], tile_width), jnp.float32)
    for component in range(3):
        offset = nodes_at[component][:, :, None, None] - chosen[:, None, :, 3 + component, :]
        distance = distance + offset * offset
    kernel = 1.0 / jnp.sqrt(1.0 + distance / (basis_radius * basis_radius))
    column = jnp.sum(kernel, axis=1).reshape(-1, tile_width)
    table = slot_table(tile_lists, received.shape[0])
    exact = lax.Precision.HIGHEST
    totals = jnp.einsum("tk,kp->tp", table, column, precision=exact)
    listed = jnp.einsum("tk,tp->kp", table, totals, precision=exact)
    listed = listed.reshape(tile_count, tile_lists.shape[1], tile_width)
    return (kernel / listed[:, None, :, :], chosen)


def map_tractions(weights, chosen, node_index, base):
    mapped = jnp.einsum(
        "anbp,abcp->can", weights, chosen[:, :, 0:3, :], precision=lax.Precision.HIGHEST
    )
    return base.at[:, node_index].add(mapped.reshape(3, -1))


def map_speeds(weights, solution_block, node_index, tile_lists, tile_slots):
    tile_count = weights.shape[0]
    tile_width = weights.shape[1]
    rows, cols, deep = solution_block.shape[1:]
    at_nodes = solution_block[
        :, node_index // (cols * deep), node_index // deep % cols, node_index % deep
    ]
    at_nodes = at_nodes.reshape(3, tile_count, tile_width)
    contrib = jnp.einsum("anbp,can->abcp", weights, at_nodes, precision=lax.Precision.HIGHEST)
    return jnp.einsum(
        "tk,kcp->tcp",
        slot_table(tile_lists, tile_slots),
        contrib.reshape(-1, 3, tile_width),
        precision=lax.Precision.HIGHEST,
    )


def apply_rows(matrix_ref, values_ref, stiff_ref, out_ref):
    span_cells, across_cells, deep_cells = stiff_ref.shape
    step = 2 if span_cells % 2 == 0 else 1
    shape = (step, across_cells, deep_cells)
    across_at = lax.broadcasted_iota(jnp.int32, shape, 1)
    deep_at = lax.broadcasted_iota(jnp.int32, shape, 2)
    corners = [(a, b, c) for a in (0, 1) for b in (0, 1) for c in (0, 1)]
    for component in range(3):
        out_ref[component, 0:span_cells] = mass_shift * values_ref[component, 0:span_cells]
        out_ref[component, span_cells] = jnp.zeros((across_cells, deep_cells), jnp.float32)

    def ahead(value, across, deep):
        if across:
            value = jnp.where(
                across_at < across_cells - 1, pltpu.roll(value, across_cells - 1, 1), 0.0
            )
        if deep:
            value = jnp.where(deep_at < deep_cells - 1, pltpu.roll(value, deep_cells - 1, 2), 0.0)
        return value

    def behind(value, across, deep):
        if across:
            value = jnp.where(across_at >= 1, pltpu.roll(value, 1, 1), 0.0)
        if deep:
            value = jnp.where(deep_at >= 1, pltpu.roll(value, 1, 2), 0.0)
        return value

    def element_rows(block, carry):
        row = block * step
        gathered = []
        for a, b, c in corners:
            for component in range(3):
                gathered.append(ahead(values_ref[component, pl.ds(row + a, step)], b, c))
        scale = stiff_ref[pl.ds(row, step)]
        for corner_id, (a, b, c) in enumerate(corners):
            for component in range(3):
                line = 3 * corner_id + component
                force = matrix_ref[line, 0] * gathered[0]
                for other in range(1, 24):
                    force = force + matrix_ref[line, other] * gathered[other]
                out_ref[component, pl.ds(row + a, step)] += behind(scale * force, b, c)
        return carry

    lax.fori_loop(0, span_cells // step, element_rows, 0)


def operator_kernel(matrix_ref, values_ref, stiff_ref, out_ref):
    apply_rows(matrix_ref, values_ref, stiff_ref, out_ref)


def whole_sum(value):
    value = jnp.sum(value, axis=(0, 1))
    value = jnp.sum(value, axis=0, keepdims=True)
    return jnp.sum(value, axis=1, keepdims=True)


def solve_kernel(matrix_ref, joined_ref, out_ref, ahead_ref, image_ref, dir_ref, img_ref):
    stiff_ref = joined_ref.at[3]
    span_cells = stiff_ref.shape[0]
    residual = joined_ref[0:3]
    ahead_ref[:, 0:span_cells] = residual
    ahead_ref[:, span_cells : span_cells + 1] = jnp.zeros_like(residual[:, 0:1])
    apply_rows(matrix_ref, ahead_ref, stiff_ref, image_ref)
    image_vec = image_ref[:, 0:span_cells]
    norm_now = whole_sum(residual * residual)
    step_size = norm_now / whole_sum(residual * image_vec)
    dir_ref[...] = residual
    img_ref[...] = image_vec
    out_ref[...] = jnp.zeros_like(residual)
    for iteration in range(ITERS):
        out_ref[...] = out_ref[...] + step_size * dir_ref[...]
        residual = residual - step_size * img_ref[...]
        if iteration + 1 < ITERS:
            ahead_ref[:, 0:span_cells] = residual
            apply_rows(matrix_ref, ahead_ref, stiff_ref, image_ref)
            image_vec = image_ref[:, 0:span_cells]
            norm_next = whole_sum(residual * residual)
            curvature = whole_sum(residual * image_vec)
            beta_ratio = norm_next / norm_now
            step_size = norm_next / (curvature - beta_ratio * norm_next / step_size)
            dir_ref[...] = residual + beta_ratio * dir_ref[...]
            img_ref[...] = image_vec + beta_ratio * img_ref[...]
            norm_now = norm_next


def partition_solve_kernel(joined, matrix):
    span_cells, across_cells, deep_cells = joined.shape[1:]
    cells = span_cells * across_cells * deep_cells
    wide = (3, span_cells + 1, across_cells, deep_cells)
    side = (3, span_cells, across_cells, deep_cells)
    return pl.pallas_call(
        solve_kernel,
        out_shape=jax.ShapeDtypeStruct(side, jnp.float32),
        in_specs=[
            pl.BlockSpec(memory_space=pltpu.SMEM),
            pl.BlockSpec(memory_space=pltpu.VMEM),
        ],
        out_specs=pl.BlockSpec(memory_space=pltpu.VMEM),
        scratch_shapes=[
            pltpu.VMEM(wide, jnp.float32),
            pltpu.VMEM(wide, jnp.float32),
            pltpu.VMEM(side, jnp.float32),
            pltpu.VMEM(side, jnp.float32),
        ],
        cost_estimate=pl.CostEstimate(
            flops=ITERS * 2 * 24 * 24 * cells, transcendentals=0, bytes_accessed=28 * cells
        ),
    )(matrix, joined)


def partition_operator(values, stiffness, matrix):
    span_cells, across_cells, deep_cells = stiffness.shape
    widened = jnp.pad(values, ((0, 0), (0, 1), (0, 0), (0, 0)))
    cells = span_cells * across_cells * deep_cells
    summed = pl.pallas_call(
        operator_kernel,
        out_shape=jax.ShapeDtypeStruct(widened.shape, jnp.float32),
        in_specs=[
            pl.BlockSpec(memory_space=pltpu.SMEM),
            pl.BlockSpec(memory_space=pltpu.VMEM),
            pl.BlockSpec(memory_space=pltpu.VMEM),
        ],
        out_specs=pl.BlockSpec(memory_space=pltpu.VMEM),
        cost_estimate=pl.CostEstimate(
            flops=2 * 24 * 24 * cells, transcendentals=0, bytes_accessed=28 * cells
        ),
    )(matrix, widened, stiffness)
    return summed[:, :span_cells]


def whole_partition(block):
    lead = block.shape[:-3]
    count = len(lead)
    every = lax.all_gather(block, "gy", axis=count + 1, tiled=True)
    return lax.all_gather(every, "gx", axis=count, tiled=True)


def own_part(whole, rows, cols):
    start = (0, lax.axis_index("gx") * rows, lax.axis_index("gy") * cols, 0)
    return lax.dynamic_slice(whole, start, (whole.shape[0], rows, cols, whole.shape[3]))


def solve_structure(right_side, operator, products):
    residual = right_side
    image_vec = operator(residual)
    norm_now, curvature = products(residual, image_vec)
    step_size = norm_now / curvature
    direction, image_dir = (residual, image_vec)
    solution = jnp.zeros_like(right_side)
    for iteration in range(ITERS):
        solution = solution + step_size * direction
        residual = residual - step_size * image_dir
        if iteration + 1 < ITERS:
            image_vec = operator(residual)
            norm_next, curvature = products(residual, image_vec)
            beta_ratio = norm_next / norm_now
            step_size = norm_next / (curvature - beta_ratio * norm_next / step_size)
            direction = residual + beta_ratio * direction
            image_dir = image_vec + beta_ratio * image_dir
            norm_now = norm_next
    return solution


def per_device(
    populations,
    solid_mask,
    wall_cells,
    body_load,
    elem_scale,
    elem_active,
    elem_matrix,
    iface_nodes,
    iface_coords,
    neighbours,
):
    group_count = lax.axis_size("group")
    span_devices = lax.axis_size("gx")
    struct_groups = max(1, group_count // 8)
    fluid_groups = group_count - struct_groups
    group_index = lax.axis_index("group")
    slab_index = group_index * span_devices + lax.axis_index("gx")
    column_index = lax.axis_index("gy")
    is_fluid = group_index < fluid_groups
    is_struct = jnp.logical_not(is_fluid)
    span_cells, across_cells, deep_cells = solid_mask.shape
    cell_count = span_cells * across_cells * deep_cells
    fluid_here = jnp.where(is_fluid, 1.0 - solid_mask.astype(jnp.float32), 0.0)
    relaxed_pops = jnp.where(
        is_fluid, collide(populations.astype(jnp.float32)), 0.0
    ).astype(jnp.bfloat16)
    marker = fluid_here.astype(jnp.bfloat16)[None]
    widened = halo_exchange(
        jnp.concatenate([relaxed_pops, marker], axis=0), fluid_groups * span_devices
    )
    widened = jnp.pad(widened, ((0, 0), (0, 0), (0, 0), (1, 1))).astype(jnp.float32)
    moved = widened[0:19]
    fluid_ext = widened[19]
    wall_index = wall_cells.reshape(-1)
    point_count = wall_index.shape[0]
    tiles_out = point_count // TILE

    def fluid_pack(operands):
        upstream, opened, bounce, reflected = stream_links(operands[0], operands[1])
        force_parts = wall_force(bounce, reflected).reshape(3, cell_count)
        picked = force_parts[:, wall_index]
        span_pos = wall_index // (across_cells * deep_cells)
        across_pos = wall_index // deep_cells % across_cells + column_index * across_cells
        deep_pos = wall_index % deep_cells
        positions = jnp.stack(
            [
                (slab_index * span_cells + span_pos).astype(jnp.float32),
                across_pos.astype(jnp.float32),
                deep_pos.astype(jnp.float32),
            ]
        )
        packed = jnp.concatenate([picked, positions], axis=0)
        return packed.reshape(6, tiles_out, TILE).transpose(1, 0, 2)

    packed = lax.cond(
        is_fluid,
        fluid_pack,
        lambda operands: jnp.zeros((tiles_out, 6, TILE), jnp.float32),
        (moved, fluid_ext),
    )
    received = lax.all_gather(packed, "group", axis=0, tiled=True)
    node_index = iface_nodes.reshape(-1)
    node_positions = iface_coords.reshape(3, -1)
    tile_lists = neighbours.reshape(neighbours.shape[2], neighbours.shape[3])
    nodes_total = body_load.shape[1] * body_load.shape[2] * body_load.shape[3]
    weight_shape = (tile_lists.shape[0], TILE, tile_lists.shape[1], TILE)

    stiffness = elem_scale * elem_active.astype(jnp.float32)

    def struct_map(operands):
        received_all, flat = operands
        weights, chosen = basis_weights(received_all, node_positions, tile_lists)
        return (weights, map_tractions(weights, chosen, node_index, flat))

    def struct_quiet(operands):
        return (jnp.zeros(weight_shape, jnp.float32), operands[1])

    weights, right_side = lax.cond(
        is_struct, struct_map, struct_quiet, (received, body_load.reshape(3, nodes_total))
    )
    right_side = right_side.reshape(body_load.shape)
    joined = whole_partition(jnp.concatenate([right_side, stiffness[None]], axis=0))
    whole_side = joined[0:3]
    stiffness = joined[3]
    rows, cols = body_load.shape[1], body_load.shape[2]

    def partition_products(first_vec, second_vec):
        pair = (jnp.sum(first_vec * first_vec), jnp.sum(first_vec * second_vec))
        if struct_groups > 1:
            pair = lax.psum(tuple(jnp.where(is_struct, x, 0.0) for x in pair), "group")
        return pair

    def partition_solve(operands):
        side, stiff, matrix = operands
        return solve_structure(
            side, lambda values: partition_operator(values, stiff, matrix), partition_products
        )

    if struct_groups > 1:
        whole_solution = partition_solve((whole_side, stiffness, elem_matrix))
    else:
        whole_solution = lax.cond(
            is_struct,
            lambda operands: partition_solve_kernel(*operands),
            lambda operands: jnp.zeros_like(operands[0][0:3]),
            (joined, elem_matrix),
        )
    solution = jnp.where(is_struct, own_part(whole_solution, rows, cols), 0.0)
    tile_slots = received.shape[0]

    def struct_back(operands):
        return map_speeds(
            operands[0], operands[1], node_index, tile_lists, tile_slots
        )

    back_terms = lax.cond(
        is_struct,
        struct_back,
        lambda operands: jnp.zeros((tile_slots, 3, TILE), jnp.float32),
        (weights, solution),
    )
    per_group = tile_slots // group_count
    route_count = fluid_groups // struct_groups
    sender_slot = jnp.clip(group_index - fluid_groups, 0, struct_groups - 1)
    own_speeds = jnp.zeros((per_group, 3, TILE), jnp.float32)
    for route_step in range(route_count):
        offset_row = (sender_slot + route_step * struct_groups) * per_group
        outgoing = lax.dynamic_slice_in_dim(back_terms, offset_row, per_group, 0)
        incoming = passed_along(outgoing, "group", (route_step + 1) * struct_groups)
        own_speeds = own_speeds + jnp.where(
            group_index // struct_groups == route_step, incoming, 0.0
        )
    speed_parts = wall_gain * own_speeds.transpose(1, 0, 2).reshape(3, point_count)
    wall_speed = jnp.zeros((3, cell_count), jnp.float32).at[:, wall_index].add(speed_parts)
    wall_speed = wall_speed.reshape(3, span_cells, across_cells, deep_cells)
    new_populations = lax.cond(
        is_fluid,
        lambda operands: stream_all(operands[0], operands[1], operands[2]),
        lambda operands: jnp.zeros(operands[0][:, 1:-1, 1:-1, 1:-1].shape, jnp.bfloat16),
        (moved, fluid_ext, wall_speed),
    )
    return (new_populations, solution)


def solution(mesh):
    placed = (
        P(None, ("group", "gx"), "gy", None),
        P(("group", "gx"), "gy", None),
        P(("group", "gx"), "gy", None),
        P(None, ("group", "gx"), "gy", None),
        P(("group", "gx"), "gy", None),
        P(("group", "gx"), "gy", None),
        P(),
        P(("group", "gx"), "gy", None),
        P(None, ("group", "gx"), "gy", None),
        P(("group", "gx"), "gy", None, None),
    )
    return jax.shard_map(
        per_device,
        mesh=mesh,
        in_specs=placed,
        out_specs=(P(None, ("group", "gx"), "gy", None), P(None, ("group", "gx"), "gy", None)),
        check_vma=False,
    )
```

```python
import jax
import jax.numpy as jnp
import numpy as np
from jax import lax
from jax.sharding import PartitionSpec as P
from jax.experimental import pallas as pl
from jax.experimental.pallas import tpu as pltpu

TILE = 128
ITERS = 3


velocity = [
    (0, 0, 0),
    (1, 0, 0),
    (-1, 0, 0),
    (0, 1, 0),
    (0, -1, 0),
    (0, 0, 1),
    (0, 0, -1),
    (1, 1, 0),
    (-1, -1, 0),
    (1, -1, 0),
    (-1, 1, 0),
    (1, 0, 1),
    (-1, 0, -1),
    (1, 0, -1),
    (-1, 0, 1),
    (0, 1, 1),
    (0, -1, -1),
    (0, 1, -1),
    (0, -1, 1),
]
opposite = [0, 2, 1, 4, 3, 6, 5, 8, 7, 10, 9, 12, 11, 14, 13, 16, 15, 18, 17]
lattice_weight = [1.0 / 3.0] + [1.0 / 18.0] * 6 + [1.0 / 36.0] * 12
relax_rate = 1.0 / 0.6
wall_gain = 60.0
basis_radius = 24.0
mass_shift = 0.5


def halo_exchange(cells, span_devices):
    columns = lax.axis_size("gy")
    axes = ("group", "gx", "gy")

    def shifted(piece, dr, dc):
        pairs = [
            (r * columns + c, (r + dr) * columns + c + dc)
            for r in range(span_devices)
            for c in range(columns)
            if 0 <= r + dr < span_devices and 0 <= c + dc < columns
        ]
        return lax.ppermute(piece, axes, pairs)

    cols = cells.shape[2]
    column = lax.axis_index("gy")
    edges = jnp.concatenate([cells[:, :, :1], cells[:, :, cols - 1 :]], axis=2)
    every = lax.all_gather(edges, "gy", axis=0)
    from_left = lax.dynamic_index_in_dim(every, jnp.maximum(column - 1, 0), 0, False)
    from_right = lax.dynamic_index_in_dim(every, jnp.minimum(column + 1, columns - 1), 0, False)
    cells = jnp.concatenate(
        [
            jnp.where(column > 0, from_left[:, :, 1:], 0.0).astype(cells.dtype),
            cells,
            jnp.where(column < columns - 1, from_right[:, :, :1], 0.0).astype(cells.dtype),
        ],
        axis=2,
    )
    rows = cells.shape[1]
    return jnp.concatenate(
        [shifted(cells[:, rows - 1 :], 1, 0), cells, shifted(cells[:, :1], -1, 0)], axis=1
    )


def passed_along(value, axis, steps):
    count = lax.axis_size(axis)
    pairs = [(source, (source + steps) % count) for source in range(count)]
    return lax.ppermute(value, axis, pairs)


def project_onto(vectors, direction):
    summed = jnp.zeros_like(vectors[0])
    for component in range(3):
        if direction[component] != 0:
            summed = summed + float(direction[component]) * vectors[component]
    return summed


def per_direction(values):
    return jnp.asarray(np.array(values, np.float32).reshape(19, 1, 1, 1))


def collide(population):
    density = jnp.sum(population, axis=0)
    velocity_parts = [
        jnp.sum(per_direction([c[component] for c in velocity]) * population, axis=0) / density
        for component in range(3)
    ]
    speed_square = (
        velocity_parts[0] * velocity_parts[0]
        + velocity_parts[1] * velocity_parts[1]
        + velocity_parts[2] * velocity_parts[2]
    )
    project = project_all(velocity_parts)
    balance = (
        per_direction(lattice_weight)
        * density
        * (1.0 + 3.0 * project + 4.5 * project * project - 1.5 * speed_square)
    )
    return population + relax_rate * (balance - population)


def project_all(vectors):
    summed = per_direction([c[0] for c in velocity]) * vectors[0]
    for component in (1, 2):
        summed = summed + per_direction([c[component] for c in velocity]) * vectors[component]
    return summed


def upstream_of(values, inner):
    for axis in range(3):
        shift = per_direction([c[axis] for c in velocity])
        pick = {
            s: lax.slice_in_dim(values, 1 - s, 1 - s + inner[axis], axis=axis + 1)
            for s in (-1, 0, 1)
        }
        values = jnp.where(shift > 0.5, pick[1], jnp.where(shift < -0.5, pick[-1], pick[0]))
    return values


def stream_links(moved, fluid_ext):
    inner = tuple(size - 2 for size in fluid_ext.shape)
    upstream = upstream_of(moved, inner)
    opened = upstream_of(jnp.broadcast_to(fluid_ext[None], (19,) + fluid_ext.shape), inner)
    bounce = 1.0 - opened
    centre = moved[:, 1 : inner[0] + 1, 1 : inner[1] + 1, 1 : inner[2] + 1]
    paired = centre[1:].reshape((9, 2) + inner)[:, ::-1].reshape((18,) + inner)
    reflected = jnp.concatenate([centre[0:1], paired], axis=0)
    return (upstream, opened, bounce, reflected)


def wall_force(bounce, reflected):
    carried = bounce * reflected
    return jnp.stack(
        [
            jnp.sum(per_direction([-2.0 * c[component] for c in velocity]) * carried, axis=0)
            for component in range(3)
        ]
    )


def stream_all(moved, fluid_ext, wall_speed):
    upstream, opened, bounce, reflected = stream_links(moved, fluid_ext)
    inside = fluid_ext[1:-1, 1:-1, 1:-1]
    speed_list = [wall_speed[0], wall_speed[1], wall_speed[2]]
    correction = per_direction([6.0 * w for w in lattice_weight]) * project_all(speed_list)
    result = inside * (opened * upstream + bounce * (reflected + correction))
    return result.astype(jnp.bfloat16)


def slot_table(tile_lists, tile_slots):
    slots = lax.broadcasted_iota(jnp.int32, (tile_slots, tile_lists.size), 0)
    return (slots == tile_lists.reshape(1, -1)).astype(jnp.float32)


def basis_weights(received, node_positions, tile_lists):
    tile_count = tile_lists.shape[0]
    tile_width = received.shape[2]
    chosen = received[tile_lists]
    nodes_at = node_positions.reshape(3, tile_count, tile_width)
    distance = jnp.zeros((tile_count, tile_width, tile_lists.shape[1], tile_width), jnp.float32)
    for component in range(3):
        offset = nodes_at[component][:, :, None, None] - chosen[:, None, :, 3 + component, :]
        distance = distance + offset * offset
    kernel = 1.0 / jnp.sqrt(1.0 + distance / (basis_radius * basis_radius))
    column = jnp.sum(kernel, axis=1).reshape(-1, tile_width)
    table = slot_table(tile_lists, received.shape[0])
    exact = lax.Precision.HIGHEST
    totals = jnp.einsum("tk,kp->tp", table, column, precision=exact)
    listed = jnp.einsum("tk,tp->kp", table, totals, precision=exact)
    listed = listed.reshape(tile_count, tile_lists.shape[1], tile_width)
    return (kernel / listed[:, None, :, :], chosen)


def map_tractions(weights, chosen, node_index, base):
    mapped = jnp.einsum(
        "anbp,abcp->can", weights, chosen[:, :, 0:3, :], precision=lax.Precision.HIGHEST
    )
    return base.at[:, node_index].add(mapped.reshape(3, -1))


def map_speeds(weights, solution_block, node_index, tile_lists, tile_slots):
    tile_count = weights.shape[0]
    tile_width = weights.shape[1]
    flat = solution_block.reshape(3, -1)
    at_nodes = flat[:, node_index].reshape(3, tile_count, tile_width)
    contrib = jnp.einsum("anbp,can->abcp", weights, at_nodes, precision=lax.Precision.HIGHEST)
    return jnp.einsum(
        "tk,kcp->tcp",
        slot_table(tile_lists, tile_slots),
        contrib.reshape(-1, 3, tile_width),
        precision=lax.Precision.HIGHEST,
    )


def apply_rows(matrix_ref, values_ref, stiff_ref, out_ref):
    span_cells, across_cells, deep_cells = stiff_ref.shape
    step = 4 if span_cells % 4 == 0 else 1
    shape = (step, across_cells, deep_cells)
    across_at = lax.broadcasted_iota(jnp.int32, shape, 1)
    deep_at = lax.broadcasted_iota(jnp.int32, shape, 2)
    corners = [(a, b, c) for a in (0, 1) for b in (0, 1) for c in (0, 1)]
    for component in range(3):
        out_ref[component, 0:span_cells] = mass_shift * values_ref[component, 0:span_cells]
        out_ref[component, span_cells] = jnp.zeros((across_cells, deep_cells), jnp.float32)

    def ahead(value, across, deep):
        if across:
            value = jnp.where(
                across_at < across_cells - 1, pltpu.roll(value, across_cells - 1, 1), 0.0
            )
        if deep:
            value = jnp.where(deep_at < deep_cells - 1, pltpu.roll(value, deep_cells - 1, 2), 0.0)
        return value

    def behind(value, across, deep):
        if across:
            value = jnp.where(across_at >= 1, pltpu.roll(value, 1, 1), 0.0)
        if deep:
            value = jnp.where(deep_at >= 1, pltpu.roll(value, 1, 2), 0.0)
        return value

    def element_rows(block, carry):
        row = block * step
        gathered = []
        for a, b, c in corners:
            for component in range(3):
                gathered.append(ahead(values_ref[component, pl.ds(row + a, step)], b, c))
        scale = stiff_ref[pl.ds(row, step)]
        for corner_id, (a, b, c) in enumerate(corners):
            for component in range(3):
                line = 3 * corner_id + component
                force = matrix_ref[line, 0] * gathered[0]
                for other in range(1, 24):
                    force = force + matrix_ref[line, other] * gathered[other]
                out_ref[component, pl.ds(row + a, step)] += behind(scale * force, b, c)
        return carry

    lax.fori_loop(0, span_cells // step, element_rows, 0)


def operator_kernel(matrix_ref, values_ref, stiff_ref, out_ref):
    apply_rows(matrix_ref, values_ref, stiff_ref, out_ref)


def whole_sum(value):
    value = jnp.sum(value, axis=(0, 1))
    value = jnp.sum(value, axis=0, keepdims=True)
    return jnp.sum(value, axis=1, keepdims=True)


def solve_kernel(matrix_ref, joined_ref, out_ref, ahead_ref, image_ref, dir_ref, img_ref):
    stiff_ref = joined_ref.at[3]
    span_cells = stiff_ref.shape[0]
    residual = joined_ref[0:3]
    ahead_ref[:, 0:span_cells] = residual
    ahead_ref[:, span_cells : span_cells + 1] = jnp.zeros_like(residual[:, 0:1])
    apply_rows(matrix_ref, ahead_ref, stiff_ref, image_ref)
    image_vec = image_ref[:, 0:span_cells]
    norm_now = whole_sum(residual * residual)
    step_size = norm_now / whole_sum(residual * image_vec)
    dir_ref[...] = residual
    img_ref[...] = image_vec
    out_ref[...] = jnp.zeros_like(residual)
    for iteration in range(ITERS):
        out_ref[...] = out_ref[...] + step_size * dir_ref[...]
        residual = residual - step_size * img_ref[...]
        if iteration + 1 < ITERS:
            ahead_ref[:, 0:span_cells] = residual
            apply_rows(matrix_ref, ahead_ref, stiff_ref, image_ref)
            image_vec = image_ref[:, 0:span_cells]
            norm_next = whole_sum(residual * residual)
            curvature = whole_sum(residual * image_vec)
            beta_ratio = norm_next / norm_now
            step_size = norm_next / (curvature - beta_ratio * norm_next / step_size)
            dir_ref[...] = residual + beta_ratio * dir_ref[...]
            img_ref[...] = image_vec + beta_ratio * img_ref[...]
            norm_now = norm_next


def partition_solve_kernel(joined, matrix):
    span_cells, across_cells, deep_cells = joined.shape[1:]
    cells = span_cells * across_cells * deep_cells
    wide = (3, span_cells + 1, across_cells, deep_cells)
    side = (3, span_cells, across_cells, deep_cells)
    return pl.pallas_call(
        solve_kernel,
        out_shape=jax.ShapeDtypeStruct(side, jnp.float32),
        in_specs=[
            pl.BlockSpec(memory_space=pltpu.SMEM),
            pl.BlockSpec(memory_space=pltpu.VMEM),
        ],
        out_specs=pl.BlockSpec(memory_space=pltpu.VMEM),
        scratch_shapes=[
            pltpu.VMEM(wide, jnp.float32),
            pltpu.VMEM(wide, jnp.float32),
            pltpu.VMEM(side, jnp.float32),
            pltpu.VMEM(side, jnp.float32),
        ],
        cost_estimate=pl.CostEstimate(
            flops=ITERS * 2 * 24 * 24 * cells, transcendentals=0, bytes_accessed=28 * cells
        ),
    )(matrix, joined)


def partition_operator(values, stiffness, matrix):
    span_cells, across_cells, deep_cells = stiffness.shape
    widened = jnp.pad(values, ((0, 0), (0, 1), (0, 0), (0, 0)))
    cells = span_cells * across_cells * deep_cells
    summed = pl.pallas_call(
        operator_kernel,
        out_shape=jax.ShapeDtypeStruct(widened.shape, jnp.float32),
        in_specs=[
            pl.BlockSpec(memory_space=pltpu.SMEM),
            pl.BlockSpec(memory_space=pltpu.VMEM),
            pl.BlockSpec(memory_space=pltpu.VMEM),
        ],
        out_specs=pl.BlockSpec(memory_space=pltpu.VMEM),
        cost_estimate=pl.CostEstimate(
            flops=2 * 24 * 24 * cells, transcendentals=0, bytes_accessed=28 * cells
        ),
    )(matrix, widened, stiffness)
    return summed[:, :span_cells]


def whole_partition(block):
    lead = block.shape[:-3]
    count = len(lead)
    every = lax.all_gather(block, "gy", axis=count + 1, tiled=True)
    return lax.all_gather(every, "gx", axis=count, tiled=True)


def own_part(whole, rows, cols):
    start = (0, lax.axis_index("gx") * rows, lax.axis_index("gy") * cols, 0)
    return lax.dynamic_slice(whole, start, (whole.shape[0], rows, cols, whole.shape[3]))


def solve_structure(right_side, operator, products):
    residual = right_side
    image_vec = operator(residual)
    norm_now, curvature = products(residual, image_vec)
    step_size = norm_now / curvature
    direction, image_dir = (residual, image_vec)
    solution = jnp.zeros_like(right_side)
    for iteration in range(ITERS):
        solution = solution + step_size * direction
        residual = residual - step_size * image_dir
        if iteration + 1 < ITERS:
            image_vec = operator(residual)
            norm_next, curvature = products(residual, image_vec)
            beta_ratio = norm_next / norm_now
            step_size = norm_next / (curvature - beta_ratio * norm_next / step_size)
            direction = residual + beta_ratio * direction
            image_dir = image_vec + beta_ratio * image_dir
            norm_now = norm_next
    return solution


def per_device(
    populations,
    solid_mask,
    wall_cells,
    body_load,
    elem_scale,
    elem_active,
    elem_matrix,
    iface_nodes,
    iface_coords,
    neighbours,
):
    group_count = lax.axis_size("group")
    span_devices = lax.axis_size("gx")
    struct_groups = max(1, group_count // 8)
    fluid_groups = group_count - struct_groups
    group_index = lax.axis_index("group")
    slab_index = group_index * span_devices + lax.axis_index("gx")
    column_index = lax.axis_index("gy")
    is_fluid = group_index < fluid_groups
    is_struct = jnp.logical_not(is_fluid)
    span_cells, across_cells, deep_cells = solid_mask.shape
    cell_count = span_cells * across_cells * deep_cells
    fluid_here = jnp.where(is_fluid, 1.0 - solid_mask.astype(jnp.float32), 0.0)
    relaxed_pops = jnp.where(
        is_fluid, collide(populations.astype(jnp.float32)), 0.0
    ).astype(jnp.bfloat16)
    marker = fluid_here.astype(jnp.bfloat16)[None]
    widened = halo_exchange(
        jnp.concatenate([relaxed_pops, marker], axis=0), fluid_groups * span_devices
    )
    widened = jnp.pad(widened, ((0, 0), (0, 0), (0, 0), (1, 1))).astype(jnp.float32)
    moved = widened[0:19]
    fluid_ext = widened[19]
    wall_index = wall_cells.reshape(-1)
    point_count = wall_index.shape[0]
    tiles_out = point_count // TILE

    def fluid_pack(operands):
        upstream, opened, bounce, reflected = stream_links(operands[0], operands[1])
        force_parts = wall_force(bounce, reflected).reshape(3, cell_count)
        picked = force_parts[:, wall_index]
        span_pos = wall_index // (across_cells * deep_cells)
        across_pos = wall_index // deep_cells % across_cells + column_index * across_cells
        deep_pos = wall_index % deep_cells
        positions = jnp.stack(
            [
                (slab_index * span_cells + span_pos).astype(jnp.float32),
                across_pos.astype(jnp.float32),
                deep_pos.astype(jnp.float32),
            ]
        )
        packed = jnp.concatenate([picked, positions], axis=0)
        return packed.reshape(6, tiles_out, TILE).transpose(1, 0, 2)

    packed = lax.cond(
        is_fluid,
        fluid_pack,
        lambda operands: jnp.zeros((tiles_out, 6, TILE), jnp.float32),
        (moved, fluid_ext),
    )
    received = lax.all_gather(packed, "group", axis=0, tiled=True)
    node_index = iface_nodes.reshape(-1)
    node_positions = iface_coords.reshape(3, -1)
    tile_lists = neighbours.reshape(neighbours.shape[2], neighbours.shape[3])
    nodes_total = body_load.shape[1] * body_load.shape[2] * body_load.shape[3]
    weight_shape = (tile_lists.shape[0], TILE, tile_lists.shape[1], TILE)

    stiffness = elem_scale * elem_active.astype(jnp.float32)

    def struct_map(operands):
        received_all, flat = operands
        weights, chosen = basis_weights(received_all, node_positions, tile_lists)
        return (weights, map_tractions(weights, chosen, node_index, flat))

    def struct_quiet(operands):
        return (jnp.zeros(weight_shape, jnp.float32), operands[1])

    weights, right_side = lax.cond(
        is_struct, struct_map, struct_quiet, (received, body_load.reshape(3, nodes_total))
    )
    right_side = right_side.reshape(body_load.shape)
    joined = whole_partition(jnp.concatenate([right_side, stiffness[None]], axis=0))
    whole_side = joined[0:3]
    stiffness = joined[3]
    rows, cols = body_load.shape[1], body_load.shape[2]

    def partition_products(first_vec, second_vec):
        pair = (jnp.sum(first_vec * first_vec), jnp.sum(first_vec * second_vec))
        if struct_groups > 1:
            pair = lax.psum(tuple(jnp.where(is_struct, x, 0.0) for x in pair), "group")
        return pair

    def partition_solve(operands):
        side, stiff, matrix = operands
        return solve_structure(
            side, lambda values: partition_operator(values, stiff, matrix), partition_products
        )

    if struct_groups > 1:
        whole_solution = partition_solve((whole_side, stiffness, elem_matrix))
    else:
        whole_solution = lax.cond(
            is_struct,
            lambda operands: partition_solve_kernel(*operands),
            lambda operands: jnp.zeros_like(operands[0][0:3]),
            (joined, elem_matrix),
        )
    solution = jnp.where(is_struct, own_part(whole_solution, rows, cols), 0.0)
    tile_slots = received.shape[0]

    def struct_back(operands):
        return map_speeds(
            operands[0], operands[1], node_index, tile_lists, tile_slots
        )

    back_terms = lax.cond(
        is_struct,
        struct_back,
        lambda operands: jnp.zeros((tile_slots, 3, TILE), jnp.float32),
        (weights, solution),
    )
    per_group = tile_slots // group_count
    route_count = fluid_groups // struct_groups
    sender_slot = jnp.clip(group_index - fluid_groups, 0, struct_groups - 1)
    own_speeds = jnp.zeros((per_group, 3, TILE), jnp.float32)
    for route_step in range(route_count):
        offset_row = (sender_slot + route_step * struct_groups) * per_group
        outgoing = lax.dynamic_slice_in_dim(back_terms, offset_row, per_group, 0)
        incoming = passed_along(outgoing, "group", (route_step + 1) * struct_groups)
        own_speeds = own_speeds + jnp.where(
            group_index // struct_groups == route_step, incoming, 0.0
        )
    speed_parts = wall_gain * own_speeds.transpose(1, 0, 2).reshape(3, point_count)
    wall_speed = jnp.zeros((3, cell_count), jnp.float32).at[:, wall_index].add(speed_parts)
    wall_speed = wall_speed.reshape(3, span_cells, across_cells, deep_cells)
    new_populations = lax.cond(
        is_fluid,
        lambda operands: stream_all(operands[0], operands[1], operands[2]),
        lambda operands: jnp.zeros(operands[0][:, 1:-1, 1:-1, 1:-1].shape, jnp.bfloat16),
        (moved, fluid_ext, wall_speed),
    )
    return (new_populations, solution)


def solution(mesh):
    placed = (
        P(None, ("group", "gx"), "gy", None),
        P(("group", "gx"), "gy", None),
        P(("group", "gx"), "gy", None),
        P(None, ("group", "gx"), "gy", None),
        P(("group", "gx"), "gy", None),
        P(("group", "gx"), "gy", None),
        P(),
        P(("group", "gx"), "gy", None),
        P(None, ("group", "gx"), "gy", None),
        P(("group", "gx"), "gy", None, None),
    )
    return jax.shard_map(
        per_device,
        mesh=mesh,
        in_specs=placed,
        out_specs=(P(None, ("group", "gx"), "gy", None), P(None, ("group", "gx"), "gy", None)),
        check_vma=False,
    )
```

```python
import jax
import jax.numpy as jnp
import numpy as np
from jax import lax
from jax.sharding import PartitionSpec as P
from jax.experimental import pallas as pl
from jax.experimental.pallas import tpu as pltpu

TILE = 128
ITERS = 3


velocity = [
    (0, 0, 0),
    (1, 0, 0),
    (-1, 0, 0),
    (0, 1, 0),
    (0, -1, 0),
    (0, 0, 1),
    (0, 0, -1),
    (1, 1, 0),
    (-1, -1, 0),
    (1, -1, 0),
    (-1, 1, 0),
    (1, 0, 1),
    (-1, 0, -1),
    (1, 0, -1),
    (-1, 0, 1),
    (0, 1, 1),
    (0, -1, -1),
    (0, 1, -1),
    (0, -1, 1),
]
opposite = [0, 2, 1, 4, 3, 6, 5, 8, 7, 10, 9, 12, 11, 14, 13, 16, 15, 18, 17]
lattice_weight = [1.0 / 3.0] + [1.0 / 18.0] * 6 + [1.0 / 36.0] * 12
relax_rate = 1.0 / 0.6
wall_gain = 60.0
basis_radius = 24.0
mass_shift = 0.5


def halo_exchange(cells, span_devices):
    columns = lax.axis_size("gy")
    axes = ("group", "gx", "gy")

    def shifted(piece, dr, dc):
        pairs = [
            (r * columns + c, (r + dr) * columns + c + dc)
            for r in range(span_devices)
            for c in range(columns)
            if 0 <= r + dr < span_devices and 0 <= c + dc < columns
        ]
        return lax.ppermute(piece, axes, pairs)

    cols = cells.shape[2]
    column = lax.axis_index("gy")
    edges = jnp.concatenate([cells[:, :, :1], cells[:, :, cols - 1 :]], axis=2)
    every = lax.all_gather(edges, "gy", axis=0)
    from_left = lax.dynamic_index_in_dim(every, jnp.maximum(column - 1, 0), 0, False)
    from_right = lax.dynamic_index_in_dim(every, jnp.minimum(column + 1, columns - 1), 0, False)
    cells = jnp.concatenate(
        [
            jnp.where(column > 0, from_left[:, :, 1:], 0.0).astype(cells.dtype),
            cells,
            jnp.where(column < columns - 1, from_right[:, :, :1], 0.0).astype(cells.dtype),
        ],
        axis=2,
    )
    rows = cells.shape[1]
    return jnp.concatenate(
        [shifted(cells[:, rows - 1 :], 1, 0), cells, shifted(cells[:, :1], -1, 0)], axis=1
    )


def passed_along(value, axis, steps):
    count = lax.axis_size(axis)
    pairs = [(source, (source + steps) % count) for source in range(count)]
    return lax.ppermute(value, axis, pairs)


def project_onto(vectors, direction):
    summed = jnp.zeros_like(vectors[0])
    for component in range(3):
        if direction[component] != 0:
            summed = summed + float(direction[component]) * vectors[component]
    return summed


def per_direction(values):
    return jnp.asarray(np.array(values, np.float32).reshape(19, 1, 1, 1))


def collide(population):
    density = jnp.sum(population, axis=0)
    velocity_parts = [
        jnp.sum(per_direction([c[component] for c in velocity]) * population, axis=0) / density
        for component in range(3)
    ]
    speed_square = (
        velocity_parts[0] * velocity_parts[0]
        + velocity_parts[1] * velocity_parts[1]
        + velocity_parts[2] * velocity_parts[2]
    )
    project = project_all(velocity_parts)
    balance = (
        per_direction(lattice_weight)
        * density
        * (1.0 + 3.0 * project + 4.5 * project * project - 1.5 * speed_square)
    )
    return population + relax_rate * (balance - population)


def project_all(vectors):
    summed = per_direction([c[0] for c in velocity]) * vectors[0]
    for component in (1, 2):
        summed = summed + per_direction([c[component] for c in velocity]) * vectors[component]
    return summed


def upstream_of(values, inner):
    for axis in range(3):
        shift = per_direction([c[axis] for c in velocity])
        pick = {
            s: lax.slice_in_dim(values, 1 - s, 1 - s + inner[axis], axis=axis + 1)
            for s in (-1, 0, 1)
        }
        values = jnp.where(shift > 0.5, pick[1], jnp.where(shift < -0.5, pick[-1], pick[0]))
    return values


def stream_links(moved, fluid_ext):
    inner = tuple(size - 2 for size in fluid_ext.shape)
    upstream = upstream_of(moved, inner)
    opened = upstream_of(jnp.broadcast_to(fluid_ext[None], (19,) + fluid_ext.shape), inner)
    bounce = 1.0 - opened
    centre = moved[:, 1 : inner[0] + 1, 1 : inner[1] + 1, 1 : inner[2] + 1]
    paired = centre[1:].reshape((9, 2) + inner)[:, ::-1].reshape((18,) + inner)
    reflected = jnp.concatenate([centre[0:1], paired], axis=0)
    return (upstream, opened, bounce, reflected)


def wall_force(bounce, reflected):
    carried = bounce * reflected
    return jnp.stack(
        [
            jnp.sum(per_direction([-2.0 * c[component] for c in velocity]) * carried, axis=0)
            for component in range(3)
        ]
    )


def stream_all(moved, fluid_ext, wall_speed):
    upstream, opened, bounce, reflected = stream_links(moved, fluid_ext)
    inside = fluid_ext[1:-1, 1:-1, 1:-1]
    speed_list = [wall_speed[0], wall_speed[1], wall_speed[2]]
    correction = per_direction([6.0 * w for w in lattice_weight]) * project_all(speed_list)
    result = inside * (opened * upstream + bounce * (reflected + correction))
    return result.astype(jnp.bfloat16)


def slot_table(tile_lists, tile_slots):
    slots = lax.broadcasted_iota(jnp.int32, (tile_slots, tile_lists.size), 0)
    return (slots == tile_lists.reshape(1, -1)).astype(jnp.float32)


def basis_weights(received, node_positions, tile_lists):
    tile_count = tile_lists.shape[0]
    tile_width = received.shape[2]
    chosen = received[tile_lists]
    nodes_at = node_positions.reshape(3, tile_count, tile_width)
    distance = jnp.zeros((tile_count, tile_width, tile_lists.shape[1], tile_width), jnp.float32)
    for component in range(3):
        offset = nodes_at[component][:, :, None, None] - chosen[:, None, :, 3 + component, :]
        distance = distance + offset * offset
    kernel = 1.0 / jnp.sqrt(1.0 + distance / (basis_radius * basis_radius))
    column = jnp.sum(kernel, axis=1).reshape(-1, tile_width)
    table = slot_table(tile_lists, received.shape[0])
    exact = lax.Precision.HIGHEST
    totals = jnp.einsum("tk,kp->tp", table, column, precision=exact)
    listed = jnp.einsum("tk,tp->kp", table, totals, precision=exact)
    listed = listed.reshape(tile_count, tile_lists.shape[1], tile_width)
    return (kernel / listed[:, None, :, :], chosen)


def map_tractions(weights, chosen, node_index, base):
    mapped = jnp.einsum(
        "anbp,abcp->can", weights, chosen[:, :, 0:3, :], precision=lax.Precision.HIGHEST
    )
    return base.at[:, node_index].add(mapped.reshape(3, -1))


def map_speeds(weights, solution_block, node_index, tile_lists, tile_slots):
    tile_count = weights.shape[0]
    tile_width = weights.shape[1]
    flat = solution_block.reshape(3, -1)
    at_nodes = flat[:, node_index].reshape(3, tile_count, tile_width)
    contrib = jnp.einsum("anbp,can->abcp", weights, at_nodes, precision=lax.Precision.HIGHEST)
    return jnp.einsum(
        "tk,kcp->tcp",
        slot_table(tile_lists, tile_slots),
        contrib.reshape(-1, 3, tile_width),
        precision=lax.Precision.HIGHEST,
    )


def apply_rows(matrix_ref, values_ref, stiff_ref, out_ref):
    span_cells, across_cells, deep_cells = stiff_ref.shape
    step = next(size for size in (8, 4, 2, 1) if span_cells % size == 0)
    shape = (step, across_cells, deep_cells)
    across_at = lax.broadcasted_iota(jnp.int32, shape, 1)
    deep_at = lax.broadcasted_iota(jnp.int32, shape, 2)
    corners = [(a, b, c) for a in (0, 1) for b in (0, 1) for c in (0, 1)]
    for component in range(3):
        out_ref[component, 0:span_cells] = mass_shift * values_ref[component, 0:span_cells]
        out_ref[component, span_cells] = jnp.zeros((across_cells, deep_cells), jnp.float32)

    def ahead(value, across, deep):
        if across:
            value = jnp.where(
                across_at < across_cells - 1, pltpu.roll(value, across_cells - 1, 1), 0.0
            )
        if deep:
            value = jnp.where(deep_at < deep_cells - 1, pltpu.roll(value, deep_cells - 1, 2), 0.0)
        return value

    def behind(value, across, deep):
        if across:
            value = jnp.where(across_at >= 1, pltpu.roll(value, 1, 1), 0.0)
        if deep:
            value = jnp.where(deep_at >= 1, pltpu.roll(value, 1, 2), 0.0)
        return value

    def element_rows(block, carry):
        row = block * step
        gathered = []
        for a, b, c in corners:
            for component in range(3):
                gathered.append(ahead(values_ref[component, pl.ds(row + a, step)], b, c))
        scale = stiff_ref[pl.ds(row, step)]
        for corner_id, (a, b, c) in enumerate(corners):
            for component in range(3):
                line = 3 * corner_id + component
                force = matrix_ref[line, 0] * gathered[0]
                for other in range(1, 24):
                    force = force + matrix_ref[line, other] * gathered[other]
                out_ref[component, pl.ds(row + a, step)] += behind(scale * force, b, c)
        return carry

    lax.fori_loop(0, span_cells // step, element_rows, 0)


def operator_kernel(matrix_ref, values_ref, stiff_ref, out_ref):
    apply_rows(matrix_ref, values_ref, stiff_ref, out_ref)


def whole_sum(value):
    value = jnp.sum(value, axis=(0, 1))
    value = jnp.sum(value, axis=0, keepdims=True)
    return jnp.sum(value, axis=1, keepdims=True)


def solve_kernel(matrix_ref, joined_ref, out_ref, ahead_ref, image_ref, dir_ref, img_ref):
    stiff_ref = joined_ref.at[3]
    span_cells = stiff_ref.shape[0]
    residual = joined_ref[0:3]
    ahead_ref[:, 0:span_cells] = residual
    ahead_ref[:, span_cells : span_cells + 1] = jnp.zeros_like(residual[:, 0:1])
    apply_rows(matrix_ref, ahead_ref, stiff_ref, image_ref)
    image_vec = image_ref[:, 0:span_cells]
    norm_now = whole_sum(residual * residual)
    step_size = norm_now / whole_sum(residual * image_vec)
    dir_ref[...] = residual
    img_ref[...] = image_vec
    out_ref[...] = jnp.zeros_like(residual)
    for iteration in range(ITERS):
        out_ref[...] = out_ref[...] + step_size * dir_ref[...]
        residual = residual - step_size * img_ref[...]
        if iteration + 1 < ITERS:
            ahead_ref[:, 0:span_cells] = residual
            apply_rows(matrix_ref, ahead_ref, stiff_ref, image_ref)
            image_vec = image_ref[:, 0:span_cells]
            norm_next = whole_sum(residual * residual)
            curvature = whole_sum(residual * image_vec)
            beta_ratio = norm_next / norm_now
            step_size = norm_next / (curvature - beta_ratio * norm_next / step_size)
            dir_ref[...] = residual + beta_ratio * dir_ref[...]
            img_ref[...] = image_vec + beta_ratio * img_ref[...]
            norm_now = norm_next


def partition_solve_kernel(joined, matrix):
    span_cells, across_cells, deep_cells = joined.shape[1:]
    cells = span_cells * across_cells * deep_cells
    wide = (3, span_cells + 1, across_cells, deep_cells)
    side = (3, span_cells, across_cells, deep_cells)
    return pl.pallas_call(
        solve_kernel,
        out_shape=jax.ShapeDtypeStruct(side, jnp.float32),
        in_specs=[
            pl.BlockSpec(memory_space=pltpu.SMEM),
            pl.BlockSpec(memory_space=pltpu.VMEM),
        ],
        out_specs=pl.BlockSpec(memory_space=pltpu.VMEM),
        scratch_shapes=[
            pltpu.VMEM(wide, jnp.float32),
            pltpu.VMEM(wide, jnp.float32),
            pltpu.VMEM(side, jnp.float32),
            pltpu.VMEM(side, jnp.float32),
        ],
        cost_estimate=pl.CostEstimate(
            flops=ITERS * 2 * 24 * 24 * cells, transcendentals=0, bytes_accessed=28 * cells
        ),
    )(matrix, joined)


def partition_operator(values, stiffness, matrix):
    span_cells, across_cells, deep_cells = stiffness.shape
    widened = jnp.pad(values, ((0, 0), (0, 1), (0, 0), (0, 0)))
    cells = span_cells * across_cells * deep_cells
    summed = pl.pallas_call(
        operator_kernel,
        out_shape=jax.ShapeDtypeStruct(widened.shape, jnp.float32),
        in_specs=[
            pl.BlockSpec(memory_space=pltpu.SMEM),
            pl.BlockSpec(memory_space=pltpu.VMEM),
            pl.BlockSpec(memory_space=pltpu.VMEM),
        ],
        out_specs=pl.BlockSpec(memory_space=pltpu.VMEM),
        cost_estimate=pl.CostEstimate(
            flops=2 * 24 * 24 * cells, transcendentals=0, bytes_accessed=28 * cells
        ),
    )(matrix, widened, stiffness)
    return summed[:, :span_cells]


def whole_partition(block):
    lead = block.shape[:-3]
    count = len(lead)
    every = lax.all_gather(block, "gy", axis=count + 1, tiled=True)
    return lax.all_gather(every, "gx", axis=count, tiled=True)


def own_part(whole, rows, cols):
    start = (0, lax.axis_index("gx") * rows, lax.axis_index("gy") * cols, 0)
    return lax.dynamic_slice(whole, start, (whole.shape[0], rows, cols, whole.shape[3]))


def solve_structure(right_side, operator, products):
    residual = right_side
    image_vec = operator(residual)
    norm_now, curvature = products(residual, image_vec)
    step_size = norm_now / curvature
    direction, image_dir = (residual, image_vec)
    solution = jnp.zeros_like(right_side)
    for iteration in range(ITERS):
        solution = solution + step_size * direction
        residual = residual - step_size * image_dir
        if iteration + 1 < ITERS:
            image_vec = operator(residual)
            norm_next, curvature = products(residual, image_vec)
            beta_ratio = norm_next / norm_now
            step_size = norm_next / (curvature - beta_ratio * norm_next / step_size)
            direction = residual + beta_ratio * direction
            image_dir = image_vec + beta_ratio * image_dir
            norm_now = norm_next
    return solution


def per_device(
    populations,
    solid_mask,
    wall_cells,
    body_load,
    elem_scale,
    elem_active,
    elem_matrix,
    iface_nodes,
    iface_coords,
    neighbours,
):
    group_count = lax.axis_size("group")
    span_devices = lax.axis_size("gx")
    struct_groups = max(1, group_count // 8)
    fluid_groups = group_count - struct_groups
    group_index = lax.axis_index("group")
    slab_index = group_index * span_devices + lax.axis_index("gx")
    column_index = lax.axis_index("gy")
    is_fluid = group_index < fluid_groups
    is_struct = jnp.logical_not(is_fluid)
    span_cells, across_cells, deep_cells = solid_mask.shape
    cell_count = span_cells * across_cells * deep_cells
    fluid_here = jnp.where(is_fluid, 1.0 - solid_mask.astype(jnp.float32), 0.0)
    relaxed_pops = jnp.where(
        is_fluid, collide(populations.astype(jnp.float32)), 0.0
    ).astype(jnp.bfloat16)
    marker = fluid_here.astype(jnp.bfloat16)[None]
    widened = halo_exchange(
        jnp.concatenate([relaxed_pops, marker], axis=0), fluid_groups * span_devices
    )
    widened = jnp.pad(widened, ((0, 0), (0, 0), (0, 0), (1, 1))).astype(jnp.float32)
    moved = widened[0:19]
    fluid_ext = widened[19]
    wall_index = wall_cells.reshape(-1)
    point_count = wall_index.shape[0]
    tiles_out = point_count // TILE

    def fluid_pack(operands):
        upstream, opened, bounce, reflected = stream_links(operands[0], operands[1])
        force_parts = wall_force(bounce, reflected).reshape(3, cell_count)
        picked = force_parts[:, wall_index]
        span_pos = wall_index // (across_cells * deep_cells)
        across_pos = wall_index // deep_cells % across_cells + column_index * across_cells
        deep_pos = wall_index % deep_cells
        positions = jnp.stack(
            [
                (slab_index * span_cells + span_pos).astype(jnp.float32),
                across_pos.astype(jnp.float32),
                deep_pos.astype(jnp.float32),
            ]
        )
        packed = jnp.concatenate([picked, positions], axis=0)
        return packed.reshape(6, tiles_out, TILE).transpose(1, 0, 2)

    packed = lax.cond(
        is_fluid,
        fluid_pack,
        lambda operands: jnp.zeros((tiles_out, 6, TILE), jnp.float32),
        (moved, fluid_ext),
    )
    received = lax.all_gather(packed, "group", axis=0, tiled=True)
    node_index = iface_nodes.reshape(-1)
    node_positions = iface_coords.reshape(3, -1)
    tile_lists = neighbours.reshape(neighbours.shape[2], neighbours.shape[3])
    nodes_total = body_load.shape[1] * body_load.shape[2] * body_load.shape[3]
    weight_shape = (tile_lists.shape[0], TILE, tile_lists.shape[1], TILE)

    stiffness = elem_scale * elem_active.astype(jnp.float32)

    def struct_map(operands):
        received_all, flat = operands
        weights, chosen = basis_weights(received_all, node_positions, tile_lists)
        return (weights, map_tractions(weights, chosen, node_index, flat))

    def struct_quiet(operands):
        return (jnp.zeros(weight_shape, jnp.float32), operands[1])

    weights, right_side = lax.cond(
        is_struct, struct_map, struct_quiet, (received, body_load.reshape(3, nodes_total))
    )
    right_side = right_side.reshape(body_load.shape)
    joined = whole_partition(jnp.concatenate([right_side, stiffness[None]], axis=0))
    whole_side = joined[0:3]
    stiffness = joined[3]
    rows, cols = body_load.shape[1], body_load.shape[2]

    def partition_products(first_vec, second_vec):
        pair = (jnp.sum(first_vec * first_vec), jnp.sum(first_vec * second_vec))
        if struct_groups > 1:
            pair = lax.psum(tuple(jnp.where(is_struct, x, 0.0) for x in pair), "group")
        return pair

    def partition_solve(operands):
        side, stiff, matrix = operands
        return solve_structure(
            side, lambda values: partition_operator(values, stiff, matrix), partition_products
        )

    if struct_groups > 1:
        whole_solution = partition_solve((whole_side, stiffness, elem_matrix))
    else:
        whole_solution = lax.cond(
            is_struct,
            lambda operands: partition_solve_kernel(*operands),
            lambda operands: jnp.zeros_like(operands[0][0:3]),
            (joined, elem_matrix),
        )
    solution = jnp.where(is_struct, own_part(whole_solution, rows, cols), 0.0)
    tile_slots = received.shape[0]

    def struct_back(operands):
        return map_speeds(
            operands[0], operands[1], node_index, tile_lists, tile_slots
        )

    back_terms = lax.cond(
        is_struct,
        struct_back,
        lambda operands: jnp.zeros((tile_slots, 3, TILE), jnp.float32),
        (weights, solution),
    )
    per_group = tile_slots // group_count
    route_count = fluid_groups // struct_groups
    sender_slot = jnp.clip(group_index - fluid_groups, 0, struct_groups - 1)
    own_speeds = jnp.zeros((per_group, 3, TILE), jnp.float32)
    for route_step in range(route_count):
        offset_row = (sender_slot + route_step * struct_groups) * per_group
        outgoing = lax.dynamic_slice_in_dim(back_terms, offset_row, per_group, 0)
        incoming = passed_along(outgoing, "group", (route_step + 1) * struct_groups)
        own_speeds = own_speeds + jnp.where(
            group_index // struct_groups == route_step, incoming, 0.0
        )
    speed_parts = wall_gain * own_speeds.transpose(1, 0, 2).reshape(3, point_count)
    wall_speed = jnp.zeros((3, cell_count), jnp.float32).at[:, wall_index].add(speed_parts)
    wall_speed = wall_speed.reshape(3, span_cells, across_cells, deep_cells)
    new_populations = lax.cond(
        is_fluid,
        lambda operands: stream_all(operands[0], operands[1], operands[2]),
        lambda operands: jnp.zeros(operands[0][:, 1:-1, 1:-1, 1:-1].shape, jnp.bfloat16),
        (moved, fluid_ext, wall_speed),
    )
    return (new_populations, solution)


def solution(mesh):
    placed = (
        P(None, ("group", "gx"), "gy", None),
        P(("group", "gx"), "gy", None),
        P(("group", "gx"), "gy", None),
        P(None, ("group", "gx"), "gy", None),
        P(("group", "gx"), "gy", None),
        P(("group", "gx"), "gy", None),
        P(),
        P(("group", "gx"), "gy", None),
        P(None, ("group", "gx"), "gy", None),
        P(("group", "gx"), "gy", None, None),
    )
    return jax.shard_map(
        per_device,
        mesh=mesh,
        in_specs=placed,
        out_specs=(P(None, ("group", "gx"), "gy", None), P(None, ("group", "gx"), "gy", None)),
        check_vma=False,
    )
```

```python
import jax
import jax.numpy as jnp
import numpy as np
from jax import lax
from jax.sharding import PartitionSpec as P
from jax.experimental import pallas as pl
from jax.experimental.pallas import tpu as pltpu

TILE = 128
ITERS = 3


velocity = [
    (0, 0, 0),
    (1, 0, 0),
    (-1, 0, 0),
    (0, 1, 0),
    (0, -1, 0),
    (0, 0, 1),
    (0, 0, -1),
    (1, 1, 0),
    (-1, -1, 0),
    (1, -1, 0),
    (-1, 1, 0),
    (1, 0, 1),
    (-1, 0, -1),
    (1, 0, -1),
    (-1, 0, 1),
    (0, 1, 1),
    (0, -1, -1),
    (0, 1, -1),
    (0, -1, 1),
]
opposite = [0, 2, 1, 4, 3, 6, 5, 8, 7, 10, 9, 12, 11, 14, 13, 16, 15, 18, 17]
lattice_weight = [1.0 / 3.0] + [1.0 / 18.0] * 6 + [1.0 / 36.0] * 12
relax_rate = 1.0 / 0.6
wall_gain = 60.0
basis_radius = 24.0
mass_shift = 0.5


def halo_exchange(cells, span_devices):
    columns = lax.axis_size("gy")
    axes = ("group", "gx", "gy")

    def shifted(piece, dr, dc):
        pairs = [
            (r * columns + c, (r + dr) * columns + c + dc)
            for r in range(span_devices)
            for c in range(columns)
            if 0 <= r + dr < span_devices and 0 <= c + dc < columns
        ]
        return lax.ppermute(piece, axes, pairs)

    cols = cells.shape[2]
    column = lax.axis_index("gy")
    edges = jnp.concatenate([cells[:, :, :1], cells[:, :, cols - 1 :]], axis=2)
    every = lax.all_gather(edges, "gy", axis=0)
    from_left = lax.dynamic_index_in_dim(every, jnp.maximum(column - 1, 0), 0, False)
    from_right = lax.dynamic_index_in_dim(every, jnp.minimum(column + 1, columns - 1), 0, False)
    cells = jnp.concatenate(
        [
            jnp.where(column > 0, from_left[:, :, 1:], 0.0).astype(cells.dtype),
            cells,
            jnp.where(column < columns - 1, from_right[:, :, :1], 0.0).astype(cells.dtype),
        ],
        axis=2,
    )
    rows = cells.shape[1]
    return jnp.concatenate(
        [shifted(cells[:, rows - 1 :], 1, 0), cells, shifted(cells[:, :1], -1, 0)], axis=1
    )


def passed_along(value, axis, steps):
    count = lax.axis_size(axis)
    pairs = [(source, (source + steps) % count) for source in range(count)]
    return lax.ppermute(value, axis, pairs)


def project_onto(vectors, direction):
    summed = jnp.zeros_like(vectors[0])
    for component in range(3):
        if direction[component] != 0:
            summed = summed + float(direction[component]) * vectors[component]
    return summed


def per_direction(values):
    return jnp.asarray(np.array(values, np.float32).reshape(19, 1, 1, 1))


def collide(population):
    density = jnp.sum(population, axis=0)
    velocity_parts = [
        jnp.sum(per_direction([c[component] for c in velocity]) * population, axis=0) / density
        for component in range(3)
    ]
    speed_square = (
        velocity_parts[0] * velocity_parts[0]
        + velocity_parts[1] * velocity_parts[1]
        + velocity_parts[2] * velocity_parts[2]
    )
    project = project_all(velocity_parts)
    balance = (
        per_direction(lattice_weight)
        * density
        * (1.0 + 3.0 * project + 4.5 * project * project - 1.5 * speed_square)
    )
    return population + relax_rate * (balance - population)


def project_all(vectors):
    summed = per_direction([c[0] for c in velocity]) * vectors[0]
    for component in (1, 2):
        summed = summed + per_direction([c[component] for c in velocity]) * vectors[component]
    return summed


def upstream_of(values, inner):
    for axis in range(3):
        shift = per_direction([c[axis] for c in velocity])
        pick = {
            s: lax.slice_in_dim(values, 1 - s, 1 - s + inner[axis], axis=axis + 1)
            for s in (-1, 0, 1)
        }
        values = jnp.where(shift > 0.5, pick[1], jnp.where(shift < -0.5, pick[-1], pick[0]))
    return values


def stream_links(moved, fluid_ext):
    inner = tuple(size - 2 for size in fluid_ext.shape)
    upstream = upstream_of(moved, inner)
    opened = upstream_of(jnp.broadcast_to(fluid_ext[None], (19,) + fluid_ext.shape), inner)
    bounce = 1.0 - opened
    centre = moved[:, 1 : inner[0] + 1, 1 : inner[1] + 1, 1 : inner[2] + 1]
    paired = centre[1:].reshape((9, 2) + inner)[:, ::-1].reshape((18,) + inner)
    reflected = jnp.concatenate([centre[0:1], paired], axis=0)
    return (upstream, opened, bounce, reflected)


def wall_force(bounce, reflected):
    carried = bounce * reflected
    return jnp.stack(
        [
            jnp.sum(per_direction([-2.0 * c[component] for c in velocity]) * carried, axis=0)
            for component in range(3)
        ]
    )


def stream_all(moved, fluid_ext, wall_speed):
    upstream, opened, bounce, reflected = stream_links(moved, fluid_ext)
    inside = fluid_ext[1:-1, 1:-1, 1:-1]
    speed_list = [wall_speed[0], wall_speed[1], wall_speed[2]]
    correction = per_direction([6.0 * w for w in lattice_weight]) * project_all(speed_list)
    result = inside * (opened * upstream + bounce * (reflected + correction))
    return result.astype(jnp.bfloat16)


def slot_table(tile_lists, tile_slots):
    slots = lax.broadcasted_iota(jnp.int32, (tile_slots, tile_lists.size), 0)
    return (slots == tile_lists.reshape(1, -1)).astype(jnp.float32)


def basis_weights(received, node_positions, tile_lists):
    tile_count = tile_lists.shape[0]
    tile_width = received.shape[2]
    chosen = received[tile_lists]
    nodes_at = node_positions.reshape(3, tile_count, tile_width)
    distance = jnp.zeros((tile_count, tile_width, tile_lists.shape[1], tile_width), jnp.float32)
    for component in range(3):
        offset = nodes_at[component][:, :, None, None] - chosen[:, None, :, 3 + component, :]
        distance = distance + offset * offset
    kernel = 1.0 / jnp.sqrt(1.0 + distance / (basis_radius * basis_radius))
    column = jnp.sum(kernel, axis=1).reshape(-1, tile_width)
    table = slot_table(tile_lists, received.shape[0])
    exact = lax.Precision.HIGHEST
    totals = jnp.einsum("tk,kp->tp", table, column, precision=exact)
    listed = jnp.einsum("tk,tp->kp", table, totals, precision=exact)
    listed = listed.reshape(tile_count, tile_lists.shape[1], tile_width)
    return (kernel / listed[:, None, :, :], chosen)


def map_tractions(weights, chosen, node_index, base):
    mapped = jnp.einsum(
        "anbp,abcp->can", weights, chosen[:, :, 0:3, :], precision=lax.Precision.HIGHEST
    )
    return base.at[:, node_index].add(mapped.reshape(3, -1))


def map_speeds(weights, solution_block, node_index, tile_lists, tile_slots):
    tile_count = weights.shape[0]
    tile_width = weights.shape[1]
    flat = solution_block.reshape(3, -1)
    at_nodes = flat[:, node_index].reshape(3, tile_count, tile_width)
    contrib = jnp.einsum("anbp,can->abcp", weights, at_nodes, precision=lax.Precision.HIGHEST)
    return jnp.einsum(
        "tk,kcp->tcp",
        slot_table(tile_lists, tile_slots),
        contrib.reshape(-1, 3, tile_width),
        precision=lax.Precision.HIGHEST,
    )


def apply_rows(matrix_ref, values_ref, stiff_ref, out_ref):
    span_cells, across_cells, deep_cells = stiff_ref.shape
    step = next(size for size in (8, 4, 2, 1) if span_cells % size == 0)
    shape = (step, across_cells, deep_cells)
    across_at = lax.broadcasted_iota(jnp.int32, shape, 1)
    deep_at = lax.broadcasted_iota(jnp.int32, shape, 2)
    corners = [(a, b, c) for a in (0, 1) for b in (0, 1) for c in (0, 1)]
    for component in range(3):
        out_ref[component, 0:span_cells] = mass_shift * values_ref[component, 0:span_cells]
        out_ref[component, span_cells] = jnp.zeros((across_cells, deep_cells), jnp.float32)

    def ahead(value, across, deep):
        if across:
            value = jnp.where(
                across_at < across_cells - 1, pltpu.roll(value, across_cells - 1, 1), 0.0
            )
        if deep:
            value = jnp.where(deep_at < deep_cells - 1, pltpu.roll(value, deep_cells - 1, 2), 0.0)
        return value

    def behind(value, across, deep):
        if across:
            value = jnp.where(across_at >= 1, pltpu.roll(value, 1, 1), 0.0)
        if deep:
            value = jnp.where(deep_at >= 1, pltpu.roll(value, 1, 2), 0.0)
        return value

    def element_rows(block, carry):
        row = block * step
        gathered = []
        for a, b, c in corners:
            for component in range(3):
                gathered.append(ahead(values_ref[component, pl.ds(row + a, step)], b, c))
        scale = stiff_ref[pl.ds(row, step)]
        for corner_id, (a, b, c) in enumerate(corners):
            for component in range(3):
                line = 3 * corner_id + component
                force = matrix_ref[line, 0] * gathered[0]
                for other in range(1, 24):
                    force = force + matrix_ref[line, other] * gathered[other]
                out_ref[component, pl.ds(row + a, step)] += behind(scale * force, b, c)
        return carry

    lax.fori_loop(0, span_cells // step, element_rows, 0)


def operator_kernel(matrix_ref, values_ref, stiff_ref, out_ref):
    apply_rows(matrix_ref, values_ref, stiff_ref, out_ref)


def whole_sum(value):
    value = jnp.sum(value, axis=(0, 1))
    value = jnp.sum(value, axis=0, keepdims=True)
    return jnp.sum(value, axis=1, keepdims=True)


def solve_kernel(matrix_ref, joined_ref, out_ref, ahead_ref, image_ref, dir_ref, img_ref):
    stiff_ref = joined_ref.at[3]
    span_cells = stiff_ref.shape[0]
    residual = joined_ref[0:3]
    ahead_ref[:, 0:span_cells] = residual
    ahead_ref[:, span_cells : span_cells + 1] = jnp.zeros_like(residual[:, 0:1])
    apply_rows(matrix_ref, ahead_ref, stiff_ref, image_ref)
    image_vec = image_ref[:, 0:span_cells]
    norm_now = whole_sum(residual * residual)
    step_size = norm_now / whole_sum(residual * image_vec)
    dir_ref[...] = residual
    img_ref[...] = image_vec
    out_ref[...] = jnp.zeros_like(residual)
    for iteration in range(ITERS):
        out_ref[...] = out_ref[...] + step_size * dir_ref[...]
        residual = residual - step_size * img_ref[...]
        if iteration + 1 < ITERS:
            ahead_ref[:, 0:span_cells] = residual
            apply_rows(matrix_ref, ahead_ref, stiff_ref, image_ref)
            image_vec = image_ref[:, 0:span_cells]
            norm_next = whole_sum(residual * residual)
            curvature = whole_sum(residual * image_vec)
            beta_ratio = norm_next / norm_now
            step_size = norm_next / (curvature - beta_ratio * norm_next / step_size)
            dir_ref[...] = residual + beta_ratio * dir_ref[...]
            img_ref[...] = image_vec + beta_ratio * img_ref[...]
            norm_now = norm_next


def partition_solve_kernel(joined, matrix):
    span_cells, across_cells, deep_cells = joined.shape[1:]
    cells = span_cells * across_cells * deep_cells
    wide = (3, span_cells + 1, across_cells, deep_cells)
    side = (3, span_cells, across_cells, deep_cells)
    return pl.pallas_call(
        solve_kernel,
        out_shape=jax.ShapeDtypeStruct(side, jnp.float32),
        in_specs=[
            pl.BlockSpec(memory_space=pltpu.SMEM),
            pl.BlockSpec(memory_space=pltpu.VMEM),
        ],
        out_specs=pl.BlockSpec(memory_space=pltpu.VMEM),
        scratch_shapes=[
            pltpu.VMEM(wide, jnp.float32),
            pltpu.VMEM(wide, jnp.float32),
            pltpu.VMEM(side, jnp.float32),
            pltpu.VMEM(side, jnp.float32),
        ],
        cost_estimate=pl.CostEstimate(
            flops=ITERS * 2 * 24 * 24 * cells, transcendentals=0, bytes_accessed=28 * cells
        ),
    )(matrix, joined)


def partition_operator(values, stiffness, matrix):
    span_cells, across_cells, deep_cells = stiffness.shape
    widened = jnp.pad(values, ((0, 0), (0, 1), (0, 0), (0, 0)))
    cells = span_cells * across_cells * deep_cells
    summed = pl.pallas_call(
        operator_kernel,
        out_shape=jax.ShapeDtypeStruct(widened.shape, jnp.float32),
        in_specs=[
            pl.BlockSpec(memory_space=pltpu.SMEM),
            pl.BlockSpec(memory_space=pltpu.VMEM),
            pl.BlockSpec(memory_space=pltpu.VMEM),
        ],
        out_specs=pl.BlockSpec(memory_space=pltpu.VMEM),
        cost_estimate=pl.CostEstimate(
            flops=2 * 24 * 24 * cells, transcendentals=0, bytes_accessed=28 * cells
        ),
    )(matrix, widened, stiffness)
    return summed[:, :span_cells]


def whole_partition(block):
    lead = block.shape[:-3]
    count = len(lead)
    every = lax.all_gather(block, "gy", axis=count + 1, tiled=True)
    return lax.all_gather(every, "gx", axis=count, tiled=True)


def own_part(whole, rows, cols):
    start = (0, lax.axis_index("gx") * rows, lax.axis_index("gy") * cols, 0)
    return lax.dynamic_slice(whole, start, (whole.shape[0], rows, cols, whole.shape[3]))


def solve_structure(right_side, operator, products):
    residual = right_side
    image_vec = operator(residual)
    norm_now, curvature = products(residual, image_vec)
    step_size = norm_now / curvature
    direction, image_dir = (residual, image_vec)
    solution = jnp.zeros_like(right_side)
    for iteration in range(ITERS):
        solution = solution + step_size * direction
        residual = residual - step_size * image_dir
        if iteration + 1 < ITERS:
            image_vec = operator(residual)
            norm_next, curvature = products(residual, image_vec)
            beta_ratio = norm_next / norm_now
            step_size = norm_next / (curvature - beta_ratio * norm_next / step_size)
            direction = residual + beta_ratio * direction
            image_dir = image_vec + beta_ratio * image_dir
            norm_now = norm_next
    return solution


def per_device(
    populations,
    solid_mask,
    wall_cells,
    body_load,
    elem_scale,
    elem_active,
    elem_matrix,
    iface_nodes,
    iface_coords,
    neighbours,
):
    group_count = lax.axis_size("group")
    span_devices = lax.axis_size("gx")
    struct_groups = max(1, group_count // 8)
    fluid_groups = group_count - struct_groups
    group_index = lax.axis_index("group")
    slab_index = group_index * span_devices + lax.axis_index("gx")
    column_index = lax.axis_index("gy")
    is_fluid = group_index < fluid_groups
    is_struct = jnp.logical_not(is_fluid)
    span_cells, across_cells, deep_cells = solid_mask.shape
    cell_count = span_cells * across_cells * deep_cells
    fluid_here = jnp.where(is_fluid, 1.0 - solid_mask.astype(jnp.float32), 0.0)
    relaxed_pops = jnp.where(
        is_fluid, collide(populations.astype(jnp.float32)), 0.0
    ).astype(jnp.bfloat16)
    marker = fluid_here.astype(jnp.bfloat16)[None]
    widened = halo_exchange(
        jnp.concatenate([relaxed_pops, marker], axis=0), fluid_groups * span_devices
    )
    widened = jnp.pad(widened, ((0, 0), (0, 0), (0, 0), (1, 1))).astype(jnp.float32)
    moved = widened[0:19]
    fluid_ext = widened[19]
    wall_index = wall_cells.reshape(-1)
    point_count = wall_index.shape[0]
    tiles_out = point_count // TILE

    def fluid_pack(operands):
        upstream, opened, bounce, reflected = stream_links(operands[0], operands[1])
        force_parts = wall_force(bounce, reflected).reshape(3, cell_count)
        picked = jnp.stack([jnp.take(force_parts[k], wall_index) for k in range(3)])
        span_pos = wall_index // (across_cells * deep_cells)
        across_pos = wall_index // deep_cells % across_cells + column_index * across_cells
        deep_pos = wall_index % deep_cells
        positions = jnp.stack(
            [
                (slab_index * span_cells + span_pos).astype(jnp.float32),
                across_pos.astype(jnp.float32),
                deep_pos.astype(jnp.float32),
            ]
        )
        packed = jnp.concatenate([picked, positions], axis=0)
        return packed.reshape(6, tiles_out, TILE).transpose(1, 0, 2)

    packed = lax.cond(
        is_fluid,
        fluid_pack,
        lambda operands: jnp.zeros((tiles_out, 6, TILE), jnp.float32),
        (moved, fluid_ext),
    )
    received = lax.all_gather(packed, "group", axis=0, tiled=True)
    node_index = iface_nodes.reshape(-1)
    node_positions = iface_coords.reshape(3, -1)
    tile_lists = neighbours.reshape(neighbours.shape[2], neighbours.shape[3])
    nodes_total = body_load.shape[1] * body_load.shape[2] * body_load.shape[3]
    weight_shape = (tile_lists.shape[0], TILE, tile_lists.shape[1], TILE)

    stiffness = elem_scale * elem_active.astype(jnp.float32)

    def struct_map(operands):
        received_all, flat = operands
        weights, chosen = basis_weights(received_all, node_positions, tile_lists)
        return (weights, map_tractions(weights, chosen, node_index, flat))

    def struct_quiet(operands):
        return (jnp.zeros(weight_shape, jnp.float32), operands[1])

    weights, right_side = lax.cond(
        is_struct, struct_map, struct_quiet, (received, body_load.reshape(3, nodes_total))
    )
    right_side = right_side.reshape(body_load.shape)
    joined = whole_partition(jnp.concatenate([right_side, stiffness[None]], axis=0))
    whole_side = joined[0:3]
    stiffness = joined[3]
    rows, cols = body_load.shape[1], body_load.shape[2]

    def partition_products(first_vec, second_vec):
        pair = (jnp.sum(first_vec * first_vec), jnp.sum(first_vec * second_vec))
        if struct_groups > 1:
            pair = lax.psum(tuple(jnp.where(is_struct, x, 0.0) for x in pair), "group")
        return pair

    def partition_solve(operands):
        side, stiff, matrix = operands
        return solve_structure(
            side, lambda values: partition_operator(values, stiff, matrix), partition_products
        )

    if struct_groups > 1:
        whole_solution = partition_solve((whole_side, stiffness, elem_matrix))
    else:
        whole_solution = lax.cond(
            is_struct,
            lambda operands: partition_solve_kernel(*operands),
            lambda operands: jnp.zeros_like(operands[0][0:3]),
            (joined, elem_matrix),
        )
    solution = jnp.where(is_struct, own_part(whole_solution, rows, cols), 0.0)
    tile_slots = received.shape[0]

    def struct_back(operands):
        return map_speeds(
            operands[0], operands[1], node_index, tile_lists, tile_slots
        )

    back_terms = lax.cond(
        is_struct,
        struct_back,
        lambda operands: jnp.zeros((tile_slots, 3, TILE), jnp.float32),
        (weights, solution),
    )
    per_group = tile_slots // group_count
    route_count = fluid_groups // struct_groups
    sender_slot = jnp.clip(group_index - fluid_groups, 0, struct_groups - 1)
    own_speeds = jnp.zeros((per_group, 3, TILE), jnp.float32)
    for route_step in range(route_count):
        offset_row = (sender_slot + route_step * struct_groups) * per_group
        outgoing = lax.dynamic_slice_in_dim(back_terms, offset_row, per_group, 0)
        incoming = passed_along(outgoing, "group", (route_step + 1) * struct_groups)
        own_speeds = own_speeds + jnp.where(
            group_index // struct_groups == route_step, incoming, 0.0
        )
    speed_parts = wall_gain * own_speeds.transpose(1, 0, 2).reshape(3, point_count)
    wall_speed = jnp.zeros((3, cell_count), jnp.float32).at[:, wall_index].add(speed_parts)
    wall_speed = wall_speed.reshape(3, span_cells, across_cells, deep_cells)
    new_populations = lax.cond(
        is_fluid,
        lambda operands: stream_all(operands[0], operands[1], operands[2]),
        lambda operands: jnp.zeros(operands[0][:, 1:-1, 1:-1, 1:-1].shape, jnp.bfloat16),
        (moved, fluid_ext, wall_speed),
    )
    return (new_populations, solution)


def solution(mesh):
    placed = (
        P(None, ("group", "gx"), "gy", None),
        P(("group", "gx"), "gy", None),
        P(("group", "gx"), "gy", None),
        P(None, ("group", "gx"), "gy", None),
        P(("group", "gx"), "gy", None),
        P(("group", "gx"), "gy", None),
        P(),
        P(("group", "gx"), "gy", None),
        P(None, ("group", "gx"), "gy", None),
        P(("group", "gx"), "gy", None, None),
    )
    return jax.shard_map(
        per_device,
        mesh=mesh,
        in_specs=placed,
        out_specs=(P(None, ("group", "gx"), "gy", None), P(None, ("group", "gx"), "gy", None)),
        check_vma=False,
    )
```

```python
import jax
import jax.numpy as jnp
import numpy as np
from jax import lax
from jax.sharding import PartitionSpec as P
from jax.experimental import pallas as pl
from jax.experimental.pallas import tpu as pltpu

TILE = 128
ITERS = 3


velocity = [
    (0, 0, 0),
    (1, 0, 0),
    (-1, 0, 0),
    (0, 1, 0),
    (0, -1, 0),
    (0, 0, 1),
    (0, 0, -1),
    (1, 1, 0),
    (-1, -1, 0),
    (1, -1, 0),
    (-1, 1, 0),
    (1, 0, 1),
    (-1, 0, -1),
    (1, 0, -1),
    (-1, 0, 1),
    (0, 1, 1),
    (0, -1, -1),
    (0, 1, -1),
    (0, -1, 1),
]
opposite = [0, 2, 1, 4, 3, 6, 5, 8, 7, 10, 9, 12, 11, 14, 13, 16, 15, 18, 17]
lattice_weight = [1.0 / 3.0] + [1.0 / 18.0] * 6 + [1.0 / 36.0] * 12
relax_rate = 1.0 / 0.6
wall_gain = 60.0
basis_radius = 24.0
mass_shift = 0.5


def halo_exchange(cells, span_devices):
    columns = lax.axis_size("gy")
    axes = ("group", "gx", "gy")

    def shifted(piece, dr, dc):
        pairs = [
            (r * columns + c, (r + dr) * columns + c + dc)
            for r in range(span_devices)
            for c in range(columns)
            if 0 <= r + dr < span_devices and 0 <= c + dc < columns
        ]
        return lax.ppermute(piece, axes, pairs)

    cols = cells.shape[2]
    column = lax.axis_index("gy")
    edges = jnp.concatenate([cells[:, :, :1], cells[:, :, cols - 1 :]], axis=2)
    every = lax.all_gather(edges, "gy", axis=0)
    from_left = lax.dynamic_index_in_dim(every, jnp.maximum(column - 1, 0), 0, False)
    from_right = lax.dynamic_index_in_dim(every, jnp.minimum(column + 1, columns - 1), 0, False)
    cells = jnp.concatenate(
        [
            jnp.where(column > 0, from_left[:, :, 1:], 0.0).astype(cells.dtype),
            cells,
            jnp.where(column < columns - 1, from_right[:, :, :1], 0.0).astype(cells.dtype),
        ],
        axis=2,
    )
    rows = cells.shape[1]
    return jnp.concatenate(
        [shifted(cells[:, rows - 1 :], 1, 0), cells, shifted(cells[:, :1], -1, 0)], axis=1
    )


def passed_along(value, axis, steps):
    count = lax.axis_size(axis)
    pairs = [(source, (source + steps) % count) for source in range(count)]
    return lax.ppermute(value, axis, pairs)


def project_onto(vectors, direction):
    summed = jnp.zeros_like(vectors[0])
    for component in range(3):
        if direction[component] != 0:
            summed = summed + float(direction[component]) * vectors[component]
    return summed


def per_direction(values):
    return jnp.asarray(np.array(values, np.float32).reshape(19, 1, 1, 1))


def collide(population):
    density = jnp.sum(population, axis=0)
    velocity_parts = [
        jnp.sum(per_direction([c[component] for c in velocity]) * population, axis=0) / density
        for component in range(3)
    ]
    speed_square = (
        velocity_parts[0] * velocity_parts[0]
        + velocity_parts[1] * velocity_parts[1]
        + velocity_parts[2] * velocity_parts[2]
    )
    project = project_all(velocity_parts)
    balance = (
        per_direction(lattice_weight)
        * density
        * (1.0 + 3.0 * project + 4.5 * project * project - 1.5 * speed_square)
    )
    return population + relax_rate * (balance - population)


def project_all(vectors):
    summed = per_direction([c[0] for c in velocity]) * vectors[0]
    for component in (1, 2):
        summed = summed + per_direction([c[component] for c in velocity]) * vectors[component]
    return summed


def upstream_of(values, inner):
    for axis in range(3):
        shift = per_direction([c[axis] for c in velocity])
        pick = {
            s: lax.slice_in_dim(values, 1 - s, 1 - s + inner[axis], axis=axis + 1)
            for s in (-1, 0, 1)
        }
        values = jnp.where(shift > 0.5, pick[1], jnp.where(shift < -0.5, pick[-1], pick[0]))
    return values


def stream_links(moved, fluid_ext):
    inner = tuple(size - 2 for size in fluid_ext.shape)
    upstream = upstream_of(moved, inner)
    opened = upstream_of(jnp.broadcast_to(fluid_ext[None], (19,) + fluid_ext.shape), inner)
    bounce = 1.0 - opened
    centre = moved[:, 1 : inner[0] + 1, 1 : inner[1] + 1, 1 : inner[2] + 1]
    paired = centre[1:].reshape((9, 2) + inner)[:, ::-1].reshape((18,) + inner)
    reflected = jnp.concatenate([centre[0:1], paired], axis=0)
    return (upstream, opened, bounce, reflected)


def wall_force(bounce, reflected):
    carried = bounce * reflected
    return jnp.stack(
        [
            jnp.sum(per_direction([-2.0 * c[component] for c in velocity]) * carried, axis=0)
            for component in range(3)
        ]
    )


def stream_all(moved, fluid_ext, wall_speed):
    upstream, opened, bounce, reflected = stream_links(moved, fluid_ext)
    inside = fluid_ext[1:-1, 1:-1, 1:-1]
    speed_list = [wall_speed[0], wall_speed[1], wall_speed[2]]
    correction = per_direction([6.0 * w for w in lattice_weight]) * project_all(speed_list)
    result = inside * (opened * upstream + bounce * (reflected + correction))
    return result.astype(jnp.bfloat16)


def slot_table(tile_lists, tile_slots):
    slots = lax.broadcasted_iota(jnp.int32, (tile_slots, tile_lists.size), 0)
    return (slots == tile_lists.reshape(1, -1)).astype(jnp.float32)


def basis_weights(received, node_positions, tile_lists):
    tile_count = tile_lists.shape[0]
    tile_width = received.shape[2]
    chosen = received[tile_lists]
    nodes_at = node_positions.reshape(3, tile_count, tile_width)
    distance = jnp.zeros((tile_count, tile_width, tile_lists.shape[1], tile_width), jnp.float32)
    for component in range(3):
        offset = nodes_at[component][:, :, None, None] - chosen[:, None, :, 3 + component, :]
        distance = distance + offset * offset
    kernel = 1.0 / jnp.sqrt(1.0 + distance / (basis_radius * basis_radius))
    column = jnp.sum(kernel, axis=1).reshape(-1, tile_width)
    table = slot_table(tile_lists, received.shape[0])
    exact = lax.Precision.HIGHEST
    totals = jnp.einsum("tk,kp->tp", table, column, precision=exact)
    listed = jnp.einsum("tk,tp->kp", table, totals, precision=exact)
    listed = listed.reshape(tile_count, tile_lists.shape[1], tile_width)
    return (kernel / listed[:, None, :, :], chosen)


def map_tractions(weights, chosen, node_index, base):
    mapped = jnp.einsum(
        "anbp,abcp->can", weights, chosen[:, :, 0:3, :], precision=lax.Precision.HIGHEST
    )
    return base.at[:, node_index].add(mapped.reshape(3, -1))


def map_speeds(weights, solution_block, node_index, tile_lists, tile_slots):
    tile_count = weights.shape[0]
    tile_width = weights.shape[1]
    flat = solution_block.reshape(3, -1)
    at_nodes = flat[:, node_index].reshape(3, tile_count, tile_width)
    contrib = jnp.einsum("anbp,can->abcp", weights, at_nodes, precision=lax.Precision.HIGHEST)
    return jnp.einsum(
        "tk,kcp->tcp",
        slot_table(tile_lists, tile_slots),
        contrib.reshape(-1, 3, tile_width),
        precision=lax.Precision.HIGHEST,
    )


def apply_rows(matrix_ref, values_ref, stiff_ref, out_ref):
    span_cells, across_cells, deep_cells = stiff_ref.shape
    step = next(size for size in (16, 8, 4, 2, 1) if span_cells % size == 0)
    shape = (step, across_cells, deep_cells)
    across_at = lax.broadcasted_iota(jnp.int32, shape, 1)
    deep_at = lax.broadcasted_iota(jnp.int32, shape, 2)
    corners = [(a, b, c) for a in (0, 1) for b in (0, 1) for c in (0, 1)]
    for component in range(3):
        out_ref[component, 0:span_cells] = mass_shift * values_ref[component, 0:span_cells]
        out_ref[component, span_cells] = jnp.zeros((across_cells, deep_cells), jnp.float32)

    def ahead(value, across, deep):
        if across:
            value = jnp.where(
                across_at < across_cells - 1, pltpu.roll(value, across_cells - 1, 1), 0.0
            )
        if deep:
            value = jnp.where(deep_at < deep_cells - 1, pltpu.roll(value, deep_cells - 1, 2), 0.0)
        return value

    def behind(value, across, deep):
        if across:
            value = jnp.where(across_at >= 1, pltpu.roll(value, 1, 1), 0.0)
        if deep:
            value = jnp.where(deep_at >= 1, pltpu.roll(value, 1, 2), 0.0)
        return value

    def element_rows(block, carry):
        row = block * step
        gathered = []
        for a, b, c in corners:
            for component in range(3):
                gathered.append(ahead(values_ref[component, pl.ds(row + a, step)], b, c))
        scale = stiff_ref[pl.ds(row, step)]
        for corner_id, (a, b, c) in enumerate(corners):
            for component in range(3):
                line = 3 * corner_id + component
                force = matrix_ref[line, 0] * gathered[0]
                for other in range(1, 24):
                    force = force + matrix_ref[line, other] * gathered[other]
                out_ref[component, pl.ds(row + a, step)] += behind(scale * force, b, c)
        return carry

    lax.fori_loop(0, span_cells // step, element_rows, 0)


def operator_kernel(matrix_ref, values_ref, stiff_ref, out_ref):
    apply_rows(matrix_ref, values_ref, stiff_ref, out_ref)


def whole_sum(value):
    value = jnp.sum(value, axis=(0, 1))
    value = jnp.sum(value, axis=0, keepdims=True)
    return jnp.sum(value, axis=1, keepdims=True)


def solve_kernel(matrix_ref, joined_ref, out_ref, ahead_ref, image_ref, dir_ref, img_ref):
    stiff_ref = joined_ref.at[3]
    span_cells = stiff_ref.shape[0]
    residual = joined_ref[0:3]
    ahead_ref[:, 0:span_cells] = residual
    ahead_ref[:, span_cells : span_cells + 1] = jnp.zeros_like(residual[:, 0:1])
    apply_rows(matrix_ref, ahead_ref, stiff_ref, image_ref)
    image_vec = image_ref[:, 0:span_cells]
    norm_now = whole_sum(residual * residual)
    step_size = norm_now / whole_sum(residual * image_vec)
    dir_ref[...] = residual
    img_ref[...] = image_vec
    out_ref[...] = jnp.zeros_like(residual)
    for iteration in range(ITERS):
        out_ref[...] = out_ref[...] + step_size * dir_ref[...]
        residual = residual - step_size * img_ref[...]
        if iteration + 1 < ITERS:
            ahead_ref[:, 0:span_cells] = residual
            apply_rows(matrix_ref, ahead_ref, stiff_ref, image_ref)
            image_vec = image_ref[:, 0:span_cells]
            norm_next = whole_sum(residual * residual)
            curvature = whole_sum(residual * image_vec)
            beta_ratio = norm_next / norm_now
            step_size = norm_next / (curvature - beta_ratio * norm_next / step_size)
            dir_ref[...] = residual + beta_ratio * dir_ref[...]
            img_ref[...] = image_vec + beta_ratio * img_ref[...]
            norm_now = norm_next


def partition_solve_kernel(joined, matrix):
    span_cells, across_cells, deep_cells = joined.shape[1:]
    cells = span_cells * across_cells * deep_cells
    wide = (3, span_cells + 1, across_cells, deep_cells)
    side = (3, span_cells, across_cells, deep_cells)
    return pl.pallas_call(
        solve_kernel,
        out_shape=jax.ShapeDtypeStruct(side, jnp.float32),
        in_specs=[
            pl.BlockSpec(memory_space=pltpu.SMEM),
            pl.BlockSpec(memory_space=pltpu.VMEM),
        ],
        out_specs=pl.BlockSpec(memory_space=pltpu.VMEM),
        scratch_shapes=[
            pltpu.VMEM(wide, jnp.float32),
            pltpu.VMEM(wide, jnp.float32),
            pltpu.VMEM(side, jnp.float32),
            pltpu.VMEM(side, jnp.float32),
        ],
        cost_estimate=pl.CostEstimate(
            flops=ITERS * 2 * 24 * 24 * cells, transcendentals=0, bytes_accessed=28 * cells
        ),
    )(matrix, joined)


def partition_operator(values, stiffness, matrix):
    span_cells, across_cells, deep_cells = stiffness.shape
    widened = jnp.pad(values, ((0, 0), (0, 1), (0, 0), (0, 0)))
    cells = span_cells * across_cells * deep_cells
    summed = pl.pallas_call(
        operator_kernel,
        out_shape=jax.ShapeDtypeStruct(widened.shape, jnp.float32),
        in_specs=[
            pl.BlockSpec(memory_space=pltpu.SMEM),
            pl.BlockSpec(memory_space=pltpu.VMEM),
            pl.BlockSpec(memory_space=pltpu.VMEM),
        ],
        out_specs=pl.BlockSpec(memory_space=pltpu.VMEM),
        cost_estimate=pl.CostEstimate(
            flops=2 * 24 * 24 * cells, transcendentals=0, bytes_accessed=28 * cells
        ),
    )(matrix, widened, stiffness)
    return summed[:, :span_cells]


def whole_partition(block):
    lead = block.shape[:-3]
    count = len(lead)
    every = lax.all_gather(block, "gy", axis=count + 1, tiled=True)
    return lax.all_gather(every, "gx", axis=count, tiled=True)


def own_part(whole, rows, cols):
    start = (0, lax.axis_index("gx") * rows, lax.axis_index("gy") * cols, 0)
    return lax.dynamic_slice(whole, start, (whole.shape[0], rows, cols, whole.shape[3]))


def solve_structure(right_side, operator, products):
    residual = right_side
    image_vec = operator(residual)
    norm_now, curvature = products(residual, image_vec)
    step_size = norm_now / curvature
    direction, image_dir = (residual, image_vec)
    solution = jnp.zeros_like(right_side)
    for iteration in range(ITERS):
        solution = solution + step_size * direction
        residual = residual - step_size * image_dir
        if iteration + 1 < ITERS:
            image_vec = operator(residual)
            norm_next, curvature = products(residual, image_vec)
            beta_ratio = norm_next / norm_now
            step_size = norm_next / (curvature - beta_ratio * norm_next / step_size)
            direction = residual + beta_ratio * direction
            image_dir = image_vec + beta_ratio * image_dir
            norm_now = norm_next
    return solution


def per_device(
    populations,
    solid_mask,
    wall_cells,
    body_load,
    elem_scale,
    elem_active,
    elem_matrix,
    iface_nodes,
    iface_coords,
    neighbours,
):
    group_count = lax.axis_size("group")
    span_devices = lax.axis_size("gx")
    struct_groups = max(1, group_count // 8)
    fluid_groups = group_count - struct_groups
    group_index = lax.axis_index("group")
    slab_index = group_index * span_devices + lax.axis_index("gx")
    column_index = lax.axis_index("gy")
    is_fluid = group_index < fluid_groups
    is_struct = jnp.logical_not(is_fluid)
    span_cells, across_cells, deep_cells = solid_mask.shape
    cell_count = span_cells * across_cells * deep_cells
    fluid_here = jnp.where(is_fluid, 1.0 - solid_mask.astype(jnp.float32), 0.0)
    relaxed_pops = jnp.where(
        is_fluid, collide(populations.astype(jnp.float32)), 0.0
    ).astype(jnp.bfloat16)
    marker = fluid_here.astype(jnp.bfloat16)[None]
    widened = halo_exchange(
        jnp.concatenate([relaxed_pops, marker], axis=0), fluid_groups * span_devices
    )
    widened = jnp.pad(widened, ((0, 0), (0, 0), (0, 0), (1, 1))).astype(jnp.float32)
    moved = widened[0:19]
    fluid_ext = widened[19]
    wall_index = wall_cells.reshape(-1)
    point_count = wall_index.shape[0]
    tiles_out = point_count // TILE

    def fluid_pack(operands):
        upstream, opened, bounce, reflected = stream_links(operands[0], operands[1])
        force_parts = wall_force(bounce, reflected).reshape(3, cell_count)
        picked = force_parts[:, wall_index]
        span_pos = wall_index // (across_cells * deep_cells)
        across_pos = wall_index // deep_cells % across_cells + column_index * across_cells
        deep_pos = wall_index % deep_cells
        positions = jnp.stack(
            [
                (slab_index * span_cells + span_pos).astype(jnp.float32),
                across_pos.astype(jnp.float32),
                deep_pos.astype(jnp.float32),
            ]
        )
        packed = jnp.concatenate([picked, positions], axis=0)
        return packed.reshape(6, tiles_out, TILE).transpose(1, 0, 2)

    packed = lax.cond(
        is_fluid,
        fluid_pack,
        lambda operands: jnp.zeros((tiles_out, 6, TILE), jnp.float32),
        (moved, fluid_ext),
    )
    received = lax.all_gather(packed, "group", axis=0, tiled=True)
    node_index = iface_nodes.reshape(-1)
    node_positions = iface_coords.reshape(3, -1)
    tile_lists = neighbours.reshape(neighbours.shape[2], neighbours.shape[3])
    nodes_total = body_load.shape[1] * body_load.shape[2] * body_load.shape[3]
    weight_shape = (tile_lists.shape[0], TILE, tile_lists.shape[1], TILE)

    stiffness = elem_scale * elem_active.astype(jnp.float32)

    def struct_map(operands):
        received_all, flat = operands
        weights, chosen = basis_weights(received_all, node_positions, tile_lists)
        return (weights, map_tractions(weights, chosen, node_index, flat))

    def struct_quiet(operands):
        return (jnp.zeros(weight_shape, jnp.float32), operands[1])

    weights, right_side = lax.cond(
        is_struct, struct_map, struct_quiet, (received, body_load.reshape(3, nodes_total))
    )
    right_side = right_side.reshape(body_load.shape)
    joined = whole_partition(jnp.concatenate([right_side, stiffness[None]], axis=0))
    whole_side = joined[0:3]
    stiffness = joined[3]
    rows, cols = body_load.shape[1], body_load.shape[2]

    def partition_products(first_vec, second_vec):
        pair = (jnp.sum(first_vec * first_vec), jnp.sum(first_vec * second_vec))
        if struct_groups > 1:
            pair = lax.psum(tuple(jnp.where(is_struct, x, 0.0) for x in pair), "group")
        return pair

    def partition_solve(operands):
        side, stiff, matrix = operands
        return solve_structure(
            side, lambda values: partition_operator(values, stiff, matrix), partition_products
        )

    if struct_groups > 1:
        whole_solution = partition_solve((whole_side, stiffness, elem_matrix))
    else:
        whole_solution = lax.cond(
            is_struct,
            lambda operands: partition_solve_kernel(*operands),
            lambda operands: jnp.zeros_like(operands[0][0:3]),
            (joined, elem_matrix),
        )
    solution = jnp.where(is_struct, own_part(whole_solution, rows, cols), 0.0)
    tile_slots = received.shape[0]

    def struct_back(operands):
        return map_speeds(
            operands[0], operands[1], node_index, tile_lists, tile_slots
        )

    back_terms = lax.cond(
        is_struct,
        struct_back,
        lambda operands: jnp.zeros((tile_slots, 3, TILE), jnp.float32),
        (weights, solution),
    )
    per_group = tile_slots // group_count
    route_count = fluid_groups // struct_groups
    sender_slot = jnp.clip(group_index - fluid_groups, 0, struct_groups - 1)
    own_speeds = jnp.zeros((per_group, 3, TILE), jnp.float32)
    for route_step in range(route_count):
        offset_row = (sender_slot + route_step * struct_groups) * per_group
        outgoing = lax.dynamic_slice_in_dim(back_terms, offset_row, per_group, 0)
        incoming = passed_along(outgoing, "group", (route_step + 1) * struct_groups)
        own_speeds = own_speeds + jnp.where(
            group_index // struct_groups == route_step, incoming, 0.0
        )
    speed_parts = wall_gain * own_speeds.transpose(1, 0, 2).reshape(3, point_count)
    wall_speed = jnp.zeros((3, cell_count), jnp.float32).at[:, wall_index].add(speed_parts)
    wall_speed = wall_speed.reshape(3, span_cells, across_cells, deep_cells)
    new_populations = lax.cond(
        is_fluid,
        lambda operands: stream_all(operands[0], operands[1], operands[2]),
        lambda operands: jnp.zeros(operands[0][:, 1:-1, 1:-1, 1:-1].shape, jnp.bfloat16),
        (moved, fluid_ext, wall_speed),
    )
    return (new_populations, solution)


def solution(mesh):
    placed = (
        P(None, ("group", "gx"), "gy", None),
        P(("group", "gx"), "gy", None),
        P(("group", "gx"), "gy", None),
        P(None, ("group", "gx"), "gy", None),
        P(("group", "gx"), "gy", None),
        P(("group", "gx"), "gy", None),
        P(),
        P(("group", "gx"), "gy", None),
        P(None, ("group", "gx"), "gy", None),
        P(("group", "gx"), "gy", None, None),
    )
    return jax.shard_map(
        per_device,
        mesh=mesh,
        in_specs=placed,
        out_specs=(P(None, ("group", "gx"), "gy", None), P(None, ("group", "gx"), "gy", None)),
        check_vma=False,
    )
```

```python
import jax
import jax.numpy as jnp
import numpy as np
from jax import lax
from jax.sharding import PartitionSpec as P
from jax.experimental import pallas as pl
from jax.experimental.pallas import tpu as pltpu

TILE = 128
ITERS = 3


velocity = [
    (0, 0, 0),
    (1, 0, 0),
    (-1, 0, 0),
    (0, 1, 0),
    (0, -1, 0),
    (0, 0, 1),
    (0, 0, -1),
    (1, 1, 0),
    (-1, -1, 0),
    (1, -1, 0),
    (-1, 1, 0),
    (1, 0, 1),
    (-1, 0, -1),
    (1, 0, -1),
    (-1, 0, 1),
    (0, 1, 1),
    (0, -1, -1),
    (0, 1, -1),
    (0, -1, 1),
]
opposite = [0, 2, 1, 4, 3, 6, 5, 8, 7, 10, 9, 12, 11, 14, 13, 16, 15, 18, 17]
lattice_weight = [1.0 / 3.0] + [1.0 / 18.0] * 6 + [1.0 / 36.0] * 12
relax_rate = 1.0 / 0.6
wall_gain = 60.0
basis_radius = 24.0
mass_shift = 0.5


def halo_exchange(cells, span_devices):
    columns = lax.axis_size("gy")
    axes = ("group", "gx", "gy")

    def shifted(piece, dr, dc):
        pairs = [
            (r * columns + c, (r + dr) * columns + c + dc)
            for r in range(span_devices)
            for c in range(columns)
            if 0 <= r + dr < span_devices and 0 <= c + dc < columns
        ]
        return lax.ppermute(piece, axes, pairs)

    cols = cells.shape[2]
    column = lax.axis_index("gy")
    edges = jnp.concatenate([cells[:, :, :1], cells[:, :, cols - 1 :]], axis=2)
    every = lax.all_gather(edges, "gy", axis=0)
    from_left = lax.dynamic_index_in_dim(every, jnp.maximum(column - 1, 0), 0, False)
    from_right = lax.dynamic_index_in_dim(every, jnp.minimum(column + 1, columns - 1), 0, False)
    cells = jnp.concatenate(
        [
            jnp.where(column > 0, from_left[:, :, 1:], 0.0).astype(cells.dtype),
            cells,
            jnp.where(column < columns - 1, from_right[:, :, :1], 0.0).astype(cells.dtype),
        ],
        axis=2,
    )
    rows = cells.shape[1]
    return jnp.concatenate(
        [shifted(cells[:, rows - 1 :], 1, 0), cells, shifted(cells[:, :1], -1, 0)], axis=1
    )


def passed_along(value, axis, steps):
    count = lax.axis_size(axis)
    pairs = [(source, (source + steps) % count) for source in range(count)]
    return lax.ppermute(value, axis, pairs)


def project_onto(vectors, direction):
    summed = jnp.zeros_like(vectors[0])
    for component in range(3):
        if direction[component] != 0:
            summed = summed + float(direction[component]) * vectors[component]
    return summed


def per_direction(values):
    return jnp.asarray(np.array(values, np.float32).reshape(19, 1, 1, 1))


def collide(population):
    density = jnp.sum(population, axis=0)
    velocity_parts = [
        jnp.sum(per_direction([c[component] for c in velocity]) * population, axis=0) / density
        for component in range(3)
    ]
    speed_square = (
        velocity_parts[0] * velocity_parts[0]
        + velocity_parts[1] * velocity_parts[1]
        + velocity_parts[2] * velocity_parts[2]
    )
    project = project_all(velocity_parts)
    balance = (
        per_direction(lattice_weight)
        * density
        * (1.0 + 3.0 * project + 4.5 * project * project - 1.5 * speed_square)
    )
    return population + relax_rate * (balance - population)


def project_all(vectors):
    summed = per_direction([c[0] for c in velocity]) * vectors[0]
    for component in (1, 2):
        summed = summed + per_direction([c[component] for c in velocity]) * vectors[component]
    return summed


def upstream_of(values, inner):
    for axis in range(3):
        shift = per_direction([c[axis] for c in velocity])
        pick = {
            s: lax.slice_in_dim(values, 1 - s, 1 - s + inner[axis], axis=axis + 1)
            for s in (-1, 0, 1)
        }
        values = jnp.where(shift > 0.5, pick[1], jnp.where(shift < -0.5, pick[-1], pick[0]))
    return values


def stream_links(moved, fluid_ext):
    inner = tuple(size - 2 for size in fluid_ext.shape)
    upstream = upstream_of(moved, inner)
    opened = upstream_of(jnp.broadcast_to(fluid_ext[None], (19,) + fluid_ext.shape), inner)
    bounce = 1.0 - opened
    centre = moved[:, 1 : inner[0] + 1, 1 : inner[1] + 1, 1 : inner[2] + 1]
    paired = centre[1:].reshape((9, 2) + inner)[:, ::-1].reshape((18,) + inner)
    reflected = jnp.concatenate([centre[0:1], paired], axis=0)
    return (upstream, opened, bounce, reflected)


def wall_force(bounce, reflected):
    carried = bounce * reflected
    return jnp.stack(
        [
            jnp.sum(per_direction([-2.0 * c[component] for c in velocity]) * carried, axis=0)
            for component in range(3)
        ]
    )


def stream_all(moved, fluid_ext, wall_speed):
    upstream, opened, bounce, reflected = stream_links(moved, fluid_ext)
    inside = fluid_ext[1:-1, 1:-1, 1:-1]
    speed_list = [wall_speed[0], wall_speed[1], wall_speed[2]]
    correction = per_direction([6.0 * w for w in lattice_weight]) * project_all(speed_list)
    result = inside * (opened * upstream + bounce * (reflected + correction))
    return result.astype(jnp.bfloat16)


def slot_table(tile_lists, tile_slots):
    slots = lax.broadcasted_iota(jnp.int32, (tile_slots, tile_lists.size), 0)
    return (slots == tile_lists.reshape(1, -1)).astype(jnp.float32)


def basis_weights(received, node_positions, tile_lists):
    tile_count = tile_lists.shape[0]
    tile_width = received.shape[2]
    chosen = received[tile_lists]
    nodes_at = node_positions.reshape(3, tile_count, tile_width)
    distance = jnp.zeros((tile_count, tile_width, tile_lists.shape[1], tile_width), jnp.float32)
    for component in range(3):
        offset = nodes_at[component][:, :, None, None] - chosen[:, None, :, 3 + component, :]
        distance = distance + offset * offset
    kernel = 1.0 / jnp.sqrt(1.0 + distance / (basis_radius * basis_radius))
    column = jnp.sum(kernel, axis=1).reshape(-1, tile_width)
    table = slot_table(tile_lists, received.shape[0])
    exact = lax.Precision.HIGHEST
    totals = jnp.einsum("tk,kp->tp", table, column, precision=exact)
    listed = jnp.einsum("tk,tp->kp", table, totals, precision=exact)
    listed = listed.reshape(tile_count, tile_lists.shape[1], tile_width)
    return (kernel / listed[:, None, :, :], chosen)


def map_tractions(weights, chosen, node_index, base):
    mapped = jnp.einsum(
        "anbp,abcp->can", weights, chosen[:, :, 0:3, :], precision=lax.Precision.HIGHEST
    )
    return base.at[:, node_index].add(mapped.reshape(3, -1))


def map_speeds(weights, solution_block, node_index, tile_lists, tile_slots):
    tile_count = weights.shape[0]
    tile_width = weights.shape[1]
    flat = solution_block.reshape(3, -1)
    at_nodes = flat[:, node_index].reshape(3, tile_count, tile_width)
    contrib = jnp.einsum("anbp,can->abcp", weights, at_nodes, precision=lax.Precision.HIGHEST)
    return jnp.einsum(
        "tk,kcp->tcp",
        slot_table(tile_lists, tile_slots),
        contrib.reshape(-1, 3, tile_width),
        precision=lax.Precision.HIGHEST,
    )


def apply_rows(matrix_ref, values_ref, stiff_ref, out_ref):
    span_cells, across_cells, deep_cells = stiff_ref.shape
    step = next(size for size in (16, 8, 4, 2, 1) if span_cells % size == 0)
    shape = (step, across_cells, deep_cells)
    across_at = lax.broadcasted_iota(jnp.int32, shape, 1)
    deep_at = lax.broadcasted_iota(jnp.int32, shape, 2)
    corners = [(a, b, c) for a in (0, 1) for b in (0, 1) for c in (0, 1)]
    for component in range(3):
        out_ref[component, 0:span_cells] = mass_shift * values_ref[component, 0:span_cells]
        out_ref[component, span_cells] = jnp.zeros((across_cells, deep_cells), jnp.float32)

    def ahead(value, across, deep):
        if across:
            value = jnp.where(
                across_at < across_cells - 1, pltpu.roll(value, across_cells - 1, 1), 0.0
            )
        if deep:
            value = jnp.where(deep_at < deep_cells - 1, pltpu.roll(value, deep_cells - 1, 2), 0.0)
        return value

    def behind(value, across, deep):
        if across:
            value = jnp.where(across_at >= 1, pltpu.roll(value, 1, 1), 0.0)
        if deep:
            value = jnp.where(deep_at >= 1, pltpu.roll(value, 1, 2), 0.0)
        return value

    def element_rows(block, carry):
        row = block * step
        gathered = []
        for a, b, c in corners:
            for component in range(3):
                gathered.append(ahead(values_ref[component, pl.ds(row + a, step)], b, c))
        scale = stiff_ref[pl.ds(row, step)]
        for corner_id, (a, b, c) in enumerate(corners):
            for component in range(3):
                line = 3 * corner_id + component
                force = matrix_ref[line, 0] * gathered[0]
                for other in range(1, 24):
                    force = force + matrix_ref[line, other] * gathered[other]
                out_ref[component, pl.ds(row + a, step)] += behind(scale * force, b, c)
        return carry

    lax.fori_loop(0, span_cells // step, element_rows, 0)


def operator_kernel(matrix_ref, values_ref, stiff_ref, out_ref):
    apply_rows(matrix_ref, values_ref, stiff_ref, out_ref)


def whole_sum(value):
    value = jnp.sum(value, axis=(0, 1))
    value = jnp.sum(value, axis=0, keepdims=True)
    return jnp.sum(value, axis=1, keepdims=True)


def solve_kernel(matrix_ref, joined_ref, out_ref, ahead_ref, image_ref, dir_ref, img_ref):
    stiff_ref = joined_ref.at[3]
    span_cells = stiff_ref.shape[0]
    residual = joined_ref[0:3]
    ahead_ref[:, 0:span_cells] = residual
    ahead_ref[:, span_cells : span_cells + 1] = jnp.zeros_like(residual[:, 0:1])
    apply_rows(matrix_ref, ahead_ref, stiff_ref, image_ref)
    image_vec = image_ref[:, 0:span_cells]
    norm_now = whole_sum(residual * residual)
    step_size = norm_now / whole_sum(residual * image_vec)
    dir_ref[...] = residual
    img_ref[...] = image_vec
    out_ref[...] = jnp.zeros_like(residual)
    for iteration in range(ITERS):
        out_ref[...] = out_ref[...] + step_size * dir_ref[...]
        residual = residual - step_size * img_ref[...]
        if iteration + 1 < ITERS:
            ahead_ref[:, 0:span_cells] = residual
            apply_rows(matrix_ref, ahead_ref, stiff_ref, image_ref)
            image_vec = image_ref[:, 0:span_cells]
            norm_next = whole_sum(residual * residual)
            curvature = whole_sum(residual * image_vec)
            beta_ratio = norm_next / norm_now
            step_size = norm_next / (curvature - beta_ratio * norm_next / step_size)
            dir_ref[...] = residual + beta_ratio * dir_ref[...]
            img_ref[...] = image_vec + beta_ratio * img_ref[...]
            norm_now = norm_next


def partition_solve_kernel(joined, matrix):
    span_cells, across_cells, deep_cells = joined.shape[1:]
    cells = span_cells * across_cells * deep_cells
    wide = (3, span_cells + 1, across_cells, deep_cells)
    side = (3, span_cells, across_cells, deep_cells)
    return pl.pallas_call(
        solve_kernel,
        out_shape=jax.ShapeDtypeStruct(side, jnp.float32),
        in_specs=[
            pl.BlockSpec(memory_space=pltpu.SMEM),
            pl.BlockSpec(memory_space=pltpu.VMEM),
        ],
        out_specs=pl.BlockSpec(memory_space=pltpu.VMEM),
        scratch_shapes=[
            pltpu.VMEM(wide, jnp.float32),
            pltpu.VMEM(wide, jnp.float32),
            pltpu.VMEM(side, jnp.float32),
            pltpu.VMEM(side, jnp.float32),
        ],
        cost_estimate=pl.CostEstimate(
            flops=ITERS * 2 * 24 * 24 * cells, transcendentals=0, bytes_accessed=28 * cells
        ),
    )(matrix, joined)


def partition_operator(values, stiffness, matrix):
    span_cells, across_cells, deep_cells = stiffness.shape
    widened = jnp.pad(values, ((0, 0), (0, 1), (0, 0), (0, 0)))
    cells = span_cells * across_cells * deep_cells
    summed = pl.pallas_call(
        operator_kernel,
        out_shape=jax.ShapeDtypeStruct(widened.shape, jnp.float32),
        in_specs=[
            pl.BlockSpec(memory_space=pltpu.SMEM),
            pl.BlockSpec(memory_space=pltpu.VMEM),
            pl.BlockSpec(memory_space=pltpu.VMEM),
        ],
        out_specs=pl.BlockSpec(memory_space=pltpu.VMEM),
        cost_estimate=pl.CostEstimate(
            flops=2 * 24 * 24 * cells, transcendentals=0, bytes_accessed=28 * cells
        ),
    )(matrix, widened, stiffness)
    return summed[:, :span_cells]


def whole_partition(block):
    lead = block.shape[:-3]
    count = len(lead)
    every = lax.all_gather(block, "gx", axis=count, tiled=True)
    return lax.all_gather(every, "gy", axis=count + 1, tiled=True)


def own_part(whole, rows, cols):
    start = (0, lax.axis_index("gx") * rows, lax.axis_index("gy") * cols, 0)
    return lax.dynamic_slice(whole, start, (whole.shape[0], rows, cols, whole.shape[3]))


def solve_structure(right_side, operator, products):
    residual = right_side
    image_vec = operator(residual)
    norm_now, curvature = products(residual, image_vec)
    step_size = norm_now / curvature
    direction, image_dir = (residual, image_vec)
    solution = jnp.zeros_like(right_side)
    for iteration in range(ITERS):
        solution = solution + step_size * direction
        residual = residual - step_size * image_dir
        if iteration + 1 < ITERS:
            image_vec = operator(residual)
            norm_next, curvature = products(residual, image_vec)
            beta_ratio = norm_next / norm_now
            step_size = norm_next / (curvature - beta_ratio * norm_next / step_size)
            direction = residual + beta_ratio * direction
            image_dir = image_vec + beta_ratio * image_dir
            norm_now = norm_next
    return solution


def per_device(
    populations,
    solid_mask,
    wall_cells,
    body_load,
    elem_scale,
    elem_active,
    elem_matrix,
    iface_nodes,
    iface_coords,
    neighbours,
):
    group_count = lax.axis_size("group")
    span_devices = lax.axis_size("gx")
    struct_groups = max(1, group_count // 8)
    fluid_groups = group_count - struct_groups
    group_index = lax.axis_index("group")
    slab_index = group_index * span_devices + lax.axis_index("gx")
    column_index = lax.axis_index("gy")
    is_fluid = group_index < fluid_groups
    is_struct = jnp.logical_not(is_fluid)
    span_cells, across_cells, deep_cells = solid_mask.shape
    cell_count = span_cells * across_cells * deep_cells
    fluid_here = jnp.where(is_fluid, 1.0 - solid_mask.astype(jnp.float32), 0.0)
    relaxed_pops = jnp.where(
        is_fluid, collide(populations.astype(jnp.float32)), 0.0
    ).astype(jnp.bfloat16)
    marker = fluid_here.astype(jnp.bfloat16)[None]
    widened = halo_exchange(
        jnp.concatenate([relaxed_pops, marker], axis=0), fluid_groups * span_devices
    )
    widened = jnp.pad(widened, ((0, 0), (0, 0), (0, 0), (1, 1))).astype(jnp.float32)
    moved = widened[0:19]
    fluid_ext = widened[19]
    wall_index = wall_cells.reshape(-1)
    point_count = wall_index.shape[0]
    tiles_out = point_count // TILE

    def fluid_pack(operands):
        upstream, opened, bounce, reflected = stream_links(operands[0], operands[1])
        force_parts = wall_force(bounce, reflected).reshape(3, cell_count)
        picked = force_parts[:, wall_index]
        span_pos = wall_index // (across_cells * deep_cells)
        across_pos = wall_index // deep_cells % across_cells + column_index * across_cells
        deep_pos = wall_index % deep_cells
        positions = jnp.stack(
            [
                (slab_index * span_cells + span_pos).astype(jnp.float32),
                across_pos.astype(jnp.float32),
                deep_pos.astype(jnp.float32),
            ]
        )
        packed = jnp.concatenate([picked, positions], axis=0)
        return packed.reshape(6, tiles_out, TILE).transpose(1, 0, 2)

    packed = lax.cond(
        is_fluid,
        fluid_pack,
        lambda operands: jnp.zeros((tiles_out, 6, TILE), jnp.float32),
        (moved, fluid_ext),
    )
    received = lax.all_gather(packed, "group", axis=0, tiled=True)
    node_index = iface_nodes.reshape(-1)
    node_positions = iface_coords.reshape(3, -1)
    tile_lists = neighbours.reshape(neighbours.shape[2], neighbours.shape[3])
    nodes_total = body_load.shape[1] * body_load.shape[2] * body_load.shape[3]
    weight_shape = (tile_lists.shape[0], TILE, tile_lists.shape[1], TILE)

    stiffness = elem_scale * elem_active.astype(jnp.float32)

    def struct_map(operands):
        received_all, flat = operands
        weights, chosen = basis_weights(received_all, node_positions, tile_lists)
        return (weights, map_tractions(weights, chosen, node_index, flat))

    def struct_quiet(operands):
        return (jnp.zeros(weight_shape, jnp.float32), operands[1])

    weights, right_side = lax.cond(
        is_struct, struct_map, struct_quiet, (received, body_load.reshape(3, nodes_total))
    )
    right_side = right_side.reshape(body_load.shape)
    joined = whole_partition(jnp.concatenate([right_side, stiffness[None]], axis=0))
    whole_side = joined[0:3]
    stiffness = joined[3]
    rows, cols = body_load.shape[1], body_load.shape[2]

    def partition_products(first_vec, second_vec):
        pair = (jnp.sum(first_vec * first_vec), jnp.sum(first_vec * second_vec))
        if struct_groups > 1:
            pair = lax.psum(tuple(jnp.where(is_struct, x, 0.0) for x in pair), "group")
        return pair

    def partition_solve(operands):
        side, stiff, matrix = operands
        return solve_structure(
            side, lambda values: partition_operator(values, stiff, matrix), partition_products
        )

    if struct_groups > 1:
        whole_solution = partition_solve((whole_side, stiffness, elem_matrix))
    else:
        whole_solution = lax.cond(
            is_struct,
            lambda operands: partition_solve_kernel(*operands),
            lambda operands: jnp.zeros_like(operands[0][0:3]),
            (joined, elem_matrix),
        )
    solution = jnp.where(is_struct, own_part(whole_solution, rows, cols), 0.0)
    tile_slots = received.shape[0]

    def struct_back(operands):
        return map_speeds(
            operands[0], operands[1], node_index, tile_lists, tile_slots
        )

    back_terms = lax.cond(
        is_struct,
        struct_back,
        lambda operands: jnp.zeros((tile_slots, 3, TILE), jnp.float32),
        (weights, solution),
    )
    per_group = tile_slots // group_count
    route_count = fluid_groups // struct_groups
    sender_slot = jnp.clip(group_index - fluid_groups, 0, struct_groups - 1)
    own_speeds = jnp.zeros((per_group, 3, TILE), jnp.float32)
    for route_step in range(route_count):
        offset_row = (sender_slot + route_step * struct_groups) * per_group
        outgoing = lax.dynamic_slice_in_dim(back_terms, offset_row, per_group, 0)
        incoming = passed_along(outgoing, "group", (route_step + 1) * struct_groups)
        own_speeds = own_speeds + jnp.where(
            group_index // struct_groups == route_step, incoming, 0.0
        )
    speed_parts = wall_gain * own_speeds.transpose(1, 0, 2).reshape(3, point_count)
    wall_speed = jnp.zeros((3, cell_count), jnp.float32).at[:, wall_index].add(speed_parts)
    wall_speed = wall_speed.reshape(3, span_cells, across_cells, deep_cells)
    new_populations = lax.cond(
        is_fluid,
        lambda operands: stream_all(operands[0], operands[1], operands[2]),
        lambda operands: jnp.zeros(operands[0][:, 1:-1, 1:-1, 1:-1].shape, jnp.bfloat16),
        (moved, fluid_ext, wall_speed),
    )
    return (new_populations, solution)


def solution(mesh):
    placed = (
        P(None, ("group", "gx"), "gy", None),
        P(("group", "gx"), "gy", None),
        P(("group", "gx"), "gy", None),
        P(None, ("group", "gx"), "gy", None),
        P(("group", "gx"), "gy", None),
        P(("group", "gx"), "gy", None),
        P(),
        P(("group", "gx"), "gy", None),
        P(None, ("group", "gx"), "gy", None),
        P(("group", "gx"), "gy", None, None),
    )
    return jax.shard_map(
        per_device,
        mesh=mesh,
        in_specs=placed,
        out_specs=(P(None, ("group", "gx"), "gy", None), P(None, ("group", "gx"), "gy", None)),
        check_vma=False,
    )
```

```python
import jax
import jax.numpy as jnp
import numpy as np
from jax import lax
from jax.sharding import PartitionSpec as P
from jax.experimental import pallas as pl
from jax.experimental.pallas import tpu as pltpu

TILE = 128
ITERS = 3


velocity = [
    (0, 0, 0),
    (1, 0, 0),
    (-1, 0, 0),
    (0, 1, 0),
    (0, -1, 0),
    (0, 0, 1),
    (0, 0, -1),
    (1, 1, 0),
    (-1, -1, 0),
    (1, -1, 0),
    (-1, 1, 0),
    (1, 0, 1),
    (-1, 0, -1),
    (1, 0, -1),
    (-1, 0, 1),
    (0, 1, 1),
    (0, -1, -1),
    (0, 1, -1),
    (0, -1, 1),
]
opposite = [0, 2, 1, 4, 3, 6, 5, 8, 7, 10, 9, 12, 11, 14, 13, 16, 15, 18, 17]
lattice_weight = [1.0 / 3.0] + [1.0 / 18.0] * 6 + [1.0 / 36.0] * 12
relax_rate = 1.0 / 0.6
wall_gain = 60.0
basis_radius = 24.0
mass_shift = 0.5


def halo_exchange(cells, span_devices):
    columns = lax.axis_size("gy")
    axes = ("group", "gx", "gy")

    def shifted(piece, dr, dc):
        pairs = [
            (r * columns + c, (r + dr) * columns + c + dc)
            for r in range(span_devices)
            for c in range(columns)
            if 0 <= r + dr < span_devices and 0 <= c + dc < columns
        ]
        return lax.ppermute(piece, axes, pairs)

    cols = cells.shape[2]
    column = lax.axis_index("gy")
    edges = jnp.concatenate([cells[:, :, :1], cells[:, :, cols - 1 :]], axis=2)
    every = lax.all_gather(edges, "gy", axis=0)
    from_left = lax.dynamic_index_in_dim(every, jnp.maximum(column - 1, 0), 0, False)
    from_right = lax.dynamic_index_in_dim(every, jnp.minimum(column + 1, columns - 1), 0, False)
    cells = jnp.concatenate(
        [
            jnp.where(column > 0, from_left[:, :, 1:], 0.0).astype(cells.dtype),
            cells,
            jnp.where(column < columns - 1, from_right[:, :, :1], 0.0).astype(cells.dtype),
        ],
        axis=2,
    )
    rows = cells.shape[1]
    return jnp.concatenate(
        [shifted(cells[:, rows - 1 :], 1, 0), cells, shifted(cells[:, :1], -1, 0)], axis=1
    )


def passed_along(value, axis, steps):
    count = lax.axis_size(axis)
    pairs = [(source, (source + steps) % count) for source in range(count)]
    return lax.ppermute(value, axis, pairs)


def project_onto(vectors, direction):
    summed = jnp.zeros_like(vectors[0])
    for component in range(3):
        if direction[component] != 0:
            summed = summed + float(direction[component]) * vectors[component]
    return summed


def per_direction(values):
    return jnp.asarray(np.array(values, np.float32).reshape(19, 1, 1, 1))


def collide(population):
    density = jnp.sum(population, axis=0)
    velocity_parts = [
        jnp.sum(per_direction([c[component] for c in velocity]) * population, axis=0) / density
        for component in range(3)
    ]
    speed_square = (
        velocity_parts[0] * velocity_parts[0]
        + velocity_parts[1] * velocity_parts[1]
        + velocity_parts[2] * velocity_parts[2]
    )
    project = project_all(velocity_parts)
    balance = (
        per_direction(lattice_weight)
        * density
        * (1.0 + 3.0 * project + 4.5 * project * project - 1.5 * speed_square)
    )
    return population + relax_rate * (balance - population)


def project_all(vectors):
    summed = per_direction([c[0] for c in velocity]) * vectors[0]
    for component in (1, 2):
        summed = summed + per_direction([c[component] for c in velocity]) * vectors[component]
    return summed


def upstream_of(values, inner):
    for axis in range(3):
        shift = per_direction([c[axis] for c in velocity])
        pick = {
            s: lax.slice_in_dim(values, 1 - s, 1 - s + inner[axis], axis=axis + 1)
            for s in (-1, 0, 1)
        }
        values = jnp.where(shift > 0.5, pick[1], jnp.where(shift < -0.5, pick[-1], pick[0]))
    return values


def stream_links(moved, fluid_ext):
    inner = tuple(size - 2 for size in fluid_ext.shape)
    upstream = upstream_of(moved, inner)
    opened = upstream_of(jnp.broadcast_to(fluid_ext[None], (19,) + fluid_ext.shape), inner)
    bounce = 1.0 - opened
    centre = moved[:, 1 : inner[0] + 1, 1 : inner[1] + 1, 1 : inner[2] + 1]
    paired = centre[1:].reshape((9, 2) + inner)[:, ::-1].reshape((18,) + inner)
    reflected = jnp.concatenate([centre[0:1], paired], axis=0)
    return (upstream, opened, bounce, reflected)


def wall_force(bounce, reflected):
    carried = bounce * reflected
    return jnp.stack(
        [
            jnp.sum(per_direction([-2.0 * c[component] for c in velocity]) * carried, axis=0)
            for component in range(3)
        ]
    )


def stream_all(moved, fluid_ext, wall_speed):
    upstream, opened, bounce, reflected = stream_links(moved, fluid_ext)
    inside = fluid_ext[1:-1, 1:-1, 1:-1]
    speed_list = [wall_speed[0], wall_speed[1], wall_speed[2]]
    correction = per_direction([6.0 * w for w in lattice_weight]) * project_all(speed_list)
    result = inside * (opened * upstream + bounce * (reflected + correction))
    return result.astype(jnp.bfloat16)


def slot_table(tile_lists, tile_slots):
    slots = lax.broadcasted_iota(jnp.int32, (tile_slots, tile_lists.size), 0)
    return (slots == tile_lists.reshape(1, -1)).astype(jnp.float32)


def basis_weights(received, node_positions, tile_lists):
    tile_count = tile_lists.shape[0]
    tile_width = received.shape[2]
    chosen = received[tile_lists]
    nodes_at = node_positions.reshape(3, tile_count, tile_width)
    distance = jnp.zeros((tile_count, tile_width, tile_lists.shape[1], tile_width), jnp.float32)
    for component in range(3):
        offset = nodes_at[component][:, :, None, None] - chosen[:, None, :, 3 + component, :]
        distance = distance + offset * offset
    kernel = 1.0 / jnp.sqrt(1.0 + distance / (basis_radius * basis_radius))
    column = jnp.sum(kernel, axis=1).reshape(-1, tile_width)
    table = slot_table(tile_lists, received.shape[0])
    exact = lax.Precision.HIGHEST
    totals = jnp.einsum("tk,kp->tp", table, column, precision=exact)
    listed = jnp.einsum("tk,tp->kp", table, totals, precision=exact)
    listed = listed.reshape(tile_count, tile_lists.shape[1], tile_width)
    return (kernel / listed[:, None, :, :], chosen)


def map_tractions(weights, chosen, node_index, base):
    mapped = jnp.einsum(
        "anbp,abcp->can", weights, chosen[:, :, 0:3, :], precision=lax.Precision.HIGHEST
    )
    return base.at[:, node_index].add(mapped.reshape(3, -1))


def map_speeds(weights, solution_block, node_index, tile_lists, tile_slots):
    tile_count = weights.shape[0]
    tile_width = weights.shape[1]
    flat = solution_block.reshape(3, -1)
    at_nodes = flat[:, node_index].reshape(3, tile_count, tile_width)
    contrib = jnp.einsum("anbp,can->abcp", weights, at_nodes, precision=lax.Precision.HIGHEST)
    return jnp.einsum(
        "tk,kcp->tcp",
        slot_table(tile_lists, tile_slots),
        contrib.reshape(-1, 3, tile_width),
        precision=lax.Precision.HIGHEST,
    )


def apply_rows(matrix_ref, values_ref, stiff_ref, out_ref):
    span_cells, across_cells, deep_cells = stiff_ref.shape
    step = next(size for size in (16, 8, 4, 2, 1) if span_cells % size == 0)
    shape = (step, across_cells, deep_cells)
    across_at = lax.broadcasted_iota(jnp.int32, shape, 1)
    deep_at = lax.broadcasted_iota(jnp.int32, shape, 2)
    corners = [(a, b, c) for a in (0, 1) for b in (0, 1) for c in (0, 1)]
    for component in range(3):
        out_ref[component, 0:span_cells] = mass_shift * values_ref[component, 0:span_cells]
        out_ref[component, span_cells] = jnp.zeros((across_cells, deep_cells), jnp.float32)

    def ahead(value, across, deep):
        if across:
            value = jnp.where(
                across_at < across_cells - 1, pltpu.roll(value, across_cells - 1, 1), 0.0
            )
        if deep:
            value = jnp.where(deep_at < deep_cells - 1, pltpu.roll(value, deep_cells - 1, 2), 0.0)
        return value

    def behind(value, across, deep):
        if across:
            value = jnp.where(across_at >= 1, pltpu.roll(value, 1, 1), 0.0)
        if deep:
            value = jnp.where(deep_at >= 1, pltpu.roll(value, 1, 2), 0.0)
        return value

    def element_rows(block, carry):
        row = block * step
        gathered = []
        for a, b, c in corners:
            for component in range(3):
                gathered.append(ahead(values_ref[component, pl.ds(row + a, step)], b, c))
        scale = stiff_ref[pl.ds(row, step)]
        for corner_id, (a, b, c) in enumerate(corners):
            for component in range(3):
                line = 3 * corner_id + component
                force = matrix_ref[line, 0] * gathered[0]
                for other in range(1, 24):
                    force = force + matrix_ref[line, other] * gathered[other]
                out_ref[component, pl.ds(row + a, step)] += behind(scale * force, b, c)
        return carry

    lax.fori_loop(0, span_cells // step, element_rows, 0)


def operator_kernel(matrix_ref, values_ref, stiff_ref, out_ref):
    apply_rows(matrix_ref, values_ref, stiff_ref, out_ref)


def whole_sum(value):
    value = jnp.sum(value, axis=(0, 1))
    value = jnp.sum(value, axis=0, keepdims=True)
    return jnp.sum(value, axis=1, keepdims=True)


def solve_kernel(matrix_ref, joined_ref, out_ref, ahead_ref, image_ref, dir_ref, img_ref):
    stiff_ref = joined_ref.at[3]
    span_cells = stiff_ref.shape[0]
    residual = joined_ref[0:3]
    ahead_ref[:, 0:span_cells] = residual
    ahead_ref[:, span_cells : span_cells + 1] = jnp.zeros_like(residual[:, 0:1])
    apply_rows(matrix_ref, ahead_ref, stiff_ref, image_ref)
    image_vec = image_ref[:, 0:span_cells]
    norm_now = whole_sum(residual * residual)
    step_size = norm_now / whole_sum(residual * image_vec)
    dir_ref[...] = residual
    img_ref[...] = image_vec
    out_ref[...] = jnp.zeros_like(residual)
    for iteration in range(ITERS):
        out_ref[...] = out_ref[...] + step_size * dir_ref[...]
        residual = residual - step_size * img_ref[...]
        if iteration + 1 < ITERS:
            ahead_ref[:, 0:span_cells] = residual
            apply_rows(matrix_ref, ahead_ref, stiff_ref, image_ref)
            image_vec = image_ref[:, 0:span_cells]
            norm_next = whole_sum(residual * residual)
            curvature = whole_sum(residual * image_vec)
            beta_ratio = norm_next / norm_now
            step_size = norm_next / (curvature - beta_ratio * norm_next / step_size)
            dir_ref[...] = residual + beta_ratio * dir_ref[...]
            img_ref[...] = image_vec + beta_ratio * img_ref[...]
            norm_now = norm_next


def partition_solve_kernel(joined, matrix):
    span_cells, across_cells, deep_cells = joined.shape[1:]
    cells = span_cells * across_cells * deep_cells
    wide = (3, span_cells + 1, across_cells, deep_cells)
    side = (3, span_cells, across_cells, deep_cells)
    return pl.pallas_call(
        solve_kernel,
        out_shape=jax.ShapeDtypeStruct(side, jnp.float32),
        in_specs=[
            pl.BlockSpec(memory_space=pltpu.SMEM),
            pl.BlockSpec(memory_space=pltpu.VMEM),
        ],
        out_specs=pl.BlockSpec(memory_space=pltpu.VMEM),
        scratch_shapes=[
            pltpu.VMEM(wide, jnp.float32),
            pltpu.VMEM(wide, jnp.float32),
            pltpu.VMEM(side, jnp.float32),
            pltpu.VMEM(side, jnp.float32),
        ],
        cost_estimate=pl.CostEstimate(
            flops=ITERS * 2 * 24 * 24 * cells, transcendentals=0, bytes_accessed=28 * cells
        ),
    )(matrix, joined)


def partition_operator(values, stiffness, matrix):
    span_cells, across_cells, deep_cells = stiffness.shape
    widened = jnp.pad(values, ((0, 0), (0, 1), (0, 0), (0, 0)))
    cells = span_cells * across_cells * deep_cells
    summed = pl.pallas_call(
        operator_kernel,
        out_shape=jax.ShapeDtypeStruct(widened.shape, jnp.float32),
        in_specs=[
            pl.BlockSpec(memory_space=pltpu.SMEM),
            pl.BlockSpec(memory_space=pltpu.VMEM),
            pl.BlockSpec(memory_space=pltpu.VMEM),
        ],
        out_specs=pl.BlockSpec(memory_space=pltpu.VMEM),
        cost_estimate=pl.CostEstimate(
            flops=2 * 24 * 24 * cells, transcendentals=0, bytes_accessed=28 * cells
        ),
    )(matrix, widened, stiffness)
    return summed[:, :span_cells]


def whole_partition(block):
    lead = block.shape[:-3]
    count = len(lead)
    every = lax.all_gather(block, "gx", axis=count, tiled=True)
    return lax.all_gather(every, "gy", axis=count + 1, tiled=True)


def own_part(whole, rows, cols):
    start = (0, lax.axis_index("gx") * rows, lax.axis_index("gy") * cols, 0)
    return lax.dynamic_slice(whole, start, (whole.shape[0], rows, cols, whole.shape[3]))


def solve_structure(right_side, operator, products):
    residual = right_side
    image_vec = operator(residual)
    norm_now, curvature = products(residual, image_vec)
    step_size = norm_now / curvature
    direction, image_dir = (residual, image_vec)
    solution = jnp.zeros_like(right_side)
    for iteration in range(ITERS):
        solution = solution + step_size * direction
        residual = residual - step_size * image_dir
        if iteration + 1 < ITERS:
            image_vec = operator(residual)
            norm_next, curvature = products(residual, image_vec)
            beta_ratio = norm_next / norm_now
            step_size = norm_next / (curvature - beta_ratio * norm_next / step_size)
            direction = residual + beta_ratio * direction
            image_dir = image_vec + beta_ratio * image_dir
            norm_now = norm_next
    return solution


def per_device(
    populations,
    solid_mask,
    wall_cells,
    body_load,
    elem_scale,
    elem_active,
    elem_matrix,
    iface_nodes,
    iface_coords,
    neighbours,
):
    group_count = lax.axis_size("group")
    span_devices = lax.axis_size("gx")
    struct_groups = max(1, group_count // 8)
    fluid_groups = group_count - struct_groups
    group_index = lax.axis_index("group")
    slab_index = group_index * span_devices + lax.axis_index("gx")
    column_index = lax.axis_index("gy")
    is_fluid = group_index < fluid_groups
    is_struct = jnp.logical_not(is_fluid)
    span_cells, across_cells, deep_cells = solid_mask.shape
    cell_count = span_cells * across_cells * deep_cells
    fluid_here = jnp.where(is_fluid, 1.0 - solid_mask.astype(jnp.float32), 0.0)
    relaxed_pops = jnp.where(
        is_fluid, collide(populations.astype(jnp.float32)), 0.0
    ).astype(jnp.bfloat16)
    marker = fluid_here.astype(jnp.bfloat16)[None]
    widened = halo_exchange(
        jnp.concatenate([relaxed_pops, marker], axis=0), fluid_groups * span_devices
    )
    widened = jnp.pad(widened, ((0, 0), (0, 0), (0, 0), (1, 1))).astype(jnp.float32)
    moved = widened[0:19]
    fluid_ext = widened[19]
    wall_index = wall_cells.reshape(-1)
    point_count = wall_index.shape[0]
    tiles_out = point_count // TILE

    def fluid_pack(operands):
        upstream, opened, bounce, reflected = stream_links(operands[0], operands[1])
        force_parts = wall_force(bounce, reflected).reshape(3, cell_count)
        picked = force_parts[:, wall_index]
        span_pos = wall_index // (across_cells * deep_cells)
        across_pos = wall_index // deep_cells % across_cells + column_index * across_cells
        deep_pos = wall_index % deep_cells
        positions = jnp.stack(
            [
                (slab_index * span_cells + span_pos).astype(jnp.float32),
                across_pos.astype(jnp.float32),
                deep_pos.astype(jnp.float32),
            ]
        )
        packed = jnp.concatenate([picked, positions], axis=0)
        return packed.reshape(6, tiles_out, TILE).transpose(1, 0, 2)

    packed = lax.cond(
        is_fluid,
        fluid_pack,
        lambda operands: jnp.zeros((tiles_out, 6, TILE), jnp.float32),
        (moved, fluid_ext),
    )
    received = lax.all_gather(packed, "group", axis=0, tiled=True)
    node_index = iface_nodes.reshape(-1)
    node_positions = iface_coords.reshape(3, -1)
    tile_lists = neighbours.reshape(neighbours.shape[2], neighbours.shape[3])
    nodes_total = body_load.shape[1] * body_load.shape[2] * body_load.shape[3]
    weight_shape = (tile_lists.shape[0], TILE, tile_lists.shape[1], TILE)

    stiffness = elem_scale * elem_active.astype(jnp.float32)

    def struct_map(operands):
        received_all, flat = operands
        weights, chosen = basis_weights(received_all, node_positions, tile_lists)
        return (weights, map_tractions(weights, chosen, node_index, flat))

    def struct_quiet(operands):
        return (jnp.zeros(weight_shape, jnp.float32), operands[1])

    weights, right_side = lax.cond(
        is_struct, struct_map, struct_quiet, (received, body_load.reshape(3, nodes_total))
    )
    right_side = right_side.reshape(body_load.shape)
    joined = whole_partition(jnp.concatenate([right_side, stiffness[None]], axis=0))
    whole_side = joined[0:3]
    stiffness = joined[3]
    rows, cols = body_load.shape[1], body_load.shape[2]

    def partition_products(first_vec, second_vec):
        pair = (jnp.sum(first_vec * first_vec), jnp.sum(first_vec * second_vec))
        if struct_groups > 1:
            pair = lax.psum(tuple(jnp.where(is_struct, x, 0.0) for x in pair), "group")
        return pair

    def partition_solve(operands):
        side, stiff, matrix = operands
        return solve_structure(
            side, lambda values: partition_operator(values, stiff, matrix), partition_products
        )

    if struct_groups > 1:
        whole_solution = partition_solve((whole_side, stiffness, elem_matrix))
    else:
        whole_solution = lax.cond(
            is_struct,
            lambda operands: partition_solve_kernel(*operands),
            lambda operands: jnp.zeros_like(operands[0][0:3]),
            (joined, elem_matrix),
        )
    solution = own_part(whole_solution, rows, cols)
    if struct_groups > 1:
        solution = jnp.where(is_struct, solution, 0.0)
    tile_slots = received.shape[0]

    def struct_back(operands):
        return map_speeds(
            operands[0], operands[1], node_index, tile_lists, tile_slots
        )

    back_terms = lax.cond(
        is_struct,
        struct_back,
        lambda operands: jnp.zeros((tile_slots, 3, TILE), jnp.float32),
        (weights, solution),
    )
    per_group = tile_slots // group_count
    route_count = fluid_groups // struct_groups
    sender_slot = jnp.clip(group_index - fluid_groups, 0, struct_groups - 1)
    own_speeds = jnp.zeros((per_group, 3, TILE), jnp.float32)
    for route_step in range(route_count):
        offset_row = (sender_slot + route_step * struct_groups) * per_group
        outgoing = lax.dynamic_slice_in_dim(back_terms, offset_row, per_group, 0)
        incoming = passed_along(outgoing, "group", (route_step + 1) * struct_groups)
        own_speeds = own_speeds + jnp.where(
            group_index // struct_groups == route_step, incoming, 0.0
        )
    speed_parts = wall_gain * own_speeds.transpose(1, 0, 2).reshape(3, point_count)
    wall_speed = jnp.zeros((3, cell_count), jnp.float32).at[:, wall_index].add(speed_parts)
    wall_speed = wall_speed.reshape(3, span_cells, across_cells, deep_cells)
    new_populations = lax.cond(
        is_fluid,
        lambda operands: stream_all(operands[0], operands[1], operands[2]),
        lambda operands: jnp.zeros(operands[0][:, 1:-1, 1:-1, 1:-1].shape, jnp.bfloat16),
        (moved, fluid_ext, wall_speed),
    )
    return (new_populations, solution)


def solution(mesh):
    placed = (
        P(None, ("group", "gx"), "gy", None),
        P(("group", "gx"), "gy", None),
        P(("group", "gx"), "gy", None),
        P(None, ("group", "gx"), "gy", None),
        P(("group", "gx"), "gy", None),
        P(("group", "gx"), "gy", None),
        P(),
        P(("group", "gx"), "gy", None),
        P(None, ("group", "gx"), "gy", None),
        P(("group", "gx"), "gy", None, None),
    )
    return jax.shard_map(
        per_device,
        mesh=mesh,
        in_specs=placed,
        out_specs=(P(None, ("group", "gx"), "gy", None), P(None, ("group", "gx"), "gy", None)),
        check_vma=False,
    )
```

```python
import jax
import jax.numpy as jnp
import numpy as np
from jax import lax
from jax.sharding import PartitionSpec as P
from jax.experimental import pallas as pl
from jax.experimental.pallas import tpu as pltpu

TILE = 128
ITERS = 3


velocity = [
    (0, 0, 0),
    (1, 0, 0),
    (-1, 0, 0),
    (0, 1, 0),
    (0, -1, 0),
    (0, 0, 1),
    (0, 0, -1),
    (1, 1, 0),
    (-1, -1, 0),
    (1, -1, 0),
    (-1, 1, 0),
    (1, 0, 1),
    (-1, 0, -1),
    (1, 0, -1),
    (-1, 0, 1),
    (0, 1, 1),
    (0, -1, -1),
    (0, 1, -1),
    (0, -1, 1),
]
opposite = [0, 2, 1, 4, 3, 6, 5, 8, 7, 10, 9, 12, 11, 14, 13, 16, 15, 18, 17]
lattice_weight = [1.0 / 3.0] + [1.0 / 18.0] * 6 + [1.0 / 36.0] * 12
relax_rate = 1.0 / 0.6
wall_gain = 60.0
basis_radius = 24.0
mass_shift = 0.5


def halo_exchange(cells, span_devices):
    columns = lax.axis_size("gy")
    axes = ("group", "gx", "gy")

    def shifted(piece, dr, dc):
        pairs = [
            (r * columns + c, (r + dr) * columns + c + dc)
            for r in range(span_devices)
            for c in range(columns)
            if 0 <= r + dr < span_devices and 0 <= c + dc < columns
        ]
        return lax.ppermute(piece, axes, pairs)

    cols = cells.shape[2]
    column = lax.axis_index("gy")
    edges = jnp.concatenate([cells[:, :, :1], cells[:, :, cols - 1 :]], axis=2)
    every = lax.all_gather(edges, "gy", axis=0)
    from_left = lax.dynamic_index_in_dim(every, jnp.maximum(column - 1, 0), 0, False)
    from_right = lax.dynamic_index_in_dim(every, jnp.minimum(column + 1, columns - 1), 0, False)
    cells = jnp.concatenate(
        [
            jnp.where(column > 0, from_left[:, :, 1:], 0.0).astype(cells.dtype),
            cells,
            jnp.where(column < columns - 1, from_right[:, :, :1], 0.0).astype(cells.dtype),
        ],
        axis=2,
    )
    rows = cells.shape[1]
    return jnp.concatenate(
        [shifted(cells[:, rows - 1 :], 1, 0), cells, shifted(cells[:, :1], -1, 0)], axis=1
    )


def passed_along(value, axis, steps):
    count = lax.axis_size(axis)
    pairs = [(source, (source + steps) % count) for source in range(count)]
    return lax.ppermute(value, axis, pairs)


def project_onto(vectors, direction):
    summed = jnp.zeros_like(vectors[0])
    for component in range(3):
        if direction[component] != 0:
            summed = summed + float(direction[component]) * vectors[component]
    return summed


def per_direction(values):
    return jnp.asarray(np.array(values, np.float32).reshape(19, 1, 1, 1))


def collide(population):
    density = jnp.sum(population, axis=0)
    velocity_parts = [
        jnp.sum(per_direction([c[component] for c in velocity]) * population, axis=0) / density
        for component in range(3)
    ]
    speed_square = (
        velocity_parts[0] * velocity_parts[0]
        + velocity_parts[1] * velocity_parts[1]
        + velocity_parts[2] * velocity_parts[2]
    )
    project = project_all(velocity_parts)
    balance = (
        per_direction(lattice_weight)
        * density
        * (1.0 + 3.0 * project + 4.5 * project * project - 1.5 * speed_square)
    )
    return population + relax_rate * (balance - population)


def project_all(vectors):
    summed = per_direction([c[0] for c in velocity]) * vectors[0]
    for component in (1, 2):
        summed = summed + per_direction([c[component] for c in velocity]) * vectors[component]
    return summed


def upstream_of(values, inner):
    for axis in range(3):
        shift = per_direction([c[axis] for c in velocity])
        pick = {
            s: lax.slice_in_dim(values, 1 - s, 1 - s + inner[axis], axis=axis + 1)
            for s in (-1, 0, 1)
        }
        values = jnp.where(shift > 0.5, pick[1], jnp.where(shift < -0.5, pick[-1], pick[0]))
    return values


def stream_links(moved, fluid_ext):
    inner = tuple(size - 2 for size in fluid_ext.shape)
    upstream = upstream_of(moved, inner)
    opened = upstream_of(jnp.broadcast_to(fluid_ext[None], (19,) + fluid_ext.shape), inner)
    bounce = 1.0 - opened
    centre = moved[:, 1 : inner[0] + 1, 1 : inner[1] + 1, 1 : inner[2] + 1]
    paired = centre[1:].reshape((9, 2) + inner)[:, ::-1].reshape((18,) + inner)
    reflected = jnp.concatenate([centre[0:1], paired], axis=0)
    return (upstream, opened, bounce, reflected)


def wall_force(bounce, reflected):
    carried = bounce * reflected
    return jnp.stack(
        [
            jnp.sum(per_direction([-2.0 * c[component] for c in velocity]) * carried, axis=0)
            for component in range(3)
        ]
    )


def stream_all(moved, fluid_ext, wall_speed):
    upstream, opened, bounce, reflected = stream_links(moved, fluid_ext)
    inside = fluid_ext[1:-1, 1:-1, 1:-1]
    speed_list = [wall_speed[0], wall_speed[1], wall_speed[2]]
    correction = per_direction([6.0 * w for w in lattice_weight]) * project_all(speed_list)
    result = inside * (opened * upstream + bounce * (reflected + correction))
    return result.astype(jnp.bfloat16)


def slot_table(tile_lists, tile_slots):
    slots = lax.broadcasted_iota(jnp.int32, (tile_slots, tile_lists.size), 0)
    return (slots == tile_lists.reshape(1, -1)).astype(jnp.float32)


def basis_weights(received, node_positions, tile_lists):
    tile_count = tile_lists.shape[0]
    tile_width = received.shape[2]
    chosen = received[tile_lists]
    nodes_at = node_positions.reshape(3, tile_count, tile_width)
    distance = jnp.zeros((tile_count, tile_width, tile_lists.shape[1], tile_width), jnp.float32)
    for component in range(3):
        offset = nodes_at[component][:, :, None, None] - chosen[:, None, :, 3 + component, :]
        distance = distance + offset * offset
    kernel = 1.0 / jnp.sqrt(1.0 + distance / (basis_radius * basis_radius))
    column = jnp.sum(kernel, axis=1).reshape(-1, tile_width)
    table = slot_table(tile_lists, received.shape[0])
    exact = lax.Precision.HIGHEST
    totals = jnp.einsum("tk,kp->tp", table, column, precision=exact)
    listed = jnp.einsum("tk,tp->kp", table, totals, precision=exact)
    listed = listed.reshape(tile_count, tile_lists.shape[1], tile_width)
    return (kernel / listed[:, None, :, :], chosen)


def map_tractions(weights, chosen, node_index, base):
    mapped = jnp.einsum(
        "anbp,abcp->can", weights, chosen[:, :, 0:3, :], precision=lax.Precision.HIGHEST
    )
    return base.at[:, node_index].add(mapped.reshape(3, -1))


def map_speeds(weights, solution_block, node_index, tile_lists, tile_slots):
    tile_count = weights.shape[0]
    tile_width = weights.shape[1]
    flat = solution_block.reshape(3, -1)
    at_nodes = flat[:, node_index].reshape(3, tile_count, tile_width)
    contrib = jnp.einsum("anbp,can->abcp", weights, at_nodes, precision=lax.Precision.HIGHEST)
    return jnp.einsum(
        "tk,kcp->tcp",
        slot_table(tile_lists, tile_slots),
        contrib.reshape(-1, 3, tile_width),
        precision=lax.Precision.HIGHEST,
    )


def apply_rows(matrix_ref, values_ref, stiff_ref, out_ref):
    span_cells, across_cells, deep_cells = stiff_ref.shape
    step = next(size for size in (16, 8, 4, 2, 1) if span_cells % size == 0)
    shape = (step, across_cells, deep_cells)
    across_at = lax.broadcasted_iota(jnp.int32, shape, 1)
    deep_at = lax.broadcasted_iota(jnp.int32, shape, 2)
    corners = [(a, b, c) for a in (0, 1) for b in (0, 1) for c in (0, 1)]
    for component in range(3):
        out_ref[component, 0:span_cells] = mass_shift * values_ref[component, 0:span_cells]
        out_ref[component, span_cells] = jnp.zeros((across_cells, deep_cells), jnp.float32)

    def ahead(value, across, deep):
        if across:
            value = jnp.where(
                across_at < across_cells - 1, pltpu.roll(value, across_cells - 1, 1), 0.0
            )
        if deep:
            value = jnp.where(deep_at < deep_cells - 1, pltpu.roll(value, deep_cells - 1, 2), 0.0)
        return value

    def behind(value, across, deep):
        if across:
            value = jnp.where(across_at >= 1, pltpu.roll(value, 1, 1), 0.0)
        if deep:
            value = jnp.where(deep_at >= 1, pltpu.roll(value, 1, 2), 0.0)
        return value

    def element_rows(block, carry):
        row = block * step
        gathered = []
        for a, b, c in corners:
            for component in range(3):
                gathered.append(ahead(values_ref[component, pl.ds(row + a, step)], b, c))
        scale = stiff_ref[pl.ds(row, step)]
        for corner_id, (a, b, c) in enumerate(corners):
            for component in range(3):
                line = 3 * corner_id + component
                force = matrix_ref[line, 0] * gathered[0]
                for other in range(1, 24):
                    force = force + matrix_ref[line, other] * gathered[other]
                out_ref[component, pl.ds(row + a, step)] += behind(scale * force, b, c)
        return carry

    lax.fori_loop(0, span_cells // step, element_rows, 0)


def operator_kernel(matrix_ref, values_ref, stiff_ref, out_ref):
    apply_rows(matrix_ref, values_ref, stiff_ref, out_ref)


def whole_sum(value):
    value = jnp.sum(value, axis=(0, 1))
    value = jnp.sum(value, axis=0, keepdims=True)
    return jnp.sum(value, axis=1, keepdims=True)


def solve_kernel(matrix_ref, joined_ref, out_ref, ahead_ref, image_ref, dir_ref, img_ref):
    stiff_ref = joined_ref.at[3]
    span_cells = stiff_ref.shape[0]
    residual = joined_ref[0:3]
    ahead_ref[:, 0:span_cells] = residual
    ahead_ref[:, span_cells : span_cells + 1] = jnp.zeros_like(residual[:, 0:1])
    apply_rows(matrix_ref, ahead_ref, stiff_ref, image_ref)
    image_vec = image_ref[:, 0:span_cells]
    norm_now = whole_sum(residual * residual)
    step_size = norm_now / whole_sum(residual * image_vec)
    dir_ref[...] = residual
    img_ref[...] = image_vec
    out_ref[...] = jnp.zeros_like(residual)
    for iteration in range(ITERS):
        out_ref[...] = out_ref[...] + step_size * dir_ref[...]
        residual = residual - step_size * img_ref[...]
        if iteration + 1 < ITERS:
            ahead_ref[:, 0:span_cells] = residual
            apply_rows(matrix_ref, ahead_ref, stiff_ref, image_ref)
            image_vec = image_ref[:, 0:span_cells]
            norm_next = whole_sum(residual * residual)
            curvature = whole_sum(residual * image_vec)
            beta_ratio = norm_next / norm_now
            step_size = norm_next / (curvature - beta_ratio * norm_next / step_size)
            dir_ref[...] = residual + beta_ratio * dir_ref[...]
            img_ref[...] = image_vec + beta_ratio * img_ref[...]
            norm_now = norm_next


def partition_solve_kernel(joined, matrix):
    span_cells, across_cells, deep_cells = joined.shape[1:]
    cells = span_cells * across_cells * deep_cells
    wide = (3, span_cells + 1, across_cells, deep_cells)
    side = (3, span_cells, across_cells, deep_cells)
    return pl.pallas_call(
        solve_kernel,
        out_shape=jax.ShapeDtypeStruct(side, jnp.float32),
        in_specs=[
            pl.BlockSpec(memory_space=pltpu.SMEM),
            pl.BlockSpec(memory_space=pltpu.VMEM),
        ],
        out_specs=pl.BlockSpec(memory_space=pltpu.VMEM),
        scratch_shapes=[
            pltpu.VMEM(wide, jnp.float32),
            pltpu.VMEM(wide, jnp.float32),
            pltpu.VMEM(side, jnp.float32),
            pltpu.VMEM(side, jnp.float32),
        ],
        cost_estimate=pl.CostEstimate(
            flops=ITERS * 2 * 24 * 24 * cells, transcendentals=0, bytes_accessed=28 * cells
        ),
    )(matrix, joined)


def partition_operator(values, stiffness, matrix):
    span_cells, across_cells, deep_cells = stiffness.shape
    widened = jnp.pad(values, ((0, 0), (0, 1), (0, 0), (0, 0)))
    cells = span_cells * across_cells * deep_cells
    summed = pl.pallas_call(
        operator_kernel,
        out_shape=jax.ShapeDtypeStruct(widened.shape, jnp.float32),
        in_specs=[
            pl.BlockSpec(memory_space=pltpu.SMEM),
            pl.BlockSpec(memory_space=pltpu.VMEM),
            pl.BlockSpec(memory_space=pltpu.VMEM),
        ],
        out_specs=pl.BlockSpec(memory_space=pltpu.VMEM),
        cost_estimate=pl.CostEstimate(
            flops=2 * 24 * 24 * cells, transcendentals=0, bytes_accessed=28 * cells
        ),
    )(matrix, widened, stiffness)
    return summed[:, :span_cells]


def whole_partition(block):
    lead = block.shape[:-3]
    count = len(lead)
    every = lax.all_gather(block, "gx", axis=count, tiled=True)
    return lax.all_gather(every, "gy", axis=count + 1, tiled=True)


def own_part(whole, rows, cols):
    start = (0, lax.axis_index("gx") * rows, lax.axis_index("gy") * cols, 0)
    return lax.dynamic_slice(whole, start, (whole.shape[0], rows, cols, whole.shape[3]))


def solve_structure(right_side, operator, products):
    residual = right_side
    image_vec = operator(residual)
    norm_now, curvature = products(residual, image_vec)
    step_size = norm_now / curvature
    direction, image_dir = (residual, image_vec)
    solution = jnp.zeros_like(right_side)
    for iteration in range(ITERS):
        solution = solution + step_size * direction
        residual = residual - step_size * image_dir
        if iteration + 1 < ITERS:
            image_vec = operator(residual)
            norm_next, curvature = products(residual, image_vec)
            beta_ratio = norm_next / norm_now
            step_size = norm_next / (curvature - beta_ratio * norm_next / step_size)
            direction = residual + beta_ratio * direction
            image_dir = image_vec + beta_ratio * image_dir
            norm_now = norm_next
    return solution


def per_device(
    populations,
    solid_mask,
    wall_cells,
    body_load,
    elem_scale,
    elem_active,
    elem_matrix,
    iface_nodes,
    iface_coords,
    neighbours,
):
    group_count = lax.axis_size("group")
    span_devices = lax.axis_size("gx")
    struct_groups = max(1, group_count // 8)
    fluid_groups = group_count - struct_groups
    group_index = lax.axis_index("group")
    slab_index = group_index * span_devices + lax.axis_index("gx")
    column_index = lax.axis_index("gy")
    is_fluid = group_index < fluid_groups
    is_struct = jnp.logical_not(is_fluid)
    span_cells, across_cells, deep_cells = solid_mask.shape
    cell_count = span_cells * across_cells * deep_cells
    fluid_here = jnp.where(is_fluid, 1.0 - solid_mask.astype(jnp.float32), 0.0)
    relaxed_pops = jnp.where(
        is_fluid, collide(populations.astype(jnp.float32)), 0.0
    ).astype(jnp.bfloat16)
    marker = fluid_here.astype(jnp.bfloat16)[None]
    widened = halo_exchange(
        jnp.concatenate([relaxed_pops, marker], axis=0), fluid_groups * span_devices
    )
    widened = jnp.pad(widened, ((0, 0), (0, 0), (0, 0), (1, 1))).astype(jnp.float32)
    moved = widened[0:19]
    fluid_ext = widened[19]
    wall_index = wall_cells.reshape(-1)
    point_count = wall_index.shape[0]
    tiles_out = point_count // TILE

    def fluid_pack(operands):
        upstream, opened, bounce, reflected = stream_links(operands[0], operands[1])
        force_parts = wall_force(bounce, reflected).reshape(3, cell_count)
        picked = force_parts[:, wall_index]
        span_pos = wall_index // (across_cells * deep_cells)
        across_pos = wall_index // deep_cells % across_cells + column_index * across_cells
        deep_pos = wall_index % deep_cells
        positions = jnp.stack(
            [
                (slab_index * span_cells + span_pos).astype(jnp.float32),
                across_pos.astype(jnp.float32),
                deep_pos.astype(jnp.float32),
            ]
        )
        packed = jnp.concatenate([picked, positions], axis=0)
        return packed.reshape(6, tiles_out, TILE).transpose(1, 0, 2)

    packed = lax.cond(
        is_fluid,
        fluid_pack,
        lambda operands: jnp.zeros((tiles_out, 6, TILE), jnp.float32),
        (moved, fluid_ext),
    )
    received = lax.all_gather(packed, "group", axis=0, tiled=True)
    node_index = iface_nodes.reshape(-1)
    node_positions = iface_coords.reshape(3, -1)
    tile_lists = neighbours.reshape(neighbours.shape[2], neighbours.shape[3])
    nodes_total = body_load.shape[1] * body_load.shape[2] * body_load.shape[3]
    weight_shape = (tile_lists.shape[0], TILE, tile_lists.shape[1], TILE)

    stiffness = elem_scale * elem_active.astype(jnp.float32)

    def struct_map(operands):
        received_all, flat = operands
        weights, chosen = basis_weights(received_all, node_positions, tile_lists)
        return (weights, map_tractions(weights, chosen, node_index, flat))

    def struct_quiet(operands):
        return (jnp.zeros(weight_shape, jnp.float32), operands[1])

    weights, right_side = lax.cond(
        is_struct, struct_map, struct_quiet, (received, body_load.reshape(3, nodes_total))
    )
    right_side = right_side.reshape(body_load.shape)
    joined = whole_partition(jnp.concatenate([right_side, stiffness[None]], axis=0))
    whole_side = joined[0:3]
    stiffness = joined[3]
    rows, cols = body_load.shape[1], body_load.shape[2]

    def partition_products(first_vec, second_vec):
        pair = (jnp.sum(first_vec * first_vec), jnp.sum(first_vec * second_vec))
        if struct_groups > 1:
            pair = lax.psum(tuple(jnp.where(is_struct, x, 0.0) for x in pair), "group")
        return pair

    def partition_solve(operands):
        side, stiff, matrix = operands
        return solve_structure(
            side, lambda values: partition_operator(values, stiff, matrix), partition_products
        )

    if struct_groups > 1:
        whole_solution = partition_solve((whole_side, stiffness, elem_matrix))
    else:
        whole_solution = lax.cond(
            is_struct,
            lambda operands: partition_solve_kernel(*operands),
            lambda operands: jnp.zeros_like(operands[0][0:3]),
            (joined, elem_matrix),
        )
    solution = own_part(whole_solution, rows, cols)
    if struct_groups > 1:
        solution = jnp.where(is_struct, solution, 0.0)
    tile_slots = received.shape[0]

    def struct_back(operands):
        return map_speeds(
            operands[0], operands[1], node_index, tile_lists, tile_slots
        )

    back_terms = lax.cond(
        is_struct,
        struct_back,
        lambda operands: jnp.zeros((tile_slots, 3, TILE), jnp.float32),
        (weights, solution),
    )
    per_group = tile_slots // group_count
    route_count = fluid_groups // struct_groups
    sender_slot = jnp.clip(group_index - fluid_groups, 0, struct_groups - 1)
    own_speeds = jnp.zeros((per_group, 3, TILE), jnp.float32)
    for route_step in range(route_count):
        offset_row = (sender_slot + route_step * struct_groups) * per_group
        outgoing = lax.dynamic_slice_in_dim(back_terms, offset_row, per_group, 0)
        incoming = passed_along(outgoing, "group", (route_step + 1) * struct_groups)
        own_speeds = own_speeds + jnp.where(
            group_index // struct_groups == route_step, incoming, 0.0
        )
    speed_parts = wall_gain * own_speeds.transpose(1, 0, 2).reshape(3, point_count)
    wall_speed = jnp.zeros((3, cell_count), jnp.float32).at[:, wall_index].add(speed_parts)
    wall_speed = wall_speed.reshape(3, span_cells, across_cells, deep_cells)
    upstream, opened, bounce, reflected = stream_links(moved, fluid_ext)
    inside = fluid_ext[1:-1, 1:-1, 1:-1]
    settled = inside * (opened * upstream + bounce * reflected)
    walled = jnp.where(is_fluid, inside * bounce, 0.0)
    settled = jnp.where(is_fluid, settled, 0.0)
    correction = per_direction([6.0 * w for w in lattice_weight]) * project_all(
        [wall_speed[0], wall_speed[1], wall_speed[2]]
    )
    new_populations = (settled + walled * correction).astype(jnp.bfloat16)
    return (new_populations, solution)


def solution(mesh):
    placed = (
        P(None, ("group", "gx"), "gy", None),
        P(("group", "gx"), "gy", None),
        P(("group", "gx"), "gy", None),
        P(None, ("group", "gx"), "gy", None),
        P(("group", "gx"), "gy", None),
        P(("group", "gx"), "gy", None),
        P(),
        P(("group", "gx"), "gy", None),
        P(None, ("group", "gx"), "gy", None),
        P(("group", "gx"), "gy", None, None),
    )
    return jax.shard_map(
        per_device,
        mesh=mesh,
        in_specs=placed,
        out_specs=(P(None, ("group", "gx"), "gy", None), P(None, ("group", "gx"), "gy", None)),
        check_vma=False,
    )
```

```python
import jax
import jax.numpy as jnp
import numpy as np
from jax import lax
from jax.sharding import PartitionSpec as P
from jax.experimental import pallas as pl
from jax.experimental.pallas import tpu as pltpu

TILE = 128
ITERS = 3


velocity = [
    (0, 0, 0),
    (1, 0, 0),
    (-1, 0, 0),
    (0, 1, 0),
    (0, -1, 0),
    (0, 0, 1),
    (0, 0, -1),
    (1, 1, 0),
    (-1, -1, 0),
    (1, -1, 0),
    (-1, 1, 0),
    (1, 0, 1),
    (-1, 0, -1),
    (1, 0, -1),
    (-1, 0, 1),
    (0, 1, 1),
    (0, -1, -1),
    (0, 1, -1),
    (0, -1, 1),
]
opposite = [0, 2, 1, 4, 3, 6, 5, 8, 7, 10, 9, 12, 11, 14, 13, 16, 15, 18, 17]
lattice_weight = [1.0 / 3.0] + [1.0 / 18.0] * 6 + [1.0 / 36.0] * 12
relax_rate = 1.0 / 0.6
wall_gain = 60.0
basis_radius = 24.0
mass_shift = 0.5


def halo_exchange(cells, span_devices):
    columns = lax.axis_size("gy")
    axes = ("group", "gx", "gy")

    def shifted(piece, dr, dc):
        pairs = [
            (r * columns + c, (r + dr) * columns + c + dc)
            for r in range(span_devices)
            for c in range(columns)
            if 0 <= r + dr < span_devices and 0 <= c + dc < columns
        ]
        return lax.ppermute(piece, axes, pairs)

    cols = cells.shape[2]
    column = lax.axis_index("gy")
    edges = jnp.concatenate([cells[:, :, :1], cells[:, :, cols - 1 :]], axis=2)
    every = lax.all_gather(edges, "gy", axis=0)
    from_left = lax.dynamic_index_in_dim(every, jnp.maximum(column - 1, 0), 0, False)
    from_right = lax.dynamic_index_in_dim(every, jnp.minimum(column + 1, columns - 1), 0, False)
    cells = jnp.concatenate(
        [
            jnp.where(column > 0, from_left[:, :, 1:], 0.0).astype(cells.dtype),
            cells,
            jnp.where(column < columns - 1, from_right[:, :, :1], 0.0).astype(cells.dtype),
        ],
        axis=2,
    )
    rows = cells.shape[1]
    return jnp.concatenate(
        [shifted(cells[:, rows - 1 :], 1, 0), cells, shifted(cells[:, :1], -1, 0)], axis=1
    )


def passed_along(value, axis, steps):
    count = lax.axis_size(axis)
    pairs = [(source, (source + steps) % count) for source in range(count)]
    return lax.ppermute(value, axis, pairs)


def project_onto(vectors, direction):
    summed = jnp.zeros_like(vectors[0])
    for component in range(3):
        if direction[component] != 0:
            summed = summed + float(direction[component]) * vectors[component]
    return summed


def per_direction(values):
    return jnp.asarray(np.array(values, np.float32).reshape(19, 1, 1, 1))


def collide(population):
    density = jnp.sum(population, axis=0)
    velocity_parts = [
        jnp.sum(per_direction([c[component] for c in velocity]) * population, axis=0) / density
        for component in range(3)
    ]
    speed_square = (
        velocity_parts[0] * velocity_parts[0]
        + velocity_parts[1] * velocity_parts[1]
        + velocity_parts[2] * velocity_parts[2]
    )
    project = project_all(velocity_parts)
    balance = (
        per_direction(lattice_weight)
        * density
        * (1.0 + 3.0 * project + 4.5 * project * project - 1.5 * speed_square)
    )
    return population + relax_rate * (balance - population)


def project_all(vectors):
    summed = per_direction([c[0] for c in velocity]) * vectors[0]
    for component in (1, 2):
        summed = summed + per_direction([c[component] for c in velocity]) * vectors[component]
    return summed


def upstream_of(values, inner):
    for axis in range(3):
        shift = per_direction([c[axis] for c in velocity])
        pick = {
            s: lax.slice_in_dim(values, 1 - s, 1 - s + inner[axis], axis=axis + 1)
            for s in (-1, 0, 1)
        }
        values = jnp.where(shift > 0.5, pick[1], jnp.where(shift < -0.5, pick[-1], pick[0]))
    return values


def stream_links(moved, fluid_ext):
    inner = tuple(size - 2 for size in fluid_ext.shape)
    upstream = upstream_of(moved, inner)
    opened = upstream_of(jnp.broadcast_to(fluid_ext[None], (19,) + fluid_ext.shape), inner)
    bounce = 1.0 - opened
    centre = moved[:, 1 : inner[0] + 1, 1 : inner[1] + 1, 1 : inner[2] + 1]
    paired = centre[1:].reshape((9, 2) + inner)[:, ::-1].reshape((18,) + inner)
    reflected = jnp.concatenate([centre[0:1], paired], axis=0)
    return (upstream, opened, bounce, reflected)


def wall_force(bounce, reflected):
    carried = bounce * reflected
    return jnp.stack(
        [
            jnp.sum(per_direction([-2.0 * c[component] for c in velocity]) * carried, axis=0)
            for component in range(3)
        ]
    )


def stream_all(moved, fluid_ext, wall_speed):
    upstream, opened, bounce, reflected = stream_links(moved, fluid_ext)
    inside = fluid_ext[1:-1, 1:-1, 1:-1]
    speed_list = [wall_speed[0], wall_speed[1], wall_speed[2]]
    correction = per_direction([6.0 * w for w in lattice_weight]) * project_all(speed_list)
    result = inside * (opened * upstream + bounce * (reflected + correction))
    return result.astype(jnp.bfloat16)


def slot_table(tile_lists, tile_slots):
    slots = lax.broadcasted_iota(jnp.int32, (tile_slots, tile_lists.size), 0)
    return (slots == tile_lists.reshape(1, -1)).astype(jnp.float32)


def basis_weights(received, node_positions, tile_lists):
    tile_count = tile_lists.shape[0]
    tile_width = received.shape[2]
    chosen = received[tile_lists]
    nodes_at = node_positions.reshape(3, tile_count, tile_width)
    distance = jnp.zeros((tile_count, tile_width, tile_lists.shape[1], tile_width), jnp.float32)
    for component in range(3):
        offset = nodes_at[component][:, :, None, None] - chosen[:, None, :, 3 + component, :]
        distance = distance + offset * offset
    kernel = 1.0 / jnp.sqrt(1.0 + distance / (basis_radius * basis_radius))
    column = jnp.sum(kernel, axis=1).reshape(-1, tile_width)
    table = slot_table(tile_lists, received.shape[0])
    exact = lax.Precision.HIGHEST
    totals = jnp.einsum("tk,kp->tp", table, column, precision=exact)
    listed = jnp.einsum("tk,tp->kp", table, totals, precision=exact)
    listed = listed.reshape(tile_count, tile_lists.shape[1], tile_width)
    return (kernel / listed[:, None, :, :], chosen)


def map_tractions(weights, chosen, node_index, base):
    mapped = jnp.einsum(
        "anbp,abcp->can", weights, chosen[:, :, 0:3, :], precision=lax.Precision.HIGHEST
    )
    return base.at[:, node_index].add(mapped.reshape(3, -1))


def map_speeds(weights, solution_block, node_index, tile_lists, tile_slots):
    tile_count = weights.shape[0]
    tile_width = weights.shape[1]
    flat = solution_block.reshape(3, -1)
    at_nodes = flat[:, node_index].reshape(3, tile_count, tile_width)
    contrib = jnp.einsum("anbp,can->abcp", weights, at_nodes, precision=lax.Precision.HIGHEST)
    return jnp.einsum(
        "tk,kcp->tcp",
        slot_table(tile_lists, tile_slots),
        contrib.reshape(-1, 3, tile_width),
        precision=lax.Precision.HIGHEST,
    )


def apply_rows(matrix_ref, values_ref, stiff_ref, out_ref):
    span_cells, across_cells, deep_cells = stiff_ref.shape
    step = next(size for size in (16, 8, 4, 2, 1) if span_cells % size == 0)
    shape = (step + 1, across_cells, deep_cells)
    across_at = lax.broadcasted_iota(jnp.int32, shape, 1)
    deep_at = lax.broadcasted_iota(jnp.int32, shape, 2)
    corners = [(a, b, c) for a in (0, 1) for b in (0, 1) for c in (0, 1)]
    for component in range(3):
        out_ref[component, 0:span_cells] = mass_shift * values_ref[component, 0:span_cells]
        out_ref[component, span_cells] = jnp.zeros((across_cells, deep_cells), jnp.float32)

    def ahead(value, across, deep):
        if across:
            value = jnp.where(
                across_at < across_cells - 1, pltpu.roll(value, across_cells - 1, 1), 0.0
            )
        if deep:
            value = jnp.where(deep_at < deep_cells - 1, pltpu.roll(value, deep_cells - 1, 2), 0.0)
        return value

    def behind(value, across, deep):
        if across:
            value = jnp.where(across_at[:step] >= 1, pltpu.roll(value, 1, 1), 0.0)
        if deep:
            value = jnp.where(deep_at[:step] >= 1, pltpu.roll(value, 1, 2), 0.0)
        return value

    def element_rows(block, carry):
        row = block * step
        window = [values_ref[component, pl.ds(row, step + 1)] for component in range(3)]
        shifted = {}
        for b in (0, 1):
            for c in (0, 1):
                for component in range(3):
                    shifted[(b, c, component)] = ahead(window[component], b, c)
        gathered = []
        for a, b, c in corners:
            for component in range(3):
                gathered.append(shifted[(b, c, component)][a : a + step])
        scale = stiff_ref[pl.ds(row, step)]
        for corner_id, (a, b, c) in enumerate(corners):
            for component in range(3):
                line = 3 * corner_id + component
                force = matrix_ref[line, 0] * gathered[0]
                for other in range(1, 24):
                    force = force + matrix_ref[line, other] * gathered[other]
                out_ref[component, pl.ds(row + a, step)] += behind(scale * force, b, c)
        return carry

    lax.fori_loop(0, span_cells // step, element_rows, 0)


def operator_kernel(matrix_ref, values_ref, stiff_ref, out_ref):
    apply_rows(matrix_ref, values_ref, stiff_ref, out_ref)


def whole_sum(value):
    value = jnp.sum(value, axis=(0, 1))
    value = jnp.sum(value, axis=0, keepdims=True)
    return jnp.sum(value, axis=1, keepdims=True)


def solve_kernel(matrix_ref, joined_ref, out_ref, ahead_ref, image_ref, dir_ref, img_ref):
    stiff_ref = joined_ref.at[3]
    span_cells = stiff_ref.shape[0]
    residual = joined_ref[0:3]
    ahead_ref[:, 0:span_cells] = residual
    ahead_ref[:, span_cells : span_cells + 1] = jnp.zeros_like(residual[:, 0:1])
    apply_rows(matrix_ref, ahead_ref, stiff_ref, image_ref)
    image_vec = image_ref[:, 0:span_cells]
    norm_now = whole_sum(residual * residual)
    step_size = norm_now / whole_sum(residual * image_vec)
    dir_ref[...] = residual
    img_ref[...] = image_vec
    out_ref[...] = jnp.zeros_like(residual)
    for iteration in range(ITERS):
        out_ref[...] = out_ref[...] + step_size * dir_ref[...]
        residual = residual - step_size * img_ref[...]
        if iteration + 1 < ITERS:
            ahead_ref[:, 0:span_cells] = residual
            apply_rows(matrix_ref, ahead_ref, stiff_ref, image_ref)
            image_vec = image_ref[:, 0:span_cells]
            norm_next = whole_sum(residual * residual)
            curvature = whole_sum(residual * image_vec)
            beta_ratio = norm_next / norm_now
            step_size = norm_next / (curvature - beta_ratio * norm_next / step_size)
            dir_ref[...] = residual + beta_ratio * dir_ref[...]
            img_ref[...] = image_vec + beta_ratio * img_ref[...]
            norm_now = norm_next


def partition_solve_kernel(joined, matrix):
    span_cells, across_cells, deep_cells = joined.shape[1:]
    cells = span_cells * across_cells * deep_cells
    wide = (3, span_cells + 1, across_cells, deep_cells)
    side = (3, span_cells, across_cells, deep_cells)
    return pl.pallas_call(
        solve_kernel,
        out_shape=jax.ShapeDtypeStruct(side, jnp.float32),
        in_specs=[
            pl.BlockSpec(memory_space=pltpu.SMEM),
            pl.BlockSpec(memory_space=pltpu.VMEM),
        ],
        out_specs=pl.BlockSpec(memory_space=pltpu.VMEM),
        scratch_shapes=[
            pltpu.VMEM(wide, jnp.float32),
            pltpu.VMEM(wide, jnp.float32),
            pltpu.VMEM(side, jnp.float32),
            pltpu.VMEM(side, jnp.float32),
        ],
        cost_estimate=pl.CostEstimate(
            flops=ITERS * 2 * 24 * 24 * cells, transcendentals=0, bytes_accessed=28 * cells
        ),
    )(matrix, joined)


def partition_operator(values, stiffness, matrix):
    span_cells, across_cells, deep_cells = stiffness.shape
    widened = jnp.pad(values, ((0, 0), (0, 1), (0, 0), (0, 0)))
    cells = span_cells * across_cells * deep_cells
    summed = pl.pallas_call(
        operator_kernel,
        out_shape=jax.ShapeDtypeStruct(widened.shape, jnp.float32),
        in_specs=[
            pl.BlockSpec(memory_space=pltpu.SMEM),
            pl.BlockSpec(memory_space=pltpu.VMEM),
            pl.BlockSpec(memory_space=pltpu.VMEM),
        ],
        out_specs=pl.BlockSpec(memory_space=pltpu.VMEM),
        cost_estimate=pl.CostEstimate(
            flops=2 * 24 * 24 * cells, transcendentals=0, bytes_accessed=28 * cells
        ),
    )(matrix, widened, stiffness)
    return summed[:, :span_cells]


def whole_partition(block):
    lead = block.shape[:-3]
    count = len(lead)
    every = lax.all_gather(block, "gx", axis=count, tiled=True)
    return lax.all_gather(every, "gy", axis=count + 1, tiled=True)


def own_part(whole, rows, cols):
    start = (0, lax.axis_index("gx") * rows, lax.axis_index("gy") * cols, 0)
    return lax.dynamic_slice(whole, start, (whole.shape[0], rows, cols, whole.shape[3]))


def solve_structure(right_side, operator, products):
    residual = right_side
    image_vec = operator(residual)
    norm_now, curvature = products(residual, image_vec)
    step_size = norm_now / curvature
    direction, image_dir = (residual, image_vec)
    solution = jnp.zeros_like(right_side)
    for iteration in range(ITERS):
        solution = solution + step_size * direction
        residual = residual - step_size * image_dir
        if iteration + 1 < ITERS:
            image_vec = operator(residual)
            norm_next, curvature = products(residual, image_vec)
            beta_ratio = norm_next / norm_now
            step_size = norm_next / (curvature - beta_ratio * norm_next / step_size)
            direction = residual + beta_ratio * direction
            image_dir = image_vec + beta_ratio * image_dir
            norm_now = norm_next
    return solution


def per_device(
    populations,
    solid_mask,
    wall_cells,
    body_load,
    elem_scale,
    elem_active,
    elem_matrix,
    iface_nodes,
    iface_coords,
    neighbours,
):
    group_count = lax.axis_size("group")
    span_devices = lax.axis_size("gx")
    struct_groups = max(1, group_count // 8)
    fluid_groups = group_count - struct_groups
    group_index = lax.axis_index("group")
    slab_index = group_index * span_devices + lax.axis_index("gx")
    column_index = lax.axis_index("gy")
    is_fluid = group_index < fluid_groups
    is_struct = jnp.logical_not(is_fluid)
    span_cells, across_cells, deep_cells = solid_mask.shape
    cell_count = span_cells * across_cells * deep_cells
    fluid_here = jnp.where(is_fluid, 1.0 - solid_mask.astype(jnp.float32), 0.0)
    relaxed_pops = jnp.where(
        is_fluid, collide(populations.astype(jnp.float32)), 0.0
    ).astype(jnp.bfloat16)
    marker = fluid_here.astype(jnp.bfloat16)[None]
    widened = halo_exchange(
        jnp.concatenate([relaxed_pops, marker], axis=0), fluid_groups * span_devices
    )
    widened = jnp.pad(widened, ((0, 0), (0, 0), (0, 0), (1, 1))).astype(jnp.float32)
    moved = widened[0:19]
    fluid_ext = widened[19]
    wall_index = wall_cells.reshape(-1)
    point_count = wall_index.shape[0]
    tiles_out = point_count // TILE

    def fluid_pack(operands):
        upstream, opened, bounce, reflected = stream_links(operands[0], operands[1])
        force_parts = wall_force(bounce, reflected).reshape(3, cell_count)
        picked = force_parts[:, wall_index]
        span_pos = wall_index // (across_cells * deep_cells)
        across_pos = wall_index // deep_cells % across_cells + column_index * across_cells
        deep_pos = wall_index % deep_cells
        positions = jnp.stack(
            [
                (slab_index * span_cells + span_pos).astype(jnp.float32),
                across_pos.astype(jnp.float32),
                deep_pos.astype(jnp.float32),
            ]
        )
        packed = jnp.concatenate([picked, positions], axis=0)
        return packed.reshape(6, tiles_out, TILE).transpose(1, 0, 2)

    packed = lax.cond(
        is_fluid,
        fluid_pack,
        lambda operands: jnp.zeros((tiles_out, 6, TILE), jnp.float32),
        (moved, fluid_ext),
    )
    received = lax.all_gather(packed, "group", axis=0, tiled=True)
    node_index = iface_nodes.reshape(-1)
    node_positions = iface_coords.reshape(3, -1)
    tile_lists = neighbours.reshape(neighbours.shape[2], neighbours.shape[3])
    nodes_total = body_load.shape[1] * body_load.shape[2] * body_load.shape[3]
    weight_shape = (tile_lists.shape[0], TILE, tile_lists.shape[1], TILE)

    stiffness = elem_scale * elem_active.astype(jnp.float32)

    def struct_map(operands):
        received_all, flat = operands
        weights, chosen = basis_weights(received_all, node_positions, tile_lists)
        return (weights, map_tractions(weights, chosen, node_index, flat))

    def struct_quiet(operands):
        return (jnp.zeros(weight_shape, jnp.float32), operands[1])

    weights, right_side = lax.cond(
        is_struct, struct_map, struct_quiet, (received, body_load.reshape(3, nodes_total))
    )
    right_side = right_side.reshape(body_load.shape)
    joined = whole_partition(jnp.concatenate([right_side, stiffness[None]], axis=0))
    whole_side = joined[0:3]
    stiffness = joined[3]
    rows, cols = body_load.shape[1], body_load.shape[2]

    def partition_products(first_vec, second_vec):
        pair = (jnp.sum(first_vec * first_vec), jnp.sum(first_vec * second_vec))
        if struct_groups > 1:
            pair = lax.psum(tuple(jnp.where(is_struct, x, 0.0) for x in pair), "group")
        return pair

    def partition_solve(operands):
        side, stiff, matrix = operands
        return solve_structure(
            side, lambda values: partition_operator(values, stiff, matrix), partition_products
        )

    if struct_groups > 1:
        whole_solution = partition_solve((whole_side, stiffness, elem_matrix))
    else:
        whole_solution = lax.cond(
            is_struct,
            lambda operands: partition_solve_kernel(*operands),
            lambda operands: jnp.zeros_like(operands[0][0:3]),
            (joined, elem_matrix),
        )
    solution = own_part(whole_solution, rows, cols)
    if struct_groups > 1:
        solution = jnp.where(is_struct, solution, 0.0)
    tile_slots = received.shape[0]

    def struct_back(operands):
        return map_speeds(
            operands[0], operands[1], node_index, tile_lists, tile_slots
        )

    back_terms = lax.cond(
        is_struct,
        struct_back,
        lambda operands: jnp.zeros((tile_slots, 3, TILE), jnp.float32),
        (weights, solution),
    )
    per_group = tile_slots // group_count
    route_count = fluid_groups // struct_groups
    sender_slot = jnp.clip(group_index - fluid_groups, 0, struct_groups - 1)
    own_speeds = jnp.zeros((per_group, 3, TILE), jnp.float32)
    for route_step in range(route_count):
        offset_row = (sender_slot + route_step * struct_groups) * per_group
        outgoing = lax.dynamic_slice_in_dim(back_terms, offset_row, per_group, 0)
        incoming = passed_along(outgoing, "group", (route_step + 1) * struct_groups)
        own_speeds = own_speeds + jnp.where(
            group_index // struct_groups == route_step, incoming, 0.0
        )
    speed_parts = wall_gain * own_speeds.transpose(1, 0, 2).reshape(3, point_count)
    wall_speed = jnp.zeros((3, cell_count), jnp.float32).at[:, wall_index].add(speed_parts)
    wall_speed = wall_speed.reshape(3, span_cells, across_cells, deep_cells)
    new_populations = lax.cond(
        is_fluid,
        lambda operands: stream_all(operands[0], operands[1], operands[2]),
        lambda operands: jnp.zeros(operands[0][:, 1:-1, 1:-1, 1:-1].shape, jnp.bfloat16),
        (moved, fluid_ext, wall_speed),
    )
    return (new_populations, solution)


def solution(mesh):
    placed = (
        P(None, ("group", "gx"), "gy", None),
        P(("group", "gx"), "gy", None),
        P(("group", "gx"), "gy", None),
        P(None, ("group", "gx"), "gy", None),
        P(("group", "gx"), "gy", None),
        P(("group", "gx"), "gy", None),
        P(),
        P(("group", "gx"), "gy", None),
        P(None, ("group", "gx"), "gy", None),
        P(("group", "gx"), "gy", None, None),
    )
    return jax.shard_map(
        per_device,
        mesh=mesh,
        in_specs=placed,
        out_specs=(P(None, ("group", "gx"), "gy", None), P(None, ("group", "gx"), "gy", None)),
        check_vma=False,
    )
```
